32 devices in a mesh: ctx: 16 (over z, x, core), tp: 2 (over y).
Axes of the slice: x: 2, y: 2, z: 4, core: 2. Of those that a mesh axis runs over, the one named last changes fastest.
Arguments:
- queries: bfloat16 [8192, 4096], P(('ctx', 'tp')), may hold values from -9 to 9
- key_rows: bfloat16 [8192, 1024], P(('ctx', 'tp')), may hold values from -9 to 9
- value_rows: bfloat16 [8192, 1024], P(('ctx', 'tp')), may hold values from -6 to 6
- selected: int32 [16, 8, 3], P(None, 'tp'), may hold values from 0 to 14, as said below
- own_flag: int32 [16, 8], P(None, 'tp'), may hold values from 0 to 1, as said below
- cotangent: bfloat16 [8192, 4096], P(('ctx', 'tp')), may hold values from -6 to 6
Outputs:
- attended: bfloat16 [8192, 4096], P(('ctx', 'tp'))
- grad_queries: bfloat16 [8192, 4096], P(('ctx', 'tp'))
- grad_keys: bfloat16 [8192, 1024], P(('ctx', 'tp'))
- grad_values: bfloat16 [8192, 1024], P(('ctx', 'tp'))
The draws below stay inside these ranges and needn't reach their ends.
Inputs may be any that keep to these rules, and one draw needn't show every extreme that they name: `selected`: for query block b and key-value head g the 3 entries are distinct and below max(b, 3); for b >= 1 one of them is b - 1. `own_flag`: 1 for every block b < 3.
All inputs are finite; a program needn't handle non-finite values.
Results may differ from the reference program's by a relative error of at most 0.02.
Values may be sent and summed in bfloat16 or wider, within the bound.
No kernel may reach another device: no remote copies, remote signals or barrier semaphores. Data moves between devices by JAX's collectives and lax.ppermute only.
A program may use at most 64 MiB of HBM per device.

```python
import math
import jax
import jax.numpy as jnp
from jax import lax

HQ = 32
MEMORY_GROUPS = 8
HD = 128
BLK = 512
TOPK = 3
SEGMENT_COUNT = 16
TOKENS = 8192


def draw_queries(key, part):
    own_key = jax.random.fold_in(key, 11)
    first_key = jax.random.fold_in(own_key, 0)
    base_values = jax.random.normal(first_key, (TOKENS, HQ * HD), jnp.float32) * 1.6
    return jnp.clip(base_values, -8.0, 8.0).astype(jnp.bfloat16)


def draw_key_rows(key, part):
    own_key = jax.random.fold_in(key, 23)
    first_key = jax.random.fold_in(own_key, 0)
    base_values = jax.random.normal(first_key, (TOKENS, MEMORY_GROUPS * HD), jnp.float32) * 1.6
    return jnp.clip(base_values, -8.0, 8.0).astype(jnp.bfloat16)


def draw_selected(key, part):
    pick_key = jax.random.fold_in(key, 53)
    noise_key, opening_noise_seed = jax.random.split(pick_key)
    blocks = jnp.arange(SEGMENT_COUNT, dtype=jnp.int32)
    eligible_segments = blocks[None, None, :]
    holder_cards = blocks[:, None, None]
    noisy_logits = jax.random.randint(noise_key, (SEGMENT_COUNT, MEMORY_GROUPS, SEGMENT_COUNT), 0, 2 ** 16)
    opening_segment_lift = jax.random.randint(opening_noise_seed, (SEGMENT_COUNT, MEMORY_GROUPS, 1), 0, 2) * (eligible_segments == 0) * 2 ** 16
    newest_segment_lift = (eligible_segments == holder_cards - 1) * 2 ** 17
    segment_order = (noisy_logits + opening_segment_lift + newest_segment_lift) * SEGMENT_COUNT + (SEGMENT_COUNT - 1 - eligible_segments)
    block_limit = jnp.maximum(holder_cards, TOPK)
    segment_order = jnp.where(eligible_segments < block_limit, segment_order, -1 - eligible_segments).astype(jnp.int32)
    unused, picked = lax.top_k(segment_order, TOPK)
    return picked.astype(jnp.int32)


def draw_own_flag(key, part):
    flag_key = jax.random.fold_in(key, 41)
    coin_values = jax.random.randint(flag_key, (SEGMENT_COUNT, MEMORY_GROUPS), 0, 4)
    early_rows = (jnp.arange(SEGMENT_COUNT) < TOPK)[:, None]
    return jnp.where(early_rows | (coin_values > 0), 1, 0).astype(jnp.int32)


def level_of(stream_key, extent, pieces, low, high):
    gain, own = 1.0, jax.random.fold_in(stream_key, 6)
    for dim, blocks in pieces:
        heights = jnp.exp(jax.random.uniform(jax.random.fold_in(own, dim), (blocks,), jnp.float32, low / len(pieces), high / len(pieces)))
        gain = gain * jnp.repeat(heights, extent[dim] // blocks).reshape([-1 if axis == dim else 1 for axis in range(len(extent))])
    return gain


def centred(key, extent, deviation, bound, pieces=(), kind=jnp.bfloat16):
    drawn = jax.random.normal(key, extent, jnp.float32) * deviation
    if len(pieces) > 0:
        drawn = level_of(key, extent, pieces, -0.22, 0.18) * drawn
    return jnp.clip(drawn, min=-bound, max=bound).astype(kind)


def setup_inputs(seed: int = 0) -> dict:
    key_of = jax.random.split(jax.random.key(seed), 7)
    queries = draw_queries(jax.random.fold_in(key_of[6], 71), 0)
    key_rows = draw_key_rows(jax.random.fold_in(key_of[6], 71), 0)
    value_rows = centred(key_of[2], (TOKENS, MEMORY_GROUPS * HD), 1.0, 6.0, ((0, 32),))
    selected = draw_selected(jax.random.fold_in(key_of[6], 71), 0)
    own_flag = draw_own_flag(jax.random.fold_in(key_of[6], 71), 0)
    cotangent = centred(key_of[5], (TOKENS, HQ * HD), 1.0, 6.0, ((0, 32),))
    return dict(queries=queries, key_rows=key_rows, value_rows=value_rows, selected=selected, own_flag=own_flag, cotangent=cotangent)


def reference(queries, key_rows, value_rows, selected, own_flag, cotangent):
    group_size = HQ // MEMORY_GROUPS
    slot_count = TOPK + 1
    score_scale = 1.0 / math.sqrt(HD)
    query_blocks = queries.reshape(SEGMENT_COUNT, BLK, MEMORY_GROUPS, group_size, HD)
    upstream_blocks = cotangent.reshape(SEGMENT_COUNT, BLK, MEMORY_GROUPS, group_size, HD)
    key_heads = key_rows.reshape(SEGMENT_COUNT, BLK, MEMORY_GROUPS, HD).transpose(2, 0, 1, 3)
    value_heads = value_rows.reshape(SEGMENT_COUNT, BLK, MEMORY_GROUPS, HD).transpose(2, 0, 1, 3)
    head_ids = jnp.arange(MEMORY_GROUPS, dtype=jnp.int32)[:, None]
    row_ids = jnp.arange(BLK, dtype=jnp.int32)
    causal = row_ids[:, None] >= row_ids[None, :]
    slot_ids = jnp.arange(slot_count, dtype=jnp.int32)

    def one_block(carry, block_index):
        key_grads, value_grads = carry
        chosen = selected[block_index]
        own_ids = jnp.zeros((MEMORY_GROUPS, 1), jnp.int32) + block_index
        block_ids = jnp.concatenate([chosen, own_ids], axis=1)
        slot_live = jnp.concatenate([chosen < block_index, (own_flag[block_index] == 1)[:, None]], axis=1)
        allowed = slot_live[:, None, :, None] & ((slot_ids < TOPK)[None, None, :, None] | causal[None, :, None, :])
        key_set = key_heads[head_ids, block_ids].astype(jnp.float32)
        value_set = value_heads[head_ids, block_ids].astype(jnp.float32)
        query_f = query_blocks[block_index].astype(jnp.float32)
        upstream_f = upstream_blocks[block_index].astype(jnp.float32)
        scores = jnp.einsum('igqd,gstd->gqist', query_f, key_set) * score_scale
        scores = jnp.where(allowed[:, None], scores, -jnp.inf)
        row_max = lax.optimization_barrier(jnp.max(scores, axis=(3, 4), keepdims=True))
        weights = jnp.exp(scores - row_max)
        weight_sum = lax.optimization_barrier(jnp.sum(weights, axis=(3, 4), keepdims=True))
        softmax = weights / weight_sum
        softmax_low = lax.optimization_barrier(softmax.astype(jnp.bfloat16)).astype(jnp.float32)
        out_block = jnp.einsum('gqist,gstd->igqd', softmax_low, value_set).astype(jnp.bfloat16)
        out_f = lax.optimization_barrier(out_block).astype(jnp.float32)
        grad_probs = jnp.einsum('igqd,gstd->gqist', upstream_f, value_set)
        row_delta = jnp.einsum('igqd,igqd->gqi', upstream_f, out_f)
        grad_scores = softmax * (grad_probs - row_delta[:, :, :, None, None])
        grad_low = lax.optimization_barrier(grad_scores.astype(jnp.bfloat16)).astype(jnp.float32)
        grad_query = (score_scale * jnp.einsum('gqist,gstd->igqd', grad_low, key_set)).astype(jnp.bfloat16)
        key_part = score_scale * jnp.einsum('gqist,igqd->gstd', grad_low, query_f)
        value_part = jnp.einsum('gqist,igqd->gstd', softmax_low, upstream_f)
        key_grads = key_grads.at[head_ids, block_ids].add(key_part)
        value_grads = value_grads.at[head_ids, block_ids].add(value_part)
        return ((key_grads, value_grads), (out_block, grad_query))
    zero_grads = jnp.zeros((MEMORY_GROUPS, SEGMENT_COUNT, BLK, HD), jnp.float32)
    (key_grads, value_grads), (out_blocks, query_grads) = lax.scan(one_block, (zero_grads, zero_grads), jnp.arange(SEGMENT_COUNT, dtype=jnp.int32))
    attended = out_blocks.reshape(TOKENS, HQ * HD)
    grad_queries = query_grads.reshape(TOKENS, HQ * HD)
    grad_keys = key_grads.transpose(1, 2, 0, 3).reshape(TOKENS, MEMORY_GROUPS * HD).astype(jnp.bfloat16)
    grad_values = value_grads.transpose(1, 2, 0, 3).reshape(TOKENS, MEMORY_GROUPS * HD).astype(jnp.bfloat16)
    return (attended, grad_queries, grad_keys, grad_values)
```

```python
import functools
import math

import jax
import jax.numpy as jnp
from jax import lax
from jax.experimental import pallas as pl
from jax.experimental.pallas import tpu as pltpu
from jax.sharding import PartitionSpec as P

HD = 128
BLK = 512
TOPK = 3
ROW_TILE = 256


def attention_kernel(
    live_ref, q_ref, do_ref, kvs_ref, ko_ref, vo_ref,
    o_ref, dq_ref, dsel_ref, dko_ref, dvo_ref, *, slot_count, row_tile, scale
):
    g = pl.program_id(0)
    h = pl.program_id(1)
    t = pl.program_id(2)

    @pl.when((h == 0) & (t == 0))
    def _():
        dsel_ref[...] = jnp.zeros(dsel_ref.shape, dsel_ref.dtype)
        dko_ref[...] = jnp.zeros(dko_ref.shape, dko_ref.dtype)
        dvo_ref[...] = jnp.zeros(dvo_ref.shape, dvo_ref.dtype)

    q = q_ref[...]
    do = do_ref[...]
    keys = [kvs_ref[r, 0] for r in range(slot_count - 1)] + [ko_ref[...]]
    values = [kvs_ref[r, 1] for r in range(slot_count - 1)] + [vo_ref[...]]
    trans_b = (((1,), (1,)), ((), ()))
    trans_a = (((0,), (0,)), ((), ()))
    scores = []
    for r in range(slot_count):
        s = lax.dot_general(q, keys[r], trans_b, preferred_element_type=jnp.float32) * scale
        live = live_ref[g * slot_count + r] > 0
        if r == slot_count - 1:
            row = t * row_tile + lax.broadcasted_iota(jnp.int32, s.shape, 0)
            col = lax.broadcasted_iota(jnp.int32, s.shape, 1)
            s = jnp.where(live & (row >= col), s, -jnp.inf)
        else:
            s = jnp.where(live, s, -jnp.inf)
        scores.append(s)
    row_max = scores[0].max(axis=1, keepdims=True)
    for s in scores[1:]:
        row_max = jnp.maximum(row_max, s.max(axis=1, keepdims=True))
    weights = [jnp.exp(s - row_max) for s in scores]
    total = weights[0].sum(axis=1, keepdims=True)
    for w in weights[1:]:
        total = total + w.sum(axis=1, keepdims=True)
    inverse = 1.0 / total
    probs = [w * inverse for w in weights]
    probs_low = [p.astype(jnp.bfloat16) for p in probs]
    out = jnp.dot(probs_low[0], values[0], preferred_element_type=jnp.float32)
    for r in range(1, slot_count):
        out = out + jnp.dot(probs_low[r], values[r], preferred_element_type=jnp.float32)
    out_low = out.astype(jnp.bfloat16)
    o_ref[...] = out_low
    delta = jnp.sum(do.astype(jnp.float32) * out_low.astype(jnp.float32), axis=1, keepdims=True)
    grad_q = None
    for r in range(slot_count):
        grad_p = lax.dot_general(do, values[r], trans_b, preferred_element_type=jnp.float32)
        grad_s = (probs[r] * (grad_p - delta)).astype(jnp.bfloat16)
        part = jnp.dot(grad_s, keys[r], preferred_element_type=jnp.float32)
        grad_q = part if grad_q is None else grad_q + part
        key_part = lax.dot_general(grad_s, q, trans_a, preferred_element_type=jnp.float32) * scale
        value_part = lax.dot_general(probs_low[r], do, trans_a, preferred_element_type=jnp.float32)
        if r == slot_count - 1:
            dko_ref[...] += key_part
            dvo_ref[...] += value_part
        else:
            dsel_ref[r, 0] += key_part
            dsel_ref[r, 1] += value_part
    dq_ref[...] = (grad_q * scale).astype(jnp.bfloat16)


def attention(live, query_heads, upstream_heads, fetched, key_heads, value_heads, group_size):
    tokens, _ = query_heads.shape
    head_count = key_heads.shape[1] // HD
    slot_count = TOPK + 1
    row_tile = min(ROW_TILE, tokens)
    tiles = tokens // row_tile
    grid = (head_count, group_size, tiles)
    kernel = functools.partial(
        attention_kernel, slot_count=slot_count, row_tile=row_tile, scale=1.0 / math.sqrt(HD)
    )
    head_block = pl.BlockSpec((row_tile, HD), lambda g, h, t, live: (t, g * group_size + h))
    sel_block = pl.BlockSpec((None, TOPK, 2, BLK, HD), lambda g, h, t, live: (g, 0, 0, 0, 0))
    own_block = pl.BlockSpec((BLK, HD), lambda g, h, t, live: (0, g))
    flops = 12 * head_count * group_size * tokens * slot_count * BLK * HD
    bytes_accessed = 2 * (4 * query_heads.size + 3 * fetched.size + 6 * key_heads.size)
    return pl.pallas_call(
        kernel,
        grid_spec=pltpu.PrefetchScalarGridSpec(
            num_scalar_prefetch=1,
            grid=grid,
            in_specs=[head_block, head_block, sel_block, own_block, own_block],
            out_specs=[head_block, head_block, sel_block, own_block, own_block],
        ),
        out_shape=[
            jax.ShapeDtypeStruct(query_heads.shape, jnp.bfloat16),
            jax.ShapeDtypeStruct(query_heads.shape, jnp.bfloat16),
            jax.ShapeDtypeStruct(fetched.shape, jnp.float32),
            jax.ShapeDtypeStruct(key_heads.shape, jnp.float32),
            jax.ShapeDtypeStruct(key_heads.shape, jnp.float32),
        ],
        compiler_params=pltpu.CompilerParams(
            dimension_semantics=("arbitrary", "arbitrary", "arbitrary"),
        ),
        cost_estimate=pl.CostEstimate(
            flops=flops,
            transcendentals=head_count * group_size * tokens * slot_count * BLK,
            bytes_accessed=bytes_accessed,
        ),
    )(live, query_heads, upstream_heads, fetched, key_heads, value_heads)


def body(queries, key_rows, value_rows, selected, own_flag, cotangent):
    holders = lax.axis_size("ctx")
    tp_size = lax.axis_size("tp")
    position = lax.axis_index("ctx")
    rows_in = queries.shape[0]
    q_cols = queries.shape[1] // tp_size
    k_cols = key_rows.shape[1] // tp_size
    packed = jnp.concatenate(
        [
            queries.reshape(rows_in, tp_size, q_cols),
            cotangent.reshape(rows_in, tp_size, q_cols),
            key_rows.reshape(rows_in, tp_size, k_cols),
            value_rows.reshape(rows_in, tp_size, k_cols),
        ],
        axis=2,
    )
    packed = lax.all_to_all(packed, "tp", split_axis=1, concat_axis=0, tiled=True)
    tokens = rows_in * tp_size
    packed = packed.reshape(tokens, 2 * q_cols + 2 * k_cols)
    query_heads = packed[:, :q_cols]
    upstream_heads = packed[:, q_cols : 2 * q_cols]
    key_heads = packed[:, 2 * q_cols : 2 * q_cols + k_cols]
    value_heads = packed[:, 2 * q_cols + k_cols :]
    assert tokens == BLK
    head_count = k_cols // HD
    group_size = q_cols // k_cols
    span_rows = BLK // holders

    kv = jnp.stack(
        [key_heads.reshape(holders, span_rows, head_count, HD),
         value_heads.reshape(holders, span_rows, head_count, HD)],
        axis=1,
    )
    spread = lax.all_to_all(kv, "ctx", split_axis=0, concat_axis=0, tiled=True)
    head_ids = jnp.arange(head_count, dtype=jnp.int32)[None, :, None]
    send = spread[selected, :, :, head_ids, :]
    got = lax.all_to_all(send, "ctx", split_axis=0, concat_axis=4, tiled=True)
    fetched = got[0]

    my_selected = lax.dynamic_index_in_dim(selected, position, 0, keepdims=False)
    my_flags = lax.dynamic_index_in_dim(own_flag, position, 0, keepdims=False)
    live = jnp.concatenate(
        [(my_selected < position).astype(jnp.int32), (my_flags == 1).astype(jnp.int32)[:, None]],
        axis=1,
    ).reshape(-1)

    attended, grad_queries, grad_sel, grad_key_own, grad_value_own = attention(
        live, query_heads, upstream_heads, fetched, key_heads, value_heads, group_size
    )

    send_back = grad_sel.astype(jnp.bfloat16).reshape(head_count, TOPK, 2, holders, span_rows, HD)
    got_back = lax.all_to_all(send_back, "ctx", split_axis=3, concat_axis=1, tiled=True)
    flat = got_back.reshape(head_count, holders * TOPK, 2 * span_rows * HD).astype(jnp.float32)
    targets = selected.transpose(1, 0, 2).reshape(head_count, holders * TOPK)
    table = (targets[:, None, :] == jnp.arange(holders, dtype=jnp.int32)[None, :, None]).astype(
        jnp.float32
    )
    summed = jnp.einsum("gjn,gnx->gjx", table, flat, precision=lax.Precision.HIGHEST)
    owner = summed.reshape(head_count, holders, 2, span_rows, HD).astype(jnp.bfloat16)
    back = lax.all_to_all(owner, "ctx", split_axis=1, concat_axis=3, tiled=True)
    back = back[:, 0].astype(jnp.float32)
    total_keys = back[:, 0].transpose(1, 0, 2).reshape(tokens, k_cols) + grad_key_own
    total_values = back[:, 1].transpose(1, 0, 2).reshape(tokens, k_cols) + grad_value_own

    out = jnp.concatenate(
        [attended, grad_queries, total_keys.astype(jnp.bfloat16), total_values.astype(jnp.bfloat16)],
        axis=1,
    )
    out = out.reshape(tp_size, rows_in, 2 * q_cols + 2 * k_cols)
    out = lax.all_to_all(out, "tp", split_axis=0, concat_axis=0, tiled=True)
    out = out.reshape(tp_size, rows_in, 2 * q_cols + 2 * k_cols).transpose(1, 0, 2)

    def columns(lo, width):
        return out[:, :, lo : lo + width].reshape(rows_in, tp_size * width)

    return (
        columns(0, q_cols),
        columns(q_cols, q_cols),
        columns(2 * q_cols, k_cols),
        columns(2 * q_cols + k_cols, k_cols),
    )


def solution(mesh):
    in_specs = (
        P(("ctx", "tp"), None),
        P(("ctx", "tp"), None),
        P(("ctx", "tp"), None),
        P(None, "tp", None),
        P(None, "tp"),
        P(("ctx", "tp"), None),
    )
    out_specs = (
        P(("ctx", "tp"), None),
        P(("ctx", "tp"), None),
        P(("ctx", "tp"), None),
        P(("ctx", "tp"), None),
    )
    return jax.shard_map(body, mesh=mesh, in_specs=in_specs, out_specs=out_specs, check_vma=False)
```

```python
import functools
import math

import jax
import jax.numpy as jnp
from jax import lax
from jax.experimental import pallas as pl
from jax.experimental.pallas import tpu as pltpu
from jax.sharding import PartitionSpec as P

HD = 128
BLK = 512
TOPK = 3


def attention_kernel(
    live_ref, tp_ref, q_ref, do_ref, kvs_ref, ko_ref, vo_ref,
    o_ref, dq_ref, dsel_ref, dko_ref, dvo_ref, *, slot_count, row_tile, scale
):
    g = pl.program_id(0)
    h = pl.program_id(1)
    t = pl.program_id(2)

    @pl.when((h == 0) & (t == 0))
    def _():
        dsel_ref[...] = jnp.zeros(dsel_ref.shape, dsel_ref.dtype)
        dko_ref[...] = jnp.zeros(dko_ref.shape, dko_ref.dtype)
        dvo_ref[...] = jnp.zeros(dvo_ref.shape, dvo_ref.dtype)

    q = q_ref[...]
    do = do_ref[...]
    keys = [kvs_ref[r, 0] for r in range(slot_count - 1)] + [ko_ref[...]]
    values = [kvs_ref[r, 1] for r in range(slot_count - 1)] + [vo_ref[...]]
    trans_b = (((1,), (1,)), ((), ()))
    trans_a = (((0,), (0,)), ((), ()))
    scores = []
    for r in range(slot_count):
        s = lax.dot_general(q, keys[r], trans_b, preferred_element_type=jnp.float32) * scale
        live = live_ref[g * slot_count + r] > 0
        if r == slot_count - 1:
            row = t * row_tile + lax.broadcasted_iota(jnp.int32, s.shape, 0)
            col = lax.broadcasted_iota(jnp.int32, s.shape, 1)
            s = jnp.where(live & (row >= col), s, -jnp.inf)
        else:
            s = jnp.where(live, s, -jnp.inf)
        scores.append(s)
    row_max = scores[0].max(axis=1, keepdims=True)
    for s in scores[1:]:
        row_max = jnp.maximum(row_max, s.max(axis=1, keepdims=True))
    weights = [jnp.exp(s - row_max) for s in scores]
    total = weights[0].sum(axis=1, keepdims=True)
    for w in weights[1:]:
        total = total + w.sum(axis=1, keepdims=True)
    inverse = 1.0 / total
    probs = [w * inverse for w in weights]
    probs_low = [p.astype(jnp.bfloat16) for p in probs]
    out = jnp.dot(probs_low[0], values[0], preferred_element_type=jnp.float32)
    for r in range(1, slot_count):
        out = out + jnp.dot(probs_low[r], values[r], preferred_element_type=jnp.float32)
    out_low = out.astype(jnp.bfloat16)
    o_ref[...] = out_low
    delta = jnp.sum(do.astype(jnp.float32) * out_low.astype(jnp.float32), axis=1, keepdims=True)
    grad_q = None
    for r in range(slot_count):
        grad_p = lax.dot_general(do, values[r], trans_b, preferred_element_type=jnp.float32)
        grad_s = (probs[r] * (grad_p - delta)).astype(jnp.bfloat16)
        part = jnp.dot(grad_s, keys[r], preferred_element_type=jnp.float32)
        grad_q = part if grad_q is None else grad_q + part
        key_part = lax.dot_general(grad_s, q, trans_a, preferred_element_type=jnp.float32) * scale
        value_part = lax.dot_general(probs_low[r], do, trans_a, preferred_element_type=jnp.float32)
        if r == slot_count - 1:
            dko_ref[...] += key_part
            dvo_ref[...] += value_part
        else:
            dsel_ref[r, 0] += key_part
            dsel_ref[r, 1] += value_part
    dq_ref[...] = (grad_q * scale).astype(jnp.bfloat16)


def attention(live, tp_info, query_stack, upstream_stack, fetched, key_heads, value_heads, group_size):
    tp_size, row_tile, q_cols = query_stack.shape
    tokens = tp_size * row_tile
    head_count = key_heads.shape[1] // HD
    slot_count = TOPK + 1
    grid = (head_count, group_size, tp_size)
    kernel = functools.partial(
        attention_kernel, slot_count=slot_count, row_tile=row_tile, scale=1.0 / math.sqrt(HD)
    )

    def piece_in(g, h, t, live, tp):
        return ((tp[0] - t + tp_size) % tp_size, 0, g * group_size + h)

    def piece_out(g, h, t, live, tp):
        return ((t - tp[0] + tp_size) % tp_size, 0, g * group_size + h)

    in_block = pl.BlockSpec((None, row_tile, HD), piece_in)
    out_block = pl.BlockSpec((None, row_tile, HD), piece_out)
    sel_block = pl.BlockSpec((None, TOPK, 2, BLK, HD), lambda g, h, t, live, tp: (g, 0, 0, 0, 0))
    own_block = pl.BlockSpec((BLK, HD), lambda g, h, t, live, tp: (0, g))
    flops = 12 * head_count * group_size * tokens * slot_count * BLK * HD
    bytes_accessed = 2 * (4 * query_stack.size + 3 * fetched.size + 6 * key_heads.size)
    return pl.pallas_call(
        kernel,
        grid_spec=pltpu.PrefetchScalarGridSpec(
            num_scalar_prefetch=2,
            grid=grid,
            in_specs=[in_block, in_block, sel_block, own_block, own_block],
            out_specs=[out_block, out_block, sel_block, own_block, own_block],
        ),
        out_shape=[
            jax.ShapeDtypeStruct(query_stack.shape, jnp.bfloat16),
            jax.ShapeDtypeStruct(query_stack.shape, jnp.bfloat16),
            jax.ShapeDtypeStruct(fetched.shape, jnp.float32),
            jax.ShapeDtypeStruct(key_heads.shape, jnp.float32),
            jax.ShapeDtypeStruct(key_heads.shape, jnp.float32),
        ],
        compiler_params=pltpu.CompilerParams(
            dimension_semantics=("arbitrary", "arbitrary", "arbitrary"),
        ),
        cost_estimate=pl.CostEstimate(
            flops=flops,
            transcendentals=head_count * group_size * tokens * slot_count * BLK,
            bytes_accessed=bytes_accessed,
        ),
    )(live, tp_info, query_stack, upstream_stack, fetched, key_heads, value_heads)


def shift(x, axis, step, size):
    return lax.ppermute(x, axis, perm=[(s, (s + step) % size) for s in range(size)])


def tp_receive(x, me, size):
    width = x.shape[1] // size
    pieces = [lax.dynamic_slice_in_dim(x, me * width, width, 1)]
    for step in range(1, size):
        dest = (me + step) % size
        pieces.append(shift(lax.dynamic_slice_in_dim(x, dest * width, width, 1), "tp", step, size))
    return jnp.stack(pieces)


def tp_send(stack, me, size):
    pieces = [stack[0]] + [shift(stack[step], "tp", step, size) for step in range(1, size)]
    order = (me - jnp.arange(size, dtype=jnp.int32)) % size
    arranged = jnp.take(jnp.stack(pieces), order, axis=0)
    return arranged.transpose(1, 0, 2).reshape(stack.shape[1], size * stack.shape[2])


def source_order(stack, me, size):
    order = (me - jnp.arange(size, dtype=jnp.int32)) % size
    return jnp.take(stack, order, axis=0)


def body(queries, key_rows, value_rows, selected, own_flag, cotangent):
    holders = lax.axis_size("ctx")
    tp_size = lax.axis_size("tp")
    position = lax.axis_index("ctx")
    me = lax.axis_index("tp")
    rows_in = queries.shape[0]
    q_cols = queries.shape[1] // tp_size
    k_cols = key_rows.shape[1] // tp_size
    tokens = rows_in * tp_size
    assert tokens == BLK
    key_heads = source_order(tp_receive(key_rows, me, tp_size), me, tp_size).reshape(tokens, k_cols)
    value_heads = source_order(tp_receive(value_rows, me, tp_size), me, tp_size).reshape(tokens, k_cols)
    query_stack = tp_receive(queries, me, tp_size)
    upstream_stack = tp_receive(cotangent, me, tp_size)
    head_count = k_cols // HD
    group_size = q_cols // k_cols
    span_rows = BLK // holders

    kv = jnp.stack(
        [key_heads.reshape(holders, span_rows, head_count, HD),
         value_heads.reshape(holders, span_rows, head_count, HD)],
        axis=1,
    )
    spread = lax.all_to_all(kv, "ctx", split_axis=0, concat_axis=0, tiled=True)
    head_ids = jnp.arange(head_count, dtype=jnp.int32)[None, :, None]
    send = spread[selected, :, :, head_ids, :]
    got = lax.all_to_all(send, "ctx", split_axis=0, concat_axis=4, tiled=True)
    fetched = got[0]

    my_selected = lax.dynamic_index_in_dim(selected, position, 0, keepdims=False)
    my_flags = lax.dynamic_index_in_dim(own_flag, position, 0, keepdims=False)
    live = jnp.concatenate(
        [(my_selected < position).astype(jnp.int32), (my_flags == 1).astype(jnp.int32)[:, None]],
        axis=1,
    ).reshape(-1)

    tp_info = me.astype(jnp.int32).reshape(1)
    attended, grad_queries, grad_sel, grad_key_own, grad_value_own = attention(
        live, tp_info, query_stack, upstream_stack, fetched, key_heads, value_heads, group_size
    )
    attended = tp_send(attended, me, tp_size)
    grad_queries = tp_send(grad_queries, me, tp_size)

    send_back = grad_sel.astype(jnp.bfloat16).reshape(head_count, TOPK, 2, holders, span_rows, HD)
    got_back = lax.all_to_all(send_back, "ctx", split_axis=3, concat_axis=1, tiled=True)
    flat = got_back.reshape(head_count, holders * TOPK, 2 * span_rows * HD).astype(jnp.float32)
    targets = selected.transpose(1, 0, 2).reshape(head_count, holders * TOPK)
    table = (targets[:, None, :] == jnp.arange(holders, dtype=jnp.int32)[None, :, None]).astype(
        jnp.float32
    )
    summed = jnp.einsum("gjn,gnx->gjx", table, flat, precision=lax.Precision.HIGHEST)
    owner = summed.reshape(head_count, holders, 2, span_rows, HD).astype(jnp.bfloat16)
    back = lax.all_to_all(owner, "ctx", split_axis=1, concat_axis=3, tiled=True)
    back = back[:, 0].astype(jnp.float32)
    total_keys = back[:, 0].transpose(1, 0, 2).reshape(tokens, k_cols) + grad_key_own
    total_values = back[:, 1].transpose(1, 0, 2).reshape(tokens, k_cols) + grad_value_own

    def rows_by_destination(total):
        stack = total.astype(jnp.bfloat16).reshape(tp_size, rows_in, k_cols)
        order = (me + jnp.arange(tp_size, dtype=jnp.int32)) % tp_size
        return tp_send(jnp.take(stack, order, axis=0), me, tp_size)

    return (attended, grad_queries, rows_by_destination(total_keys), rows_by_destination(total_values))


def solution(mesh):
    in_specs = (
        P(("ctx", "tp"), None),
        P(("ctx", "tp"), None),
        P(("ctx", "tp"), None),
        P(None, "tp", None),
        P(None, "tp"),
        P(("ctx", "tp"), None),
    )
    out_specs = (
        P(("ctx", "tp"), None),
        P(("ctx", "tp"), None),
        P(("ctx", "tp"), None),
        P(("ctx", "tp"), None),
    )
    return jax.shard_map(body, mesh=mesh, in_specs=in_specs, out_specs=out_specs, check_vma=False)
```

```python
import functools
import math

import jax
import jax.numpy as jnp
from jax import lax
from jax.experimental import pallas as pl
from jax.experimental.pallas import tpu as pltpu
from jax.sharding import PartitionSpec as P

HD = 128
BLK = 512
TOPK = 3


def attention_kernel(
    live_ref, tp_ref, q_ref, do_ref, kvs_ref, ko_ref, vo_ref,
    o_ref, dq_ref, dsel_ref, dko_ref, dvo_ref, *, slot_count, row_tile, scale
):
    g = pl.program_id(0)
    h = pl.program_id(1)
    t = pl.program_id(2)

    @pl.when((h == 0) & (t == 0))
    def _():
        dsel_ref[...] = jnp.zeros(dsel_ref.shape, dsel_ref.dtype)
        dko_ref[...] = jnp.zeros(dko_ref.shape, dko_ref.dtype)
        dvo_ref[...] = jnp.zeros(dvo_ref.shape, dvo_ref.dtype)

    q = q_ref[...]
    do = do_ref[...]
    keys = [kvs_ref[r, 0] for r in range(slot_count - 1)] + [ko_ref[...]]
    values = [kvs_ref[r, 1] for r in range(slot_count - 1)] + [vo_ref[...]]
    trans_b = (((1,), (1,)), ((), ()))
    trans_a = (((0,), (0,)), ((), ()))
    scores = []
    for r in range(slot_count):
        s = lax.dot_general(q, keys[r], trans_b, preferred_element_type=jnp.float32) * scale
        live = live_ref[g * slot_count + r] > 0
        if r == slot_count - 1:
            row = t * row_tile + lax.broadcasted_iota(jnp.int32, s.shape, 0)
            col = lax.broadcasted_iota(jnp.int32, s.shape, 1)
            s = jnp.where(live & (row >= col), s, -jnp.inf)
        else:
            s = jnp.where(live, s, -jnp.inf)
        scores.append(s)
    row_max = scores[0].max(axis=1, keepdims=True)
    for s in scores[1:]:
        row_max = jnp.maximum(row_max, s.max(axis=1, keepdims=True))
    weights = [jnp.exp(s - row_max) for s in scores]
    total = weights[0].sum(axis=1, keepdims=True)
    for w in weights[1:]:
        total = total + w.sum(axis=1, keepdims=True)
    inverse = 1.0 / total
    probs = [w * inverse for w in weights]
    probs_low = [p.astype(jnp.bfloat16) for p in probs]
    out = jnp.dot(probs_low[0], values[0], preferred_element_type=jnp.float32)
    for r in range(1, slot_count):
        out = out + jnp.dot(probs_low[r], values[r], preferred_element_type=jnp.float32)
    out_low = out.astype(jnp.bfloat16)
    o_ref[...] = out_low
    delta = jnp.sum(do.astype(jnp.float32) * out_low.astype(jnp.float32), axis=1, keepdims=True)
    grad_q = None
    for r in range(slot_count):
        grad_p = lax.dot_general(do, values[r], trans_b, preferred_element_type=jnp.float32)
        grad_s = (probs[r] * (grad_p - delta)).astype(jnp.bfloat16)
        part = jnp.dot(grad_s, keys[r], preferred_element_type=jnp.float32)
        grad_q = part if grad_q is None else grad_q + part
        key_part = lax.dot_general(grad_s, q, trans_a, preferred_element_type=jnp.float32) * scale
        value_part = lax.dot_general(probs_low[r], do, trans_a, preferred_element_type=jnp.float32)
        if r == slot_count - 1:
            dko_ref[...] += key_part
            dvo_ref[...] += value_part
        else:
            dsel_ref[r, 0] += key_part
            dsel_ref[r, 1] += value_part
    dq_ref[...] = (grad_q * scale).astype(jnp.bfloat16)


def attention(live, tp_info, query_stack, upstream_stack, fetched, key_heads, value_heads, group_size, first):
    tp_size, row_tile, _ = query_stack.shape
    tokens = tp_size * row_tile
    head_count = fetched.shape[0]
    q_cols = head_count * group_size * HD
    slot_count = TOPK + 1
    grid = (head_count, group_size, tp_size)
    kernel = functools.partial(
        attention_kernel, slot_count=slot_count, row_tile=row_tile, scale=1.0 / math.sqrt(HD)
    )

    def piece_in(g, h, t, live, tp):
        return ((tp[0] - t + tp_size) % tp_size, 0, (first + g) * group_size + h)

    def piece_out(g, h, t, live, tp):
        return ((t - tp[0] + tp_size) % tp_size, 0, g * group_size + h)

    in_block = pl.BlockSpec((None, row_tile, HD), piece_in)
    out_block = pl.BlockSpec((None, row_tile, HD), piece_out)
    sel_block = pl.BlockSpec((None, TOPK, 2, BLK, HD), lambda g, h, t, live, tp: (g, 0, 0, 0, 0))
    own_in = pl.BlockSpec((BLK, HD), lambda g, h, t, live, tp: (0, first + g))
    own_out = pl.BlockSpec((BLK, HD), lambda g, h, t, live, tp: (0, g))
    flops = 12 * head_count * group_size * tokens * slot_count * BLK * HD
    bytes_accessed = 2 * (4 * tokens * q_cols + 3 * fetched.size + 6 * tokens * head_count * HD)
    return pl.pallas_call(
        kernel,
        grid_spec=pltpu.PrefetchScalarGridSpec(
            num_scalar_prefetch=2,
            grid=grid,
            in_specs=[in_block, in_block, sel_block, own_in, own_in],
            out_specs=[out_block, out_block, sel_block, own_out, own_out],
        ),
        out_shape=[
            jax.ShapeDtypeStruct((tp_size, row_tile, q_cols), jnp.bfloat16),
            jax.ShapeDtypeStruct((tp_size, row_tile, q_cols), jnp.bfloat16),
            jax.ShapeDtypeStruct(fetched.shape, jnp.float32),
            jax.ShapeDtypeStruct((tokens, head_count * HD), jnp.float32),
            jax.ShapeDtypeStruct((tokens, head_count * HD), jnp.float32),
        ],
        compiler_params=pltpu.CompilerParams(
            dimension_semantics=("arbitrary", "arbitrary", "arbitrary"),
        ),
        cost_estimate=pl.CostEstimate(
            flops=flops,
            transcendentals=head_count * group_size * tokens * slot_count * BLK,
            bytes_accessed=bytes_accessed,
        ),
    )(live, tp_info, query_stack, upstream_stack, fetched, key_heads, value_heads)


def shift(x, axis, step, size):
    return lax.ppermute(x, axis, perm=[(s, (s + step) % size) for s in range(size)])


def tp_receive(x, me, size):
    width = x.shape[1] // size
    pieces = [lax.dynamic_slice_in_dim(x, me * width, width, 1)]
    for step in range(1, size):
        dest = (me + step) % size
        pieces.append(shift(lax.dynamic_slice_in_dim(x, dest * width, width, 1), "tp", step, size))
    return jnp.stack(pieces)


def tp_send(stack, me, size):
    pieces = [stack[0]] + [shift(stack[step], "tp", step, size) for step in range(1, size)]
    order = (me - jnp.arange(size, dtype=jnp.int32)) % size
    arranged = jnp.take(jnp.stack(pieces), order, axis=0)
    return arranged.transpose(1, 0, 2).reshape(stack.shape[1], size * stack.shape[2])


def source_order(stack, me, size):
    order = (me - jnp.arange(size, dtype=jnp.int32)) % size
    return jnp.take(stack, order, axis=0)


def body(queries, key_rows, value_rows, selected, own_flag, cotangent):
    holders = lax.axis_size("ctx")
    tp_size = lax.axis_size("tp")
    position = lax.axis_index("ctx")
    me = lax.axis_index("tp")
    rows_in = queries.shape[0]
    q_cols = queries.shape[1] // tp_size
    k_cols = key_rows.shape[1] // tp_size
    tokens = rows_in * tp_size
    assert tokens == BLK
    key_heads = source_order(tp_receive(key_rows, me, tp_size), me, tp_size).reshape(tokens, k_cols)
    value_heads = source_order(tp_receive(value_rows, me, tp_size), me, tp_size).reshape(tokens, k_cols)
    query_stack = tp_receive(queries, me, tp_size)
    upstream_stack = tp_receive(cotangent, me, tp_size)
    head_count = k_cols // HD
    group_size = q_cols // k_cols
    span_rows = BLK // holders

    kv = jnp.stack(
        [key_heads.reshape(holders, span_rows, head_count, HD),
         value_heads.reshape(holders, span_rows, head_count, HD)],
        axis=1,
    )
    spread = lax.all_to_all(kv, "ctx", split_axis=0, concat_axis=0, tiled=True)
    my_selected = lax.dynamic_index_in_dim(selected, position, 0, keepdims=False)
    my_flags = lax.dynamic_index_in_dim(own_flag, position, 0, keepdims=False)
    live_all = jnp.concatenate(
        [(my_selected < position).astype(jnp.int32), (my_flags == 1).astype(jnp.int32)[:, None]],
        axis=1,
    )
    tp_info = me.astype(jnp.int32).reshape(1)
    chunk_count = 2 if head_count % 2 == 0 else 1
    chunk_heads = head_count // chunk_count
    chunk_k_cols = chunk_heads * HD

    results = []
    for chunk in range(chunk_count):
        first = chunk * chunk_heads
        chunk_selected = selected[:, first : first + chunk_heads]
        head_ids = jnp.arange(first, first + chunk_heads, dtype=jnp.int32)[None, :, None]
        send = spread[chunk_selected, :, :, head_ids, :]
        got = lax.all_to_all(send, "ctx", split_axis=0, concat_axis=4, tiled=True)
        fetched = got[0]
        live = live_all[first : first + chunk_heads].reshape(-1)
        attended, grad_queries, grad_sel, grad_key_own, grad_value_own = attention(
            live, tp_info, query_stack, upstream_stack, fetched, key_heads, value_heads,
            group_size, first,
        )
        attended = tp_send(attended, me, tp_size)
        grad_queries = tp_send(grad_queries, me, tp_size)

        send_back = grad_sel.astype(jnp.bfloat16).reshape(
            chunk_heads, TOPK, 2, holders, span_rows, HD
        )
        got_back = lax.all_to_all(send_back, "ctx", split_axis=3, concat_axis=1, tiled=True)
        flat = got_back.reshape(chunk_heads, holders * TOPK, 2 * span_rows * HD).astype(
            jnp.float32
        )
        targets = chunk_selected.transpose(1, 0, 2).reshape(chunk_heads, holders * TOPK)
        table = (
            targets[:, None, :] == jnp.arange(holders, dtype=jnp.int32)[None, :, None]
        ).astype(jnp.float32)
        summed = jnp.einsum("gjn,gnx->gjx", table, flat, precision=lax.Precision.HIGHEST)
        owner = summed.reshape(chunk_heads, holders, 2, span_rows, HD).astype(jnp.bfloat16)
        back = lax.all_to_all(owner, "ctx", split_axis=1, concat_axis=3, tiled=True)
        back = back[:, 0].astype(jnp.float32)
        total_keys = back[:, 0].transpose(1, 0, 2).reshape(tokens, chunk_k_cols) + grad_key_own
        total_values = (
            back[:, 1].transpose(1, 0, 2).reshape(tokens, chunk_k_cols) + grad_value_own
        )
        results.append((attended, grad_queries, total_keys, total_values))

    def rows_by_destination(total):
        stack = total.astype(jnp.bfloat16).reshape(tp_size, rows_in, k_cols)
        order = (me + jnp.arange(tp_size, dtype=jnp.int32)) % tp_size
        return tp_send(jnp.take(stack, order, axis=0), me, tp_size)

    def interleave(parts, width):
        stacked = jnp.stack([p.reshape(rows_in, tp_size, width) for p in parts], axis=2)
        return stacked.reshape(rows_in, tp_size * len(parts) * width)

    q_width = chunk_heads * group_size * HD
    attended = interleave([r[0] for r in results], q_width)
    grad_queries = interleave([r[1] for r in results], q_width)
    total_keys = jnp.concatenate([r[2] for r in results], axis=1)
    total_values = jnp.concatenate([r[3] for r in results], axis=1)
    return (attended, grad_queries, rows_by_destination(total_keys), rows_by_destination(total_values))


def solution(mesh):
    in_specs = (
        P(("ctx", "tp"), None),
        P(("ctx", "tp"), None),
        P(("ctx", "tp"), None),
        P(None, "tp", None),
        P(None, "tp"),
        P(("ctx", "tp"), None),
    )
    out_specs = (
        P(("ctx", "tp"), None),
        P(("ctx", "tp"), None),
        P(("ctx", "tp"), None),
        P(("ctx", "tp"), None),
    )
    return jax.shard_map(body, mesh=mesh, in_specs=in_specs, out_specs=out_specs, check_vma=False)
```

```python
import functools
import math

import jax
import jax.numpy as jnp
from jax import lax
from jax.experimental import pallas as pl
from jax.experimental.pallas import tpu as pltpu
from jax.sharding import PartitionSpec as P

HD = 128
BLK = 512
TOPK = 3


def attention_kernel(
    live_ref, tp_ref, q_ref, do_ref, kvs_ref, ko_ref, vo_ref,
    o_ref, dq_ref, dsel_ref, dko_ref, dvo_ref, *, slot_count, row_tile, scale
):
    g = pl.program_id(0)
    h = pl.program_id(1)
    t = pl.program_id(2)

    @pl.when((h == 0) & (t == 0))
    def _():
        dsel_ref[...] = jnp.zeros(dsel_ref.shape, dsel_ref.dtype)
        dko_ref[...] = jnp.zeros(dko_ref.shape, dko_ref.dtype)
        dvo_ref[...] = jnp.zeros(dvo_ref.shape, dvo_ref.dtype)

    q = q_ref[...]
    do = do_ref[...]
    keys = [kvs_ref[r, 0] for r in range(slot_count - 1)] + [ko_ref[...]]
    values = [kvs_ref[r, 1] for r in range(slot_count - 1)] + [vo_ref[...]]
    trans_b = (((1,), (1,)), ((), ()))
    trans_a = (((0,), (0,)), ((), ()))
    scores = []
    for r in range(slot_count):
        s = lax.dot_general(q, keys[r], trans_b, preferred_element_type=jnp.float32) * scale
        live = live_ref[g * slot_count + r] > 0
        if r == slot_count - 1:
            row = t * row_tile + lax.broadcasted_iota(jnp.int32, s.shape, 0)
            col = lax.broadcasted_iota(jnp.int32, s.shape, 1)
            s = jnp.where(live & (row >= col), s, -jnp.inf)
        else:
            s = jnp.where(live, s, -jnp.inf)
        scores.append(s)
    row_max = scores[0].max(axis=1, keepdims=True)
    for s in scores[1:]:
        row_max = jnp.maximum(row_max, s.max(axis=1, keepdims=True))
    weights = [jnp.exp(s - row_max) for s in scores]
    total = weights[0].sum(axis=1, keepdims=True)
    for w in weights[1:]:
        total = total + w.sum(axis=1, keepdims=True)
    inverse = 1.0 / total
    probs = [w * inverse for w in weights]
    probs_low = [p.astype(jnp.bfloat16) for p in probs]
    out = jnp.dot(probs_low[0], values[0], preferred_element_type=jnp.float32)
    for r in range(1, slot_count):
        out = out + jnp.dot(probs_low[r], values[r], preferred_element_type=jnp.float32)
    out_low = out.astype(jnp.bfloat16)
    o_ref[...] = out_low
    delta = jnp.sum(do.astype(jnp.float32) * out_low.astype(jnp.float32), axis=1, keepdims=True)
    grad_q = None
    for r in range(slot_count):
        grad_p = lax.dot_general(do, values[r], trans_b, preferred_element_type=jnp.float32)
        grad_s = (probs[r] * (grad_p - delta)).astype(jnp.bfloat16)
        part = jnp.dot(grad_s, keys[r], preferred_element_type=jnp.float32)
        grad_q = part if grad_q is None else grad_q + part
        key_part = lax.dot_general(grad_s, q, trans_a, preferred_element_type=jnp.float32) * scale
        value_part = lax.dot_general(probs_low[r], do, trans_a, preferred_element_type=jnp.float32)
        if r == slot_count - 1:
            dko_ref[...] += key_part
            dvo_ref[...] += value_part
        else:
            dsel_ref[r, 0] += key_part
            dsel_ref[r, 1] += value_part
    dq_ref[...] = (grad_q * scale).astype(jnp.bfloat16)


def attention(live, tp_info, query_stack, upstream_stack, fetched, key_heads, value_heads, group_size, first):
    tp_size, row_tile, _ = query_stack.shape
    tokens = tp_size * row_tile
    head_count = fetched.shape[0]
    q_cols = head_count * group_size * HD
    slot_count = TOPK + 1
    grid = (head_count, group_size, tp_size)
    kernel = functools.partial(
        attention_kernel, slot_count=slot_count, row_tile=row_tile, scale=1.0 / math.sqrt(HD)
    )

    def piece_in(g, h, t, live, tp):
        return ((tp[0] - t + tp_size) % tp_size, 0, g * group_size + h)

    def piece_out(g, h, t, live, tp):
        return ((t - tp[0] + tp_size) % tp_size, 0, g * group_size + h)

    in_block = pl.BlockSpec((None, row_tile, HD), piece_in)
    out_block = pl.BlockSpec((None, row_tile, HD), piece_out)
    sel_block = pl.BlockSpec((None, TOPK, 2, BLK, HD), lambda g, h, t, live, tp: (g, 0, 0, 0, 0))
    own_in = pl.BlockSpec((BLK, HD), lambda g, h, t, live, tp: (0, first + g))
    own_out = pl.BlockSpec((BLK, HD), lambda g, h, t, live, tp: (0, g))
    flops = 12 * head_count * group_size * tokens * slot_count * BLK * HD
    bytes_accessed = 2 * (4 * tokens * q_cols + 3 * fetched.size + 6 * tokens * head_count * HD)
    return pl.pallas_call(
        kernel,
        grid_spec=pltpu.PrefetchScalarGridSpec(
            num_scalar_prefetch=2,
            grid=grid,
            in_specs=[in_block, in_block, sel_block, own_in, own_in],
            out_specs=[out_block, out_block, sel_block, own_out, own_out],
        ),
        out_shape=[
            jax.ShapeDtypeStruct((tp_size, row_tile, q_cols), jnp.bfloat16),
            jax.ShapeDtypeStruct((tp_size, row_tile, q_cols), jnp.bfloat16),
            jax.ShapeDtypeStruct(fetched.shape, jnp.float32),
            jax.ShapeDtypeStruct((tokens, head_count * HD), jnp.float32),
            jax.ShapeDtypeStruct((tokens, head_count * HD), jnp.float32),
        ],
        compiler_params=pltpu.CompilerParams(
            dimension_semantics=("arbitrary", "arbitrary", "arbitrary"),
        ),
        cost_estimate=pl.CostEstimate(
            flops=flops,
            transcendentals=head_count * group_size * tokens * slot_count * BLK,
            bytes_accessed=bytes_accessed,
        ),
    )(live, tp_info, query_stack, upstream_stack, fetched, key_heads, value_heads)


def shift(x, axis, step, size):
    return lax.ppermute(x, axis, perm=[(s, (s + step) % size) for s in range(size)])


def tp_receive(x, me, size):
    width = x.shape[1] // size
    pieces = [lax.dynamic_slice_in_dim(x, me * width, width, 1)]
    for step in range(1, size):
        dest = (me + step) % size
        pieces.append(shift(lax.dynamic_slice_in_dim(x, dest * width, width, 1), "tp", step, size))
    return jnp.stack(pieces)


def tp_send(stack, me, size):
    pieces = [stack[0]] + [shift(stack[step], "tp", step, size) for step in range(1, size)]
    order = (me - jnp.arange(size, dtype=jnp.int32)) % size
    arranged = jnp.take(jnp.stack(pieces), order, axis=0)
    return arranged.transpose(1, 0, 2).reshape(stack.shape[1], size * stack.shape[2])


def source_order(stack, me, size):
    order = (me - jnp.arange(size, dtype=jnp.int32)) % size
    return jnp.take(stack, order, axis=0)


def body(queries, key_rows, value_rows, selected, own_flag, cotangent):
    holders = lax.axis_size("ctx")
    tp_size = lax.axis_size("tp")
    position = lax.axis_index("ctx")
    me = lax.axis_index("tp")
    rows_in = queries.shape[0]
    q_cols = queries.shape[1] // tp_size
    k_cols = key_rows.shape[1] // tp_size
    tokens = rows_in * tp_size
    assert tokens == BLK
    key_heads = source_order(tp_receive(key_rows, me, tp_size), me, tp_size).reshape(tokens, k_cols)
    value_heads = source_order(tp_receive(value_rows, me, tp_size), me, tp_size).reshape(tokens, k_cols)
    head_count = k_cols // HD
    group_size = q_cols // k_cols
    span_rows = BLK // holders

    kv = jnp.stack(
        [key_heads.reshape(holders, span_rows, head_count, HD),
         value_heads.reshape(holders, span_rows, head_count, HD)],
        axis=1,
    )
    spread = lax.all_to_all(kv, "ctx", split_axis=0, concat_axis=0, tiled=True)
    my_selected = lax.dynamic_index_in_dim(selected, position, 0, keepdims=False)
    my_flags = lax.dynamic_index_in_dim(own_flag, position, 0, keepdims=False)
    live_all = jnp.concatenate(
        [(my_selected < position).astype(jnp.int32), (my_flags == 1).astype(jnp.int32)[:, None]],
        axis=1,
    )
    tp_info = me.astype(jnp.int32).reshape(1)
    chunk_count = 2 if head_count % 2 == 0 else 1
    chunk_heads = head_count // chunk_count
    chunk_k_cols = chunk_heads * HD

    q_width = chunk_heads * group_size * HD

    def chunk_columns(x, chunk):
        return x.reshape(rows_in, tp_size, chunk_count, q_width)[:, :, chunk].reshape(
            rows_in, tp_size * q_width
        )

    results = []
    for chunk in range(chunk_count):
        first = chunk * chunk_heads
        query_stack = tp_receive(chunk_columns(queries, chunk), me, tp_size)
        upstream_stack = tp_receive(chunk_columns(cotangent, chunk), me, tp_size)
        chunk_selected = selected[:, first : first + chunk_heads]
        head_ids = jnp.arange(first, first + chunk_heads, dtype=jnp.int32)[None, :, None]
        send = spread[chunk_selected, :, :, head_ids, :]
        got = lax.all_to_all(send, "ctx", split_axis=0, concat_axis=4, tiled=True)
        fetched = got[0]
        live = live_all[first : first + chunk_heads].reshape(-1)
        attended, grad_queries, grad_sel, grad_key_own, grad_value_own = attention(
            live, tp_info, query_stack, upstream_stack, fetched, key_heads, value_heads,
            group_size, first,
        )
        attended = tp_send(attended, me, tp_size)
        grad_queries = tp_send(grad_queries, me, tp_size)

        send_back = grad_sel.astype(jnp.bfloat16).reshape(
            chunk_heads, TOPK, 2, holders, span_rows, HD
        )
        got_back = lax.all_to_all(send_back, "ctx", split_axis=3, concat_axis=1, tiled=True)
        flat = got_back.reshape(chunk_heads, holders * TOPK, 2 * span_rows * HD).astype(
            jnp.float32
        )
        targets = chunk_selected.transpose(1, 0, 2).reshape(chunk_heads, holders * TOPK)
        table = (
            targets[:, None, :] == jnp.arange(holders, dtype=jnp.int32)[None, :, None]
        ).astype(jnp.float32)
        summed = jnp.einsum("gjn,gnx->gjx", table, flat, precision=lax.Precision.HIGHEST)
        owner = summed.reshape(chunk_heads, holders, 2, span_rows, HD).astype(jnp.bfloat16)
        back = lax.all_to_all(owner, "ctx", split_axis=1, concat_axis=3, tiled=True)
        back = back[:, 0].astype(jnp.float32)
        total_keys = back[:, 0].transpose(1, 0, 2).reshape(tokens, chunk_k_cols) + grad_key_own
        total_values = (
            back[:, 1].transpose(1, 0, 2).reshape(tokens, chunk_k_cols) + grad_value_own
        )
        results.append((attended, grad_queries, total_keys, total_values))

    def rows_by_destination(total):
        stack = total.astype(jnp.bfloat16).reshape(tp_size, rows_in, k_cols)
        order = (me + jnp.arange(tp_size, dtype=jnp.int32)) % tp_size
        return tp_send(jnp.take(stack, order, axis=0), me, tp_size)

    def interleave(parts, width):
        stacked = jnp.stack([p.reshape(rows_in, tp_size, width) for p in parts], axis=2)
        return stacked.reshape(rows_in, tp_size * len(parts) * width)

    attended = interleave([r[0] for r in results], q_width)
    grad_queries = interleave([r[1] for r in results], q_width)
    total_keys = jnp.concatenate([r[2] for r in results], axis=1)
    total_values = jnp.concatenate([r[3] for r in results], axis=1)
    return (attended, grad_queries, rows_by_destination(total_keys), rows_by_destination(total_values))


def solution(mesh):
    in_specs = (
        P(("ctx", "tp"), None),
        P(("ctx", "tp"), None),
        P(("ctx", "tp"), None),
        P(None, "tp", None),
        P(None, "tp"),
        P(("ctx", "tp"), None),
    )
    out_specs = (
        P(("ctx", "tp"), None),
        P(("ctx", "tp"), None),
        P(("ctx", "tp"), None),
        P(("ctx", "tp"), None),
    )
    return jax.shard_map(body, mesh=mesh, in_specs=in_specs, out_specs=out_specs, check_vma=False)
```

```python
import functools
import math

import jax
import jax.numpy as jnp
from jax import lax
from jax.experimental import pallas as pl
from jax.experimental.pallas import tpu as pltpu
from jax.sharding import PartitionSpec as P

HD = 128
BLK = 512
TOPK = 3


def attention_kernel(
    live_ref, tp_ref, q_ref, do_ref, kvs_ref, ko_ref, vo_ref,
    o_ref, dq_ref, dsel_ref, dko_ref, dvo_ref, *, slot_count, row_tile, scale
):
    g = pl.program_id(0)
    h = pl.program_id(1)
    t = pl.program_id(2)

    @pl.when((h == 0) & (t == 0))
    def _():
        dsel_ref[...] = jnp.zeros(dsel_ref.shape, dsel_ref.dtype)
        dko_ref[...] = jnp.zeros(dko_ref.shape, dko_ref.dtype)
        dvo_ref[...] = jnp.zeros(dvo_ref.shape, dvo_ref.dtype)

    q = q_ref[...]
    do = do_ref[...]
    keys = [kvs_ref[r, 0] for r in range(slot_count - 1)] + [ko_ref[...]]
    values = [kvs_ref[r, 1] for r in range(slot_count - 1)] + [vo_ref[...]]
    trans_b = (((1,), (1,)), ((), ()))
    trans_a = (((0,), (0,)), ((), ()))
    scores = []
    for r in range(slot_count):
        s = lax.dot_general(q, keys[r], trans_b, preferred_element_type=jnp.float32) * scale
        live = live_ref[g * slot_count + r] > 0
        if r == slot_count - 1:
            row = t * row_tile + lax.broadcasted_iota(jnp.int32, s.shape, 0)
            col = lax.broadcasted_iota(jnp.int32, s.shape, 1)
            s = jnp.where(live & (row >= col), s, -jnp.inf)
        else:
            s = jnp.where(live, s, -jnp.inf)
        scores.append(s)
    row_max = scores[0].max(axis=1, keepdims=True)
    for s in scores[1:]:
        row_max = jnp.maximum(row_max, s.max(axis=1, keepdims=True))
    weights = [jnp.exp(s - row_max) for s in scores]
    total = weights[0].sum(axis=1, keepdims=True)
    for w in weights[1:]:
        total = total + w.sum(axis=1, keepdims=True)
    inverse = 1.0 / total
    probs = [w * inverse for w in weights]
    probs_low = [p.astype(jnp.bfloat16) for p in probs]
    out = jnp.dot(probs_low[0], values[0], preferred_element_type=jnp.float32)
    for r in range(1, slot_count):
        out = out + jnp.dot(probs_low[r], values[r], preferred_element_type=jnp.float32)
    out_low = out.astype(jnp.bfloat16)
    o_ref[...] = out_low
    delta = jnp.sum(do.astype(jnp.float32) * out_low.astype(jnp.float32), axis=1, keepdims=True)
    grad_q = None
    for r in range(slot_count):
        grad_p = lax.dot_general(do, values[r], trans_b, preferred_element_type=jnp.float32)
        grad_s = (probs[r] * (grad_p - delta)).astype(jnp.bfloat16)
        part = jnp.dot(grad_s, keys[r], preferred_element_type=jnp.float32)
        grad_q = part if grad_q is None else grad_q + part
        key_part = lax.dot_general(grad_s, q, trans_a, preferred_element_type=jnp.float32) * scale
        value_part = lax.dot_general(probs_low[r], do, trans_a, preferred_element_type=jnp.float32)
        if r == slot_count - 1:
            dko_ref[...] += key_part
            dvo_ref[...] += value_part
        else:
            dsel_ref[r, 0] += key_part
            dsel_ref[r, 1] += value_part
    dq_ref[...] = (grad_q * scale).astype(jnp.bfloat16)


def attention(live, tp_info, query_stack, upstream_stack, fetched, key_heads, value_heads, group_size, first):
    tp_size, row_tile, _ = query_stack.shape
    tokens = tp_size * row_tile
    head_count = fetched.shape[0]
    q_cols = head_count * group_size * HD
    slot_count = TOPK + 1
    grid = (head_count, group_size, tp_size)
    kernel = functools.partial(
        attention_kernel, slot_count=slot_count, row_tile=row_tile, scale=1.0 / math.sqrt(HD)
    )

    def piece_in(g, h, t, live, tp):
        return ((tp[0] - t + tp_size) % tp_size, 0, g * group_size + h)

    def piece_out(g, h, t, live, tp):
        return ((t - tp[0] + tp_size) % tp_size, 0, g * group_size + h)

    in_block = pl.BlockSpec((None, row_tile, HD), piece_in)
    out_block = pl.BlockSpec((None, row_tile, HD), piece_out)
    sel_block = pl.BlockSpec((None, TOPK, 2, BLK, HD), lambda g, h, t, live, tp: (g, 0, 0, 0, 0))
    own_in = pl.BlockSpec((BLK, HD), lambda g, h, t, live, tp: (0, first + g))
    own_out = pl.BlockSpec((BLK, HD), lambda g, h, t, live, tp: (0, g))
    flops = 12 * head_count * group_size * tokens * slot_count * BLK * HD
    bytes_accessed = 2 * (4 * tokens * q_cols + 3 * fetched.size + 6 * tokens * head_count * HD)
    return pl.pallas_call(
        kernel,
        grid_spec=pltpu.PrefetchScalarGridSpec(
            num_scalar_prefetch=2,
            grid=grid,
            in_specs=[in_block, in_block, sel_block, own_in, own_in],
            out_specs=[out_block, out_block, sel_block, own_out, own_out],
        ),
        out_shape=[
            jax.ShapeDtypeStruct((tp_size, row_tile, q_cols), jnp.bfloat16),
            jax.ShapeDtypeStruct((tp_size, row_tile, q_cols), jnp.bfloat16),
            jax.ShapeDtypeStruct(fetched.shape, jnp.float32),
            jax.ShapeDtypeStruct((tokens, head_count * HD), jnp.float32),
            jax.ShapeDtypeStruct((tokens, head_count * HD), jnp.float32),
        ],
        compiler_params=pltpu.CompilerParams(
            dimension_semantics=("arbitrary", "arbitrary", "arbitrary"),
        ),
        cost_estimate=pl.CostEstimate(
            flops=flops,
            transcendentals=head_count * group_size * tokens * slot_count * BLK,
            bytes_accessed=bytes_accessed,
        ),
    )(live, tp_info, query_stack, upstream_stack, fetched, key_heads, value_heads)


def shift(x, axis, step, size):
    return lax.ppermute(x, axis, perm=[(s, (s + step) % size) for s in range(size)])


def tp_receive(x, me, size, width=None, offset=0):
    stride = x.shape[1] // size
    width = stride if width is None else width
    pieces = [lax.dynamic_slice_in_dim(x, me * stride + offset, width, 1)]
    for step in range(1, size):
        dest = (me + step) % size
        piece = lax.dynamic_slice_in_dim(x, dest * stride + offset, width, 1)
        pieces.append(shift(piece, "tp", step, size))
    return jnp.stack(pieces)


def tp_send(stack, me, size):
    pieces = [stack[0]] + [shift(stack[step], "tp", step, size) for step in range(1, size)]
    order = (me - jnp.arange(size, dtype=jnp.int32)) % size
    arranged = jnp.take(jnp.stack(pieces), order, axis=0)
    return arranged.transpose(1, 0, 2).reshape(stack.shape[1], size * stack.shape[2])


def source_order(stack, me, size):
    order = (me - jnp.arange(size, dtype=jnp.int32)) % size
    return jnp.take(stack, order, axis=0)


def body(queries, key_rows, value_rows, selected, own_flag, cotangent):
    holders = lax.axis_size("ctx")
    tp_size = lax.axis_size("tp")
    position = lax.axis_index("ctx")
    me = lax.axis_index("tp")
    rows_in = queries.shape[0]
    q_cols = queries.shape[1] // tp_size
    k_cols = key_rows.shape[1] // tp_size
    tokens = rows_in * tp_size
    assert tokens == BLK
    key_heads = source_order(tp_receive(key_rows, me, tp_size), me, tp_size).reshape(tokens, k_cols)
    value_heads = source_order(tp_receive(value_rows, me, tp_size), me, tp_size).reshape(tokens, k_cols)
    head_count = k_cols // HD
    group_size = q_cols // k_cols
    span_rows = BLK // holders

    kv = jnp.stack(
        [key_heads.reshape(holders, span_rows, head_count, HD),
         value_heads.reshape(holders, span_rows, head_count, HD)],
        axis=1,
    )
    spread = lax.all_to_all(kv, "ctx", split_axis=0, concat_axis=0, tiled=True)
    my_selected = lax.dynamic_index_in_dim(selected, position, 0, keepdims=False)
    my_flags = lax.dynamic_index_in_dim(own_flag, position, 0, keepdims=False)
    live_all = jnp.concatenate(
        [(my_selected < position).astype(jnp.int32), (my_flags == 1).astype(jnp.int32)[:, None]],
        axis=1,
    )
    tp_info = me.astype(jnp.int32).reshape(1)
    chunk_count = 2 if head_count % 2 == 0 else 1
    chunk_heads = head_count // chunk_count

    q_width = chunk_heads * group_size * HD

    results = []
    for chunk in range(chunk_count):
        first = chunk * chunk_heads
        query_stack = tp_receive(queries, me, tp_size, q_width, chunk * q_width)
        upstream_stack = tp_receive(cotangent, me, tp_size, q_width, chunk * q_width)
        chunk_selected = selected[:, first : first + chunk_heads]
        head_ids = jnp.arange(first, first + chunk_heads, dtype=jnp.int32)[None, :, None]
        send = spread[chunk_selected, :, :, head_ids, :]
        got = lax.all_to_all(send, "ctx", split_axis=0, concat_axis=4, tiled=True)
        fetched = got[0]
        live = live_all[first : first + chunk_heads].reshape(-1)
        attended, grad_queries, grad_sel, grad_key_own, grad_value_own = attention(
            live, tp_info, query_stack, upstream_stack, fetched, key_heads, value_heads,
            group_size, first,
        )
        attended = tp_send(attended, me, tp_size)
        grad_queries = tp_send(grad_queries, me, tp_size)

        send_back = grad_sel.astype(jnp.bfloat16).reshape(
            chunk_heads, TOPK, 2, holders, span_rows, HD
        )
        got_back = lax.all_to_all(send_back, "ctx", split_axis=3, concat_axis=1, tiled=True)
        flat = got_back.reshape(chunk_heads, holders * TOPK, 2 * span_rows * HD).astype(
            jnp.float32
        )
        targets = chunk_selected.transpose(1, 0, 2).reshape(chunk_heads, holders * TOPK)
        table = (
            targets[:, None, :] == jnp.arange(holders, dtype=jnp.int32)[None, :, None]
        ).astype(jnp.float32)
        summed = jnp.einsum("gjn,gnx->gjx", table, flat, precision=lax.Precision.HIGHEST)
        results.append((attended, grad_queries, summed, grad_key_own, grad_value_own))

    summed = jnp.concatenate([r[2] for r in results], axis=0)
    owner = summed.reshape(head_count, holders, 2, span_rows, HD).astype(jnp.bfloat16)
    back = lax.all_to_all(owner, "ctx", split_axis=1, concat_axis=3, tiled=True)
    back = back[:, 0].astype(jnp.float32)
    own_keys = jnp.concatenate([r[3] for r in results], axis=1)
    own_values = jnp.concatenate([r[4] for r in results], axis=1)
    total_keys = back[:, 0].transpose(1, 0, 2).reshape(tokens, k_cols) + own_keys
    total_values = back[:, 1].transpose(1, 0, 2).reshape(tokens, k_cols) + own_values

    def rows_by_destination(total):
        stack = total.astype(jnp.bfloat16).reshape(tp_size, rows_in, k_cols)
        order = (me + jnp.arange(tp_size, dtype=jnp.int32)) % tp_size
        return tp_send(jnp.take(stack, order, axis=0), me, tp_size)

    def interleave(parts, width):
        stacked = jnp.stack([p.reshape(rows_in, tp_size, width) for p in parts], axis=2)
        return stacked.reshape(rows_in, tp_size * len(parts) * width)

    attended = interleave([r[0] for r in results], q_width)
    grad_queries = interleave([r[1] for r in results], q_width)
    return (attended, grad_queries, rows_by_destination(total_keys), rows_by_destination(total_values))


def solution(mesh):
    in_specs = (
        P(("ctx", "tp"), None),
        P(("ctx", "tp"), None),
        P(("ctx", "tp"), None),
        P(None, "tp", None),
        P(None, "tp"),
        P(("ctx", "tp"), None),
    )
    out_specs = (
        P(("ctx", "tp"), None),
        P(("ctx", "tp"), None),
        P(("ctx", "tp"), None),
        P(("ctx", "tp"), None),
    )
    return jax.shard_map(body, mesh=mesh, in_specs=in_specs, out_specs=out_specs, check_vma=False)
```

```python
import functools
import math

import jax
import jax.numpy as jnp
from jax import lax
from jax.experimental import pallas as pl
from jax.experimental.pallas import tpu as pltpu
from jax.sharding import PartitionSpec as P

HD = 128
BLK = 512
TOPK = 3


def attention_kernel(
    live_ref, tp_ref, q_ref, do_ref, kvs_ref, ko_ref, vo_ref,
    o_ref, dq_ref, dsel_ref, dko_ref, dvo_ref, acc_ref, *, slot_count, row_tile, scale
):
    g = pl.program_id(0)
    h = pl.program_id(1)
    t = pl.program_id(2)

    @pl.when((h == 0) & (t == 0))
    def _():
        acc_ref[...] = jnp.zeros(acc_ref.shape, acc_ref.dtype)

    q = q_ref[...]
    do = do_ref[...]
    keys = [kvs_ref[r, 0] for r in range(slot_count - 1)] + [ko_ref[...]]
    values = [kvs_ref[r, 1] for r in range(slot_count - 1)] + [vo_ref[...]]
    trans_b = (((1,), (1,)), ((), ()))
    q_t = q.T
    do_t = do.T
    scores = []
    for r in range(slot_count):
        s = lax.dot_general(q, keys[r], trans_b, preferred_element_type=jnp.float32) * scale
        live = live_ref[g * slot_count + r] > 0
        if r == slot_count - 1:
            row = t * row_tile + lax.broadcasted_iota(jnp.int32, s.shape, 0)
            col = lax.broadcasted_iota(jnp.int32, s.shape, 1)
            s = jnp.where(live & (row >= col), s, -jnp.inf)
        else:
            s = jnp.where(live, s, -jnp.inf)
        scores.append(s)
    row_max = scores[0].max(axis=1, keepdims=True)
    for s in scores[1:]:
        row_max = jnp.maximum(row_max, s.max(axis=1, keepdims=True))
    weights = [jnp.exp(s - row_max) for s in scores]
    total = weights[0].sum(axis=1, keepdims=True)
    for w in weights[1:]:
        total = total + w.sum(axis=1, keepdims=True)
    inverse = 1.0 / total
    probs = [w * inverse for w in weights]
    probs_low = [p.astype(jnp.bfloat16) for p in probs]
    out = jnp.dot(probs_low[0], values[0], preferred_element_type=jnp.float32)
    for r in range(1, slot_count):
        out = out + jnp.dot(probs_low[r], values[r], preferred_element_type=jnp.float32)
    out_low = out.astype(jnp.bfloat16)
    o_ref[...] = out_low
    delta = jnp.sum(do.astype(jnp.float32) * out_low.astype(jnp.float32), axis=1, keepdims=True)
    grad_q = None
    for r in range(slot_count):
        grad_p = lax.dot_general(do, values[r], trans_b, preferred_element_type=jnp.float32)
        grad_s = (probs[r] * (grad_p - delta)).astype(jnp.bfloat16)
        part = jnp.dot(grad_s, keys[r], preferred_element_type=jnp.float32)
        grad_q = part if grad_q is None else grad_q + part
        acc_ref[r, 0] += jnp.dot(q_t, grad_s, preferred_element_type=jnp.float32) * scale
        acc_ref[r, 1] += jnp.dot(do_t, probs_low[r], preferred_element_type=jnp.float32)
    dq_ref[...] = (grad_q * scale).astype(jnp.bfloat16)

    @pl.when((h == pl.num_programs(1) - 1) & (t == pl.num_programs(2) - 1))
    def _():
        for r in range(slot_count - 1):
            dsel_ref[r, 0] = acc_ref[r, 0].T
            dsel_ref[r, 1] = acc_ref[r, 1].T
        dko_ref[...] = acc_ref[slot_count - 1, 0].T
        dvo_ref[...] = acc_ref[slot_count - 1, 1].T


def attention(live, tp_info, query_stack, upstream_stack, fetched, key_heads, value_heads, group_size, first):
    tp_size, row_tile, _ = query_stack.shape
    tokens = tp_size * row_tile
    head_count = fetched.shape[0]
    q_cols = head_count * group_size * HD
    slot_count = TOPK + 1
    grid = (head_count, group_size, tp_size)
    kernel = functools.partial(
        attention_kernel, slot_count=slot_count, row_tile=row_tile, scale=1.0 / math.sqrt(HD)
    )

    def piece_in(g, h, t, live, tp):
        return ((tp[0] - t + tp_size) % tp_size, 0, g * group_size + h)

    def piece_out(g, h, t, live, tp):
        return ((t - tp[0] + tp_size) % tp_size, 0, g * group_size + h)

    in_block = pl.BlockSpec((None, row_tile, HD), piece_in)
    out_block = pl.BlockSpec((None, row_tile, HD), piece_out)
    sel_block = pl.BlockSpec((None, TOPK, 2, BLK, HD), lambda g, h, t, live, tp: (g, 0, 0, 0, 0))
    own_in = pl.BlockSpec((BLK, HD), lambda g, h, t, live, tp: (0, first + g))
    own_out = pl.BlockSpec((BLK, HD), lambda g, h, t, live, tp: (0, g))
    flops = 12 * head_count * group_size * tokens * slot_count * BLK * HD
    bytes_accessed = 2 * (4 * tokens * q_cols + 3 * fetched.size + 6 * tokens * head_count * HD)
    return pl.pallas_call(
        kernel,
        grid_spec=pltpu.PrefetchScalarGridSpec(
            num_scalar_prefetch=2,
            grid=grid,
            in_specs=[in_block, in_block, sel_block, own_in, own_in],
            out_specs=[out_block, out_block, sel_block, own_out, own_out],
            scratch_shapes=[pltpu.VMEM((slot_count, 2, HD, BLK), jnp.float32)],
        ),
        out_shape=[
            jax.ShapeDtypeStruct((tp_size, row_tile, q_cols), jnp.bfloat16),
            jax.ShapeDtypeStruct((tp_size, row_tile, q_cols), jnp.bfloat16),
            jax.ShapeDtypeStruct(fetched.shape, jnp.float32),
            jax.ShapeDtypeStruct((tokens, head_count * HD), jnp.float32),
            jax.ShapeDtypeStruct((tokens, head_count * HD), jnp.float32),
        ],
        compiler_params=pltpu.CompilerParams(
            dimension_semantics=("arbitrary", "arbitrary", "arbitrary"),
        ),
        cost_estimate=pl.CostEstimate(
            flops=flops,
            transcendentals=head_count * group_size * tokens * slot_count * BLK,
            bytes_accessed=bytes_accessed,
        ),
    )(live, tp_info, query_stack, upstream_stack, fetched, key_heads, value_heads)


def shift(x, axis, step, size):
    return lax.ppermute(x, axis, perm=[(s, (s + step) % size) for s in range(size)])


def tp_receive(x, me, size):
    width = x.shape[1] // size
    pieces = [lax.dynamic_slice_in_dim(x, me * width, width, 1)]
    for step in range(1, size):
        dest = (me + step) % size
        pieces.append(shift(lax.dynamic_slice_in_dim(x, dest * width, width, 1), "tp", step, size))
    return jnp.stack(pieces)


def tp_send(stack, me, size):
    pieces = [stack[0]] + [shift(stack[step], "tp", step, size) for step in range(1, size)]
    order = (me - jnp.arange(size, dtype=jnp.int32)) % size
    arranged = jnp.take(jnp.stack(pieces), order, axis=0)
    return arranged.transpose(1, 0, 2).reshape(stack.shape[1], size * stack.shape[2])


def source_order(stack, me, size):
    order = (me - jnp.arange(size, dtype=jnp.int32)) % size
    return jnp.take(stack, order, axis=0)


def body(queries, key_rows, value_rows, selected, own_flag, cotangent):
    holders = lax.axis_size("ctx")
    tp_size = lax.axis_size("tp")
    position = lax.axis_index("ctx")
    me = lax.axis_index("tp")
    rows_in = queries.shape[0]
    q_cols = queries.shape[1] // tp_size
    k_cols = key_rows.shape[1] // tp_size
    tokens = rows_in * tp_size
    assert tokens == BLK
    key_heads = source_order(tp_receive(key_rows, me, tp_size), me, tp_size).reshape(tokens, k_cols)
    value_heads = source_order(tp_receive(value_rows, me, tp_size), me, tp_size).reshape(tokens, k_cols)
    head_count = k_cols // HD
    group_size = q_cols // k_cols
    span_rows = BLK // holders

    kv = jnp.stack(
        [key_heads.reshape(holders, span_rows, head_count, HD),
         value_heads.reshape(holders, span_rows, head_count, HD)],
        axis=1,
    )
    spread = lax.all_to_all(kv, "ctx", split_axis=0, concat_axis=0, tiled=True)
    my_selected = lax.dynamic_index_in_dim(selected, position, 0, keepdims=False)
    my_flags = lax.dynamic_index_in_dim(own_flag, position, 0, keepdims=False)
    live_all = jnp.concatenate(
        [(my_selected < position).astype(jnp.int32), (my_flags == 1).astype(jnp.int32)[:, None]],
        axis=1,
    )
    tp_info = me.astype(jnp.int32).reshape(1)
    chunk_count = 2 if head_count % 2 == 0 else 1
    chunk_heads = head_count // chunk_count
    chunk_k_cols = chunk_heads * HD

    q_width = chunk_heads * group_size * HD

    def chunk_columns(x, chunk):
        return x.reshape(rows_in, tp_size, chunk_count, q_width)[:, :, chunk].reshape(
            rows_in, tp_size * q_width
        )

    results = []
    for chunk in range(chunk_count):
        first = chunk * chunk_heads
        query_stack = tp_receive(chunk_columns(queries, chunk), me, tp_size)
        upstream_stack = tp_receive(chunk_columns(cotangent, chunk), me, tp_size)
        chunk_selected = selected[:, first : first + chunk_heads]
        head_ids = jnp.arange(first, first + chunk_heads, dtype=jnp.int32)[None, :, None]
        send = spread[chunk_selected, :, :, head_ids, :]
        got = lax.all_to_all(send, "ctx", split_axis=0, concat_axis=4, tiled=True)
        fetched = got[0]
        live = live_all[first : first + chunk_heads].reshape(-1)
        attended, grad_queries, grad_sel, grad_key_own, grad_value_own = attention(
            live, tp_info, query_stack, upstream_stack, fetched, key_heads, value_heads,
            group_size, first,
        )
        attended = tp_send(attended, me, tp_size)
        grad_queries = tp_send(grad_queries, me, tp_size)

        send_back = grad_sel.astype(jnp.bfloat16).reshape(
            chunk_heads, TOPK, 2, holders, span_rows, HD
        )
        got_back = lax.all_to_all(send_back, "ctx", split_axis=3, concat_axis=1, tiled=True)
        flat = got_back.reshape(chunk_heads, holders * TOPK, 2 * span_rows * HD).astype(
            jnp.float32
        )
        targets = chunk_selected.transpose(1, 0, 2).reshape(chunk_heads, holders * TOPK)
        table = (
            targets[:, None, :] == jnp.arange(holders, dtype=jnp.int32)[None, :, None]
        ).astype(jnp.float32)
        summed = jnp.einsum("gjn,gnx->gjx", table, flat, precision=lax.Precision.HIGHEST)
        owner = summed.reshape(chunk_heads, holders, 2, span_rows, HD).astype(jnp.bfloat16)
        back = lax.all_to_all(owner, "ctx", split_axis=1, concat_axis=3, tiled=True)
        back = back[:, 0].astype(jnp.float32)
        total_keys = back[:, 0].transpose(1, 0, 2).reshape(tokens, chunk_k_cols) + grad_key_own
        total_values = (
            back[:, 1].transpose(1, 0, 2).reshape(tokens, chunk_k_cols) + grad_value_own
        )
        results.append((attended, grad_queries, total_keys, total_values))

    def rows_by_destination(total):
        stack = total.astype(jnp.bfloat16).reshape(tp_size, rows_in, k_cols)
        order = (me + jnp.arange(tp_size, dtype=jnp.int32)) % tp_size
        return tp_send(jnp.take(stack, order, axis=0), me, tp_size)

    def interleave(parts, width):
        stacked = jnp.stack([p.reshape(rows_in, tp_size, width) for p in parts], axis=2)
        return stacked.reshape(rows_in, tp_size * len(parts) * width)

    attended = interleave([r[0] for r in results], q_width)
    grad_queries = interleave([r[1] for r in results], q_width)
    total_keys = jnp.concatenate([r[2] for r in results], axis=1)
    total_values = jnp.concatenate([r[3] for r in results], axis=1)
    return (attended, grad_queries, rows_by_destination(total_keys), rows_by_destination(total_values))


def solution(mesh):
    in_specs = (
        P(("ctx", "tp"), None),
        P(("ctx", "tp"), None),
        P(("ctx", "tp"), None),
        P(None, "tp", None),
        P(None, "tp"),
        P(("ctx", "tp"), None),
    )
    out_specs = (
        P(("ctx", "tp"), None),
        P(("ctx", "tp"), None),
        P(("ctx", "tp"), None),
        P(("ctx", "tp"), None),
    )
    return jax.shard_map(body, mesh=mesh, in_specs=in_specs, out_specs=out_specs, check_vma=False)
```

```python
import functools
import math

import jax
import jax.numpy as jnp
from jax import lax
from jax.experimental import pallas as pl
from jax.experimental.pallas import tpu as pltpu
from jax.sharding import PartitionSpec as P

HD = 128
BLK = 512
TOPK = 3


def attention_kernel(
    live_ref, tp_ref, q_ref, do_ref, kvs_ref, ko_ref, vo_ref,
    o_ref, dq_ref, dsel_ref, dko_ref, dvo_ref, acc_ref, *, slot_count, row_tile, scale
):
    g = pl.program_id(0)
    h = pl.program_id(1)
    t = pl.program_id(2)

    @pl.when((h == 0) & (t == 0))
    def _():
        acc_ref[...] = jnp.zeros(acc_ref.shape, acc_ref.dtype)

    q = q_ref[...]
    do = do_ref[...]
    keys = [kvs_ref[r, 0] for r in range(slot_count - 1)] + [ko_ref[...]]
    values = [kvs_ref[r, 1] for r in range(slot_count - 1)] + [vo_ref[...]]
    trans_b = (((1,), (1,)), ((), ()))
    q_t = q.T
    do_t = do.T
    scores = []
    for r in range(slot_count):
        s = lax.dot_general(q, keys[r], trans_b, preferred_element_type=jnp.float32) * scale
        live = live_ref[g * slot_count + r] > 0
        if r == slot_count - 1:
            row = t * row_tile + lax.broadcasted_iota(jnp.int32, s.shape, 0)
            col = lax.broadcasted_iota(jnp.int32, s.shape, 1)
            s = jnp.where(live & (row >= col), s, -jnp.inf)
        else:
            s = jnp.where(live, s, -jnp.inf)
        scores.append(s)
    row_max = scores[0].max(axis=1, keepdims=True)
    for s in scores[1:]:
        row_max = jnp.maximum(row_max, s.max(axis=1, keepdims=True))
    weights = [jnp.exp(s - row_max) for s in scores]
    total = weights[0].sum(axis=1, keepdims=True)
    for w in weights[1:]:
        total = total + w.sum(axis=1, keepdims=True)
    inverse = 1.0 / total
    probs = [w * inverse for w in weights]
    probs_low = [p.astype(jnp.bfloat16) for p in probs]
    out = jnp.dot(probs_low[0], values[0], preferred_element_type=jnp.float32)
    for r in range(1, slot_count):
        out = out + jnp.dot(probs_low[r], values[r], preferred_element_type=jnp.float32)
    out_low = out.astype(jnp.bfloat16)
    o_ref[...] = out_low
    delta = jnp.sum(do.astype(jnp.float32) * out_low.astype(jnp.float32), axis=1, keepdims=True)
    grad_q = None
    for r in range(slot_count):
        grad_p = lax.dot_general(do, values[r], trans_b, preferred_element_type=jnp.float32)
        grad_s = (probs[r] * (grad_p - delta)).astype(jnp.bfloat16)
        part = jnp.dot(grad_s, keys[r], preferred_element_type=jnp.float32)
        grad_q = part if grad_q is None else grad_q + part
        acc_ref[r, 0] += jnp.dot(q_t, grad_s, preferred_element_type=jnp.float32) * scale
        acc_ref[r, 1] += jnp.dot(do_t, probs_low[r], preferred_element_type=jnp.float32)
    dq_ref[...] = (grad_q * scale).astype(jnp.bfloat16)

    @pl.when((h == pl.num_programs(1) - 1) & (t == pl.num_programs(2) - 1))
    def _():
        for r in range(slot_count - 1):
            dsel_ref[r, 0] = acc_ref[r, 0].T
            dsel_ref[r, 1] = acc_ref[r, 1].T
        dko_ref[...] = acc_ref[slot_count - 1, 0].T
        dvo_ref[...] = acc_ref[slot_count - 1, 1].T


def attention(live, tp_info, query_stack, upstream_stack, fetched, key_heads, value_heads, group_size, first):
    tp_size, row_tile, _ = query_stack.shape
    tokens = tp_size * row_tile
    head_count = fetched.shape[0]
    q_cols = head_count * group_size * HD
    slot_count = TOPK + 1
    grid = (head_count, group_size, tp_size)
    kernel = functools.partial(
        attention_kernel, slot_count=slot_count, row_tile=row_tile, scale=1.0 / math.sqrt(HD)
    )

    def piece_in(g, h, t, live, tp):
        return ((tp[0] - t + tp_size) % tp_size, 0, g * group_size + h)

    def piece_out(g, h, t, live, tp):
        return ((t - tp[0] + tp_size) % tp_size, 0, g * group_size + h)

    in_block = pl.BlockSpec((None, row_tile, HD), piece_in)
    out_block = pl.BlockSpec((None, row_tile, HD), piece_out)
    sel_block = pl.BlockSpec((None, TOPK, 2, BLK, HD), lambda g, h, t, live, tp: (g, 0, 0, 0, 0))
    own_in = pl.BlockSpec((BLK, HD), lambda g, h, t, live, tp: (0, first + g))
    own_out = pl.BlockSpec((BLK, HD), lambda g, h, t, live, tp: (0, g))
    flops = 12 * head_count * group_size * tokens * slot_count * BLK * HD
    bytes_accessed = 2 * (4 * tokens * q_cols + 3 * fetched.size + 6 * tokens * head_count * HD)
    return pl.pallas_call(
        kernel,
        grid_spec=pltpu.PrefetchScalarGridSpec(
            num_scalar_prefetch=2,
            grid=grid,
            in_specs=[in_block, in_block, sel_block, own_in, own_in],
            out_specs=[out_block, out_block, sel_block, own_out, own_out],
            scratch_shapes=[pltpu.VMEM((slot_count, 2, HD, BLK), jnp.float32)],
        ),
        out_shape=[
            jax.ShapeDtypeStruct((tp_size, row_tile, q_cols), jnp.bfloat16),
            jax.ShapeDtypeStruct((tp_size, row_tile, q_cols), jnp.bfloat16),
            jax.ShapeDtypeStruct(fetched.shape, jnp.float32),
            jax.ShapeDtypeStruct((tokens, head_count * HD), jnp.float32),
            jax.ShapeDtypeStruct((tokens, head_count * HD), jnp.float32),
        ],
        compiler_params=pltpu.CompilerParams(
            dimension_semantics=("arbitrary", "arbitrary", "arbitrary"),
        ),
        cost_estimate=pl.CostEstimate(
            flops=flops,
            transcendentals=head_count * group_size * tokens * slot_count * BLK,
            bytes_accessed=bytes_accessed,
        ),
    )(live, tp_info, query_stack, upstream_stack, fetched, key_heads, value_heads)


def shift(x, axis, step, size):
    return lax.ppermute(x, axis, perm=[(s, (s + step) % size) for s in range(size)])


def tp_receive(x, me, size, width, offset):
    stride = x.shape[1] // size
    pieces = [lax.dynamic_slice_in_dim(x, me * stride + offset, width, 1)]
    for step in range(1, size):
        dest = (me + step) % size
        piece = lax.dynamic_slice_in_dim(x, dest * stride + offset, width, 1)
        pieces.append(shift(piece, "tp", step, size))
    return jnp.stack(pieces)


def tp_receive_many(items, me, size):
    owns, sends = [], []
    for x, width, offset in items:
        stride = x.shape[1] // size
        owns.append(lax.dynamic_slice_in_dim(x, me * stride + offset, width, 1))
        sends.append(
            [lax.dynamic_slice_in_dim(x, ((me + step) % size) * stride + offset, width, 1)
             for step in range(1, size)]
        )
    received = [
        shift(tuple(s[step - 1] for s in sends), "tp", step, size) for step in range(1, size)
    ]
    return [
        jnp.stack([owns[i]] + [received[step - 1][i] for step in range(1, size)])
        for i in range(len(items))
    ]


def tp_send(stack, me, size):
    pieces = [stack[0]] + [shift(stack[step], "tp", step, size) for step in range(1, size)]
    order = (me - jnp.arange(size, dtype=jnp.int32)) % size
    arranged = jnp.take(jnp.stack(pieces), order, axis=0)
    return arranged.transpose(1, 0, 2).reshape(stack.shape[1], size * stack.shape[2])


def source_order(stack, me, size):
    order = (me - jnp.arange(size, dtype=jnp.int32)) % size
    return jnp.take(stack, order, axis=0)


def body(queries, key_rows, value_rows, selected, own_flag, cotangent):
    holders = lax.axis_size("ctx")
    tp_size = lax.axis_size("tp")
    position = lax.axis_index("ctx")
    me = lax.axis_index("tp")
    rows_in = queries.shape[0]
    q_cols = queries.shape[1] // tp_size
    k_cols = key_rows.shape[1] // tp_size
    tokens = rows_in * tp_size
    assert tokens == BLK
    head_count = k_cols // HD
    group_size = q_cols // k_cols
    chunk_count = 2 if head_count % 2 == 0 else 1
    chunk_heads = head_count // chunk_count
    q_width = chunk_heads * group_size * HD
    key_stack, value_stack, first_queries, first_upstream = tp_receive_many(
        [(key_rows, k_cols, 0), (value_rows, k_cols, 0), (queries, q_width, 0), (cotangent, q_width, 0)],
        me, tp_size,
    )
    key_heads = source_order(key_stack, me, tp_size).reshape(tokens, k_cols)
    value_heads = source_order(value_stack, me, tp_size).reshape(tokens, k_cols)
    head_count = k_cols // HD
    group_size = q_cols // k_cols
    span_rows = BLK // holders

    kv = jnp.stack(
        [key_heads.reshape(holders, span_rows, head_count, HD),
         value_heads.reshape(holders, span_rows, head_count, HD)],
        axis=1,
    )
    kv, first_queries, first_upstream = lax.optimization_barrier((kv, first_queries, first_upstream))
    spread = lax.all_to_all(kv, "ctx", split_axis=0, concat_axis=0, tiled=True)
    my_selected = lax.dynamic_index_in_dim(selected, position, 0, keepdims=False)
    my_flags = lax.dynamic_index_in_dim(own_flag, position, 0, keepdims=False)
    live_all = jnp.concatenate(
        [(my_selected < position).astype(jnp.int32), (my_flags == 1).astype(jnp.int32)[:, None]],
        axis=1,
    )
    tp_info = me.astype(jnp.int32).reshape(1)
    chunk_k_cols = chunk_heads * HD

    results = []
    for chunk in range(chunk_count):
        first = chunk * chunk_heads
        if chunk == 0:
            query_stack, upstream_stack = first_queries, first_upstream
        else:
            query_stack = tp_receive(queries, me, tp_size, q_width, chunk * q_width)
            upstream_stack = tp_receive(cotangent, me, tp_size, q_width, chunk * q_width)
        chunk_selected = selected[:, first : first + chunk_heads]
        head_ids = jnp.arange(first, first + chunk_heads, dtype=jnp.int32)[None, :, None]
        send = spread[chunk_selected, :, :, head_ids, :]
        got = lax.all_to_all(send, "ctx", split_axis=0, concat_axis=4, tiled=True)
        fetched = got[0]
        live = live_all[first : first + chunk_heads].reshape(-1)
        attended, grad_queries, grad_sel, grad_key_own, grad_value_own = attention(
            live, tp_info, query_stack, upstream_stack, fetched, key_heads, value_heads,
            group_size, first,
        )
        attended = tp_send(attended, me, tp_size)
        grad_queries = tp_send(grad_queries, me, tp_size)

        send_back = grad_sel.astype(jnp.bfloat16).reshape(
            chunk_heads, TOPK, 2, holders, span_rows, HD
        )
        got_back = lax.all_to_all(send_back, "ctx", split_axis=3, concat_axis=1, tiled=True)
        flat = got_back.reshape(chunk_heads, holders * TOPK, 2 * span_rows * HD).astype(
            jnp.float32
        )
        targets = chunk_selected.transpose(1, 0, 2).reshape(chunk_heads, holders * TOPK)
        table = (
            targets[:, None, :] == jnp.arange(holders, dtype=jnp.int32)[None, :, None]
        ).astype(jnp.float32)
        summed = jnp.einsum("gjn,gnx->gjx", table, flat, precision=lax.Precision.HIGHEST)
        owner = summed.reshape(chunk_heads, holders, 2, span_rows, HD).astype(jnp.bfloat16)
        back = lax.all_to_all(owner, "ctx", split_axis=1, concat_axis=3, tiled=True)
        back = back[:, 0].astype(jnp.float32)
        total_keys = back[:, 0].transpose(1, 0, 2).reshape(tokens, chunk_k_cols) + grad_key_own
        total_values = (
            back[:, 1].transpose(1, 0, 2).reshape(tokens, chunk_k_cols) + grad_value_own
        )
        results.append((attended, grad_queries, total_keys, total_values))

    def rows_by_destination(total):
        stack = total.astype(jnp.bfloat16).reshape(tp_size, rows_in, k_cols)
        order = (me + jnp.arange(tp_size, dtype=jnp.int32)) % tp_size
        return tp_send(jnp.take(stack, order, axis=0), me, tp_size)

    def interleave(parts, width):
        stacked = jnp.stack([p.reshape(rows_in, tp_size, width) for p in parts], axis=2)
        return stacked.reshape(rows_in, tp_size * len(parts) * width)

    attended = interleave([r[0] for r in results], q_width)
    grad_queries = interleave([r[1] for r in results], q_width)
    total_keys = jnp.concatenate([r[2] for r in results], axis=1)
    total_values = jnp.concatenate([r[3] for r in results], axis=1)
    return (attended, grad_queries, rows_by_destination(total_keys), rows_by_destination(total_values))


def solution(mesh):
    in_specs = (
        P(("ctx", "tp"), None),
        P(("ctx", "tp"), None),
        P(("ctx", "tp"), None),
        P(None, "tp", None),
        P(None, "tp"),
        P(("ctx", "tp"), None),
    )
    out_specs = (
        P(("ctx", "tp"), None),
        P(("ctx", "tp"), None),
        P(("ctx", "tp"), None),
        P(("ctx", "tp"), None),
    )
    return jax.shard_map(body, mesh=mesh, in_specs=in_specs, out_specs=out_specs, check_vma=False)
```

```python
import functools
import math

import jax
import jax.numpy as jnp
from jax import lax
from jax.experimental import pallas as pl
from jax.experimental.pallas import tpu as pltpu
from jax.sharding import PartitionSpec as P

HD = 128
BLK = 512
TOPK = 3


def attention_kernel(
    live_ref, tp_ref, q_ref, do_ref, kvs_ref, ko_ref, vo_ref,
    o_ref, dq_ref, dsel_ref, dko_ref, dvo_ref, acc_ref, *, slot_count, row_tile, scale
):
    g = pl.program_id(0)
    h = pl.program_id(1)
    t = pl.program_id(2)

    @pl.when((h == 0) & (t == 0))
    def _():
        acc_ref[...] = jnp.zeros(acc_ref.shape, acc_ref.dtype)

    q = q_ref[...]
    do = do_ref[...]
    keys = [kvs_ref[r, 0] for r in range(slot_count - 1)] + [ko_ref[...]]
    values = [kvs_ref[r, 1] for r in range(slot_count - 1)] + [vo_ref[...]]
    trans_b = (((1,), (1,)), ((), ()))
    q_t = q.T
    do_t = do.T
    scores = []
    for r in range(slot_count):
        s = lax.dot_general(q, keys[r], trans_b, preferred_element_type=jnp.float32) * scale
        live = live_ref[g * slot_count + r] > 0
        if r == slot_count - 1:
            row = t * row_tile + lax.broadcasted_iota(jnp.int32, s.shape, 0)
            col = lax.broadcasted_iota(jnp.int32, s.shape, 1)
            s = jnp.where(live & (row >= col), s, -jnp.inf)
        else:
            s = jnp.where(live, s, -jnp.inf)
        scores.append(s)
    row_max = scores[0].max(axis=1, keepdims=True)
    for s in scores[1:]:
        row_max = jnp.maximum(row_max, s.max(axis=1, keepdims=True))
    weights = [jnp.exp(s - row_max) for s in scores]
    total = weights[0].sum(axis=1, keepdims=True)
    for w in weights[1:]:
        total = total + w.sum(axis=1, keepdims=True)
    inverse = 1.0 / total
    probs = [w * inverse for w in weights]
    probs_low = [p.astype(jnp.bfloat16) for p in probs]
    out = jnp.dot(probs_low[0], values[0], preferred_element_type=jnp.float32)
    for r in range(1, slot_count):
        out = out + jnp.dot(probs_low[r], values[r], preferred_element_type=jnp.float32)
    out_low = out.astype(jnp.bfloat16)
    o_ref[...] = out_low
    delta = jnp.sum(do.astype(jnp.float32) * out_low.astype(jnp.float32), axis=1, keepdims=True)
    grad_q = None
    for r in range(slot_count):
        grad_p = lax.dot_general(do, values[r], trans_b, preferred_element_type=jnp.float32)
        grad_s = (probs[r] * (grad_p - delta)).astype(jnp.bfloat16)
        part = jnp.dot(grad_s, keys[r], preferred_element_type=jnp.float32)
        grad_q = part if grad_q is None else grad_q + part
        acc_ref[r, 0] += jnp.dot(q_t, grad_s, preferred_element_type=jnp.float32) * scale
        acc_ref[r, 1] += jnp.dot(do_t, probs_low[r], preferred_element_type=jnp.float32)
    dq_ref[...] = (grad_q * scale).astype(jnp.bfloat16)

    @pl.when((h == pl.num_programs(1) - 1) & (t == pl.num_programs(2) - 1))
    def _():
        for r in range(slot_count - 1):
            dsel_ref[r, 0] = acc_ref[r, 0].T
            dsel_ref[r, 1] = acc_ref[r, 1].T
        dko_ref[...] = acc_ref[slot_count - 1, 0].T
        dvo_ref[...] = acc_ref[slot_count - 1, 1].T


def attention(live, tp_info, query_stack, upstream_stack, fetched, key_heads, value_heads, group_size, first):
    tp_size, row_tile, _ = query_stack.shape
    tokens = tp_size * row_tile
    head_count = fetched.shape[0]
    q_cols = head_count * group_size * HD
    slot_count = TOPK + 1
    grid = (head_count, group_size, tp_size)
    kernel = functools.partial(
        attention_kernel, slot_count=slot_count, row_tile=row_tile, scale=1.0 / math.sqrt(HD)
    )

    def piece_in(g, h, t, live, tp):
        return ((tp[0] - t + tp_size) % tp_size, 0, g * group_size + h)

    def piece_out(g, h, t, live, tp):
        return ((t - tp[0] + tp_size) % tp_size, 0, g * group_size + h)

    in_block = pl.BlockSpec((None, row_tile, HD), piece_in)
    out_block = pl.BlockSpec((None, row_tile, HD), piece_out)
    sel_block = pl.BlockSpec((None, TOPK, 2, BLK, HD), lambda g, h, t, live, tp: (g, 0, 0, 0, 0))
    own_in = pl.BlockSpec((BLK, HD), lambda g, h, t, live, tp: (0, first + g))
    own_out = pl.BlockSpec((BLK, HD), lambda g, h, t, live, tp: (0, g))
    flops = 12 * head_count * group_size * tokens * slot_count * BLK * HD
    bytes_accessed = 2 * (4 * tokens * q_cols + 3 * fetched.size + 6 * tokens * head_count * HD)
    return pl.pallas_call(
        kernel,
        grid_spec=pltpu.PrefetchScalarGridSpec(
            num_scalar_prefetch=2,
            grid=grid,
            in_specs=[in_block, in_block, sel_block, own_in, own_in],
            out_specs=[out_block, out_block, sel_block, own_out, own_out],
            scratch_shapes=[pltpu.VMEM((slot_count, 2, HD, BLK), jnp.float32)],
        ),
        out_shape=[
            jax.ShapeDtypeStruct((tp_size, row_tile, q_cols), jnp.bfloat16),
            jax.ShapeDtypeStruct((tp_size, row_tile, q_cols), jnp.bfloat16),
            jax.ShapeDtypeStruct(fetched.shape, jnp.float32),
            jax.ShapeDtypeStruct((tokens, head_count * HD), jnp.float32),
            jax.ShapeDtypeStruct((tokens, head_count * HD), jnp.float32),
        ],
        compiler_params=pltpu.CompilerParams(
            dimension_semantics=("arbitrary", "arbitrary", "arbitrary"),
        ),
        cost_estimate=pl.CostEstimate(
            flops=flops,
            transcendentals=head_count * group_size * tokens * slot_count * BLK,
            bytes_accessed=bytes_accessed,
        ),
    )(live, tp_info, query_stack, upstream_stack, fetched, key_heads, value_heads)


def shift(x, axis, step, size):
    return lax.ppermute(x, axis, perm=[(s, (s + step) % size) for s in range(size)])


def tp_receive(x, me, size, width, offset):
    stride = x.shape[1] // size
    pieces = [lax.dynamic_slice_in_dim(x, me * stride + offset, width, 1)]
    for step in range(1, size):
        dest = (me + step) % size
        piece = lax.dynamic_slice_in_dim(x, dest * stride + offset, width, 1)
        pieces.append(shift(piece, "tp", step, size))
    return jnp.stack(pieces)


def tp_receive_many(items, me, size):
    owns, sends = [], []
    for x, width, offset in items:
        stride = x.shape[1] // size
        owns.append(lax.dynamic_slice_in_dim(x, me * stride + offset, width, 1))
        sends.append(
            [lax.dynamic_slice_in_dim(x, ((me + step) % size) * stride + offset, width, 1)
             for step in range(1, size)]
        )
    received = [
        shift(tuple(s[step - 1] for s in sends), "tp", step, size) for step in range(1, size)
    ]
    return [
        jnp.stack([owns[i]] + [received[step - 1][i] for step in range(1, size)])
        for i in range(len(items))
    ]


def tp_send(stack, me, size):
    pieces = [stack[0]] + [shift(stack[step], "tp", step, size) for step in range(1, size)]
    order = (me - jnp.arange(size, dtype=jnp.int32)) % size
    arranged = jnp.take(jnp.stack(pieces), order, axis=0)
    return arranged.transpose(1, 0, 2).reshape(stack.shape[1], size * stack.shape[2])


def source_order(stack, me, size):
    order = (me - jnp.arange(size, dtype=jnp.int32)) % size
    return jnp.take(stack, order, axis=0)


def body(queries, key_rows, value_rows, selected, own_flag, cotangent):
    holders = lax.axis_size("ctx")
    tp_size = lax.axis_size("tp")
    position = lax.axis_index("ctx")
    me = lax.axis_index("tp")
    rows_in = queries.shape[0]
    q_cols = queries.shape[1] // tp_size
    k_cols = key_rows.shape[1] // tp_size
    tokens = rows_in * tp_size
    assert tokens == BLK
    head_count = k_cols // HD
    group_size = q_cols // k_cols
    chunk_count = 2 if head_count % 2 == 0 else 1
    chunk_heads = head_count // chunk_count
    q_width = chunk_heads * group_size * HD
    key_stack, value_stack, first_queries, first_upstream = tp_receive_many(
        [(key_rows, k_cols, 0), (value_rows, k_cols, 0), (queries, q_width, 0), (cotangent, q_width, 0)],
        me, tp_size,
    )
    key_heads = source_order(key_stack, me, tp_size).reshape(tokens, k_cols)
    value_heads = source_order(value_stack, me, tp_size).reshape(tokens, k_cols)
    head_count = k_cols // HD
    group_size = q_cols // k_cols
    span_rows = BLK // holders

    kv = jnp.stack(
        [key_heads.reshape(holders, span_rows, head_count, HD),
         value_heads.reshape(holders, span_rows, head_count, HD)],
        axis=1,
    )
    kv, first_queries, first_upstream = lax.optimization_barrier((kv, first_queries, first_upstream))
    spread = lax.all_to_all(kv, "ctx", split_axis=0, concat_axis=0, tiled=True)
    my_selected = lax.dynamic_index_in_dim(selected, position, 0, keepdims=False)
    my_flags = lax.dynamic_index_in_dim(own_flag, position, 0, keepdims=False)
    live_all = jnp.concatenate(
        [(my_selected < position).astype(jnp.int32), (my_flags == 1).astype(jnp.int32)[:, None]],
        axis=1,
    )
    tp_info = me.astype(jnp.int32).reshape(1)
    chunk_k_cols = chunk_heads * HD

    next_stacks = [
        tp_receive(queries, me, tp_size, q_width, (chunk_count - 1) * q_width),
        tp_receive(cotangent, me, tp_size, q_width, (chunk_count - 1) * q_width),
    ]
    results = []
    for chunk in range(chunk_count):
        first = chunk * chunk_heads
        chunk_selected = selected[:, first : first + chunk_heads]
        head_ids = jnp.arange(first, first + chunk_heads, dtype=jnp.int32)[None, :, None]
        send = spread[chunk_selected, :, :, head_ids, :]
        if chunk == 0:
            query_stack, upstream_stack = first_queries, first_upstream
            send, *next_stacks = lax.optimization_barrier((send, *next_stacks))
        else:
            query_stack, upstream_stack = next_stacks
        got = lax.all_to_all(send, "ctx", split_axis=0, concat_axis=4, tiled=True)
        fetched = got[0]
        live = live_all[first : first + chunk_heads].reshape(-1)
        attended, grad_queries, grad_sel, grad_key_own, grad_value_own = attention(
            live, tp_info, query_stack, upstream_stack, fetched, key_heads, value_heads,
            group_size, first,
        )
        attended = tp_send(attended, me, tp_size)
        grad_queries = tp_send(grad_queries, me, tp_size)

        send_back = grad_sel.astype(jnp.bfloat16).reshape(
            chunk_heads, TOPK, 2, holders, span_rows, HD
        )
        got_back = lax.all_to_all(send_back, "ctx", split_axis=3, concat_axis=1, tiled=True)
        flat = got_back.reshape(chunk_heads, holders * TOPK, 2 * span_rows * HD).astype(
            jnp.float32
        )
        targets = chunk_selected.transpose(1, 0, 2).reshape(chunk_heads, holders * TOPK)
        table = (
            targets[:, None, :] == jnp.arange(holders, dtype=jnp.int32)[None, :, None]
        ).astype(jnp.float32)
        summed = jnp.einsum("gjn,gnx->gjx", table, flat, precision=lax.Precision.HIGHEST)
        owner = summed.reshape(chunk_heads, holders, 2, span_rows, HD).astype(jnp.bfloat16)
        back = lax.all_to_all(owner, "ctx", split_axis=1, concat_axis=3, tiled=True)
        back = back[:, 0].astype(jnp.float32)
        total_keys = back[:, 0].transpose(1, 0, 2).reshape(tokens, chunk_k_cols) + grad_key_own
        total_values = (
            back[:, 1].transpose(1, 0, 2).reshape(tokens, chunk_k_cols) + grad_value_own
        )
        results.append((attended, grad_queries, total_keys, total_values))

    def rows_by_destination(total):
        stack = total.astype(jnp.bfloat16).reshape(tp_size, rows_in, k_cols)
        order = (me + jnp.arange(tp_size, dtype=jnp.int32)) % tp_size
        return tp_send(jnp.take(stack, order, axis=0), me, tp_size)

    def interleave(parts, width):
        stacked = jnp.stack([p.reshape(rows_in, tp_size, width) for p in parts], axis=2)
        return stacked.reshape(rows_in, tp_size * len(parts) * width)

    attended = interleave([r[0] for r in results], q_width)
    grad_queries = interleave([r[1] for r in results], q_width)
    total_keys = jnp.concatenate([r[2] for r in results], axis=1)
    total_values = jnp.concatenate([r[3] for r in results], axis=1)
    return (attended, grad_queries, rows_by_destination(total_keys), rows_by_destination(total_values))


def solution(mesh):
    in_specs = (
        P(("ctx", "tp"), None),
        P(("ctx", "tp"), None),
        P(("ctx", "tp"), None),
        P(None, "tp", None),
        P(None, "tp"),
        P(("ctx", "tp"), None),
    )
    out_specs = (
        P(("ctx", "tp"), None),
        P(("ctx", "tp"), None),
        P(("ctx", "tp"), None),
        P(("ctx", "tp"), None),
    )
    return jax.shard_map(body, mesh=mesh, in_specs=in_specs, out_specs=out_specs, check_vma=False)
```

```python
import functools
import math

import jax
import jax.numpy as jnp
from jax import lax
from jax.experimental import pallas as pl
from jax.experimental.pallas import tpu as pltpu
from jax.sharding import PartitionSpec as P

HD = 128
BLK = 512
TOPK = 3


def attention_kernel(
    live_ref, tp_ref, q_ref, do_ref, kvs_ref, ko_ref, vo_ref,
    o_ref, dq_ref, dsel_ref, dko_ref, dvo_ref, acc_ref, *, slot_count, row_tile, scale
):
    g = pl.program_id(0)
    h = pl.program_id(1)
    t = pl.program_id(2)

    @pl.when((h == 0) & (t == 0))
    def _():
        acc_ref[...] = jnp.zeros(acc_ref.shape, acc_ref.dtype)

    q = q_ref[...]
    do = do_ref[...]
    keys = [kvs_ref[r, 0] for r in range(slot_count - 1)] + [ko_ref[...]]
    values = [kvs_ref[r, 1] for r in range(slot_count - 1)] + [vo_ref[...]]
    trans_b = (((1,), (1,)), ((), ()))
    q_t = q.T
    do_t = do.T
    scores = []
    for r in range(slot_count):
        s = lax.dot_general(q, keys[r], trans_b, preferred_element_type=jnp.float32) * scale
        live = live_ref[g * slot_count + r] > 0
        if r == slot_count - 1:
            row = t * row_tile + lax.broadcasted_iota(jnp.int32, s.shape, 0)
            col = lax.broadcasted_iota(jnp.int32, s.shape, 1)
            s = jnp.where(live & (row >= col), s, -jnp.inf)
        else:
            s = jnp.where(live, s, -jnp.inf)
        scores.append(s)
    row_max = scores[0].max(axis=1, keepdims=True)
    for s in scores[1:]:
        row_max = jnp.maximum(row_max, s.max(axis=1, keepdims=True))
    weights = [jnp.exp(s - row_max) for s in scores]
    total = weights[0].sum(axis=1, keepdims=True)
    for w in weights[1:]:
        total = total + w.sum(axis=1, keepdims=True)
    inverse = 1.0 / total
    probs = [w * inverse for w in weights]
    probs_low = [p.astype(jnp.bfloat16) for p in probs]
    out = jnp.dot(probs_low[0], values[0], preferred_element_type=jnp.float32)
    for r in range(1, slot_count):
        out = out + jnp.dot(probs_low[r], values[r], preferred_element_type=jnp.float32)
    out_low = out.astype(jnp.bfloat16)
    o_ref[...] = out_low
    delta = jnp.sum(do.astype(jnp.float32) * out_low.astype(jnp.float32), axis=1, keepdims=True)
    grad_q = None
    for r in range(slot_count):
        grad_p = lax.dot_general(do, values[r], trans_b, preferred_element_type=jnp.float32)
        grad_s = (probs[r] * (grad_p - delta)).astype(jnp.bfloat16)
        part = jnp.dot(grad_s, keys[r], preferred_element_type=jnp.float32)
        grad_q = part if grad_q is None else grad_q + part
        acc_ref[r, 0] += jnp.dot(q_t, grad_s, preferred_element_type=jnp.float32) * scale
        acc_ref[r, 1] += jnp.dot(do_t, probs_low[r], preferred_element_type=jnp.float32)
    dq_ref[...] = (grad_q * scale).astype(jnp.bfloat16)

    @pl.when((h == pl.num_programs(1) - 1) & (t == pl.num_programs(2) - 1))
    def _():
        for r in range(slot_count - 1):
            dsel_ref[r, 0] = acc_ref[r, 0].T
            dsel_ref[r, 1] = acc_ref[r, 1].T
        dko_ref[...] = acc_ref[slot_count - 1, 0].T
        dvo_ref[...] = acc_ref[slot_count - 1, 1].T


def attention(live, tp_info, query_stack, upstream_stack, fetched, key_heads, value_heads, group_size, first):
    tp_size, row_tile, _ = query_stack.shape
    tokens = tp_size * row_tile
    head_count = fetched.shape[0]
    q_cols = head_count * group_size * HD
    slot_count = TOPK + 1
    grid = (head_count, group_size, tp_size)
    kernel = functools.partial(
        attention_kernel, slot_count=slot_count, row_tile=row_tile, scale=1.0 / math.sqrt(HD)
    )

    def piece_in(g, h, t, live, tp):
        return ((tp[0] - t + tp_size) % tp_size, 0, g * group_size + h)

    def piece_out(g, h, t, live, tp):
        return ((t - tp[0] + tp_size) % tp_size, 0, g * group_size + h)

    in_block = pl.BlockSpec((None, row_tile, HD), piece_in)
    out_block = pl.BlockSpec((None, row_tile, HD), piece_out)
    sel_block = pl.BlockSpec((None, TOPK, 2, BLK, HD), lambda g, h, t, live, tp: (g, 0, 0, 0, 0))
    own_in = pl.BlockSpec((BLK, HD), lambda g, h, t, live, tp: (0, first + g))
    own_out = pl.BlockSpec((BLK, HD), lambda g, h, t, live, tp: (0, g))
    flops = 12 * head_count * group_size * tokens * slot_count * BLK * HD
    bytes_accessed = 2 * (4 * tokens * q_cols + 3 * fetched.size + 6 * tokens * head_count * HD)
    return pl.pallas_call(
        kernel,
        grid_spec=pltpu.PrefetchScalarGridSpec(
            num_scalar_prefetch=2,
            grid=grid,
            in_specs=[in_block, in_block, sel_block, own_in, own_in],
            out_specs=[out_block, out_block, sel_block, own_out, own_out],
            scratch_shapes=[pltpu.VMEM((slot_count, 2, HD, BLK), jnp.float32)],
        ),
        out_shape=[
            jax.ShapeDtypeStruct((tp_size, row_tile, q_cols), jnp.bfloat16),
            jax.ShapeDtypeStruct((tp_size, row_tile, q_cols), jnp.bfloat16),
            jax.ShapeDtypeStruct(fetched.shape, jnp.float32),
            jax.ShapeDtypeStruct((tokens, head_count * HD), jnp.float32),
            jax.ShapeDtypeStruct((tokens, head_count * HD), jnp.float32),
        ],
        compiler_params=pltpu.CompilerParams(
            dimension_semantics=("arbitrary", "arbitrary", "arbitrary"),
        ),
        cost_estimate=pl.CostEstimate(
            flops=flops,
            transcendentals=head_count * group_size * tokens * slot_count * BLK,
            bytes_accessed=bytes_accessed,
        ),
    )(live, tp_info, query_stack, upstream_stack, fetched, key_heads, value_heads)


def shift(x, axis, step, size):
    return lax.ppermute(x, axis, perm=[(s, (s + step) % size) for s in range(size)])


def tp_receive(x, me, size, width, offset):
    stride = x.shape[1] // size
    pieces = [lax.dynamic_slice_in_dim(x, me * stride + offset, width, 1)]
    for step in range(1, size):
        dest = (me + step) % size
        piece = lax.dynamic_slice_in_dim(x, dest * stride + offset, width, 1)
        pieces.append(shift(piece, "tp", step, size))
    return jnp.stack(pieces)


def tp_receive_many(items, me, size):
    owns, sends = [], []
    for x, width, offset in items:
        stride = x.shape[1] // size
        owns.append(lax.dynamic_slice_in_dim(x, me * stride + offset, width, 1))
        sends.append(
            [lax.dynamic_slice_in_dim(x, ((me + step) % size) * stride + offset, width, 1)
             for step in range(1, size)]
        )
    received = [
        shift(tuple(s[step - 1] for s in sends), "tp", step, size) for step in range(1, size)
    ]
    return [
        jnp.stack([owns[i]] + [received[step - 1][i] for step in range(1, size)])
        for i in range(len(items))
    ]


def tp_send(stack, me, size):
    pieces = [stack[0]] + [shift(stack[step], "tp", step, size) for step in range(1, size)]
    order = (me - jnp.arange(size, dtype=jnp.int32)) % size
    arranged = jnp.take(jnp.stack(pieces), order, axis=0)
    return arranged.transpose(1, 0, 2).reshape(stack.shape[1], size * stack.shape[2])


def source_order(stack, me, size):
    order = (me - jnp.arange(size, dtype=jnp.int32)) % size
    return jnp.take(stack, order, axis=0)


def body(queries, key_rows, value_rows, selected, own_flag, cotangent):
    holders = lax.axis_size("ctx")
    tp_size = lax.axis_size("tp")
    position = lax.axis_index("ctx")
    me = lax.axis_index("tp")
    rows_in = queries.shape[0]
    q_cols = queries.shape[1] // tp_size
    k_cols = key_rows.shape[1] // tp_size
    tokens = rows_in * tp_size
    assert tokens == BLK
    head_count = k_cols // HD
    group_size = q_cols // k_cols
    chunk_count = 2 if head_count % 2 == 0 else 1
    chunk_heads = head_count // chunk_count
    q_width = chunk_heads * group_size * HD
    key_stack, value_stack, first_queries, first_upstream = tp_receive_many(
        [(key_rows, k_cols, 0), (value_rows, k_cols, 0), (queries, q_width, 0), (cotangent, q_width, 0)],
        me, tp_size,
    )
    key_heads = source_order(key_stack, me, tp_size).reshape(tokens, k_cols)
    value_heads = source_order(value_stack, me, tp_size).reshape(tokens, k_cols)
    head_count = k_cols // HD
    group_size = q_cols // k_cols
    span_rows = BLK // holders

    kv = jnp.stack(
        [key_heads.reshape(holders, span_rows, head_count, HD),
         value_heads.reshape(holders, span_rows, head_count, HD)],
        axis=1,
    )
    spread = lax.all_to_all(kv, "ctx", split_axis=0, concat_axis=0, tiled=True)
    my_selected = lax.dynamic_index_in_dim(selected, position, 0, keepdims=False)
    my_flags = lax.dynamic_index_in_dim(own_flag, position, 0, keepdims=False)
    live_all = jnp.concatenate(
        [(my_selected < position).astype(jnp.int32), (my_flags == 1).astype(jnp.int32)[:, None]],
        axis=1,
    )
    tp_info = me.astype(jnp.int32).reshape(1)
    chunk_k_cols = chunk_heads * HD

    next_stacks = [
        tp_receive(queries, me, tp_size, q_width, (chunk_count - 1) * q_width),
        tp_receive(cotangent, me, tp_size, q_width, (chunk_count - 1) * q_width),
    ]
    results = []
    for chunk in range(chunk_count):
        first = chunk * chunk_heads
        chunk_selected = selected[:, first : first + chunk_heads]
        head_ids = jnp.arange(first, first + chunk_heads, dtype=jnp.int32)[None, :, None]
        send = spread[chunk_selected, :, :, head_ids, :]
        if chunk == 0:
            query_stack, upstream_stack = first_queries, first_upstream
            send, *next_stacks = lax.optimization_barrier((send, *next_stacks))
        else:
            query_stack, upstream_stack = next_stacks
            send, _, _ = lax.optimization_barrier((send, first_queries, first_upstream))
        got = lax.all_to_all(send, "ctx", split_axis=0, concat_axis=4, tiled=True)
        fetched = got[0]
        live = live_all[first : first + chunk_heads].reshape(-1)
        attended, grad_queries, grad_sel, grad_key_own, grad_value_own = attention(
            live, tp_info, query_stack, upstream_stack, fetched, key_heads, value_heads,
            group_size, first,
        )
        attended = tp_send(attended, me, tp_size)
        grad_queries = tp_send(grad_queries, me, tp_size)

        send_back = grad_sel.astype(jnp.bfloat16).reshape(
            chunk_heads, TOPK, 2, holders, span_rows, HD
        )
        got_back = lax.all_to_all(send_back, "ctx", split_axis=3, concat_axis=1, tiled=True)
        flat = got_back.reshape(chunk_heads, holders * TOPK, 2 * span_rows * HD).astype(
            jnp.float32
        )
        targets = chunk_selected.transpose(1, 0, 2).reshape(chunk_heads, holders * TOPK)
        table = (
            targets[:, None, :] == jnp.arange(holders, dtype=jnp.int32)[None, :, None]
        ).astype(jnp.float32)
        summed = jnp.einsum("gjn,gnx->gjx", table, flat, precision=lax.Precision.HIGHEST)
        owner = summed.reshape(chunk_heads, holders, 2, span_rows, HD).astype(jnp.bfloat16)
        back = lax.all_to_all(owner, "ctx", split_axis=1, concat_axis=3, tiled=True)
        back = back[:, 0].astype(jnp.float32)
        total_keys = back[:, 0].transpose(1, 0, 2).reshape(tokens, chunk_k_cols) + grad_key_own
        total_values = (
            back[:, 1].transpose(1, 0, 2).reshape(tokens, chunk_k_cols) + grad_value_own
        )
        results.append((attended, grad_queries, total_keys, total_values))

    def rows_by_destination(total):
        stack = total.astype(jnp.bfloat16).reshape(tp_size, rows_in, k_cols)
        order = (me + jnp.arange(tp_size, dtype=jnp.int32)) % tp_size
        return tp_send(jnp.take(stack, order, axis=0), me, tp_size)

    def interleave(parts, width):
        stacked = jnp.stack([p.reshape(rows_in, tp_size, width) for p in parts], axis=2)
        return stacked.reshape(rows_in, tp_size * len(parts) * width)

    attended = interleave([r[0] for r in results], q_width)
    grad_queries = interleave([r[1] for r in results], q_width)
    total_keys = jnp.concatenate([r[2] for r in results], axis=1)
    total_values = jnp.concatenate([r[3] for r in results], axis=1)
    return (attended, grad_queries, rows_by_destination(total_keys), rows_by_destination(total_values))


def solution(mesh):
    in_specs = (
        P(("ctx", "tp"), None),
        P(("ctx", "tp"), None),
        P(("ctx", "tp"), None),
        P(None, "tp", None),
        P(None, "tp"),
        P(("ctx", "tp"), None),
    )
    out_specs = (
        P(("ctx", "tp"), None),
        P(("ctx", "tp"), None),
        P(("ctx", "tp"), None),
        P(("ctx", "tp"), None),
    )
    return jax.shard_map(body, mesh=mesh, in_specs=in_specs, out_specs=out_specs, check_vma=False)
```

```python
import functools
import math

import jax
import jax.numpy as jnp
from jax import lax
from jax.experimental import pallas as pl
from jax.experimental.pallas import tpu as pltpu
from jax.sharding import PartitionSpec as P

HD = 128
BLK = 512
TOPK = 3


def attention_kernel(
    live_ref, tp_ref, q_ref, do_ref, kvs_ref, ko_ref, vo_ref,
    o_ref, dq_ref, dsel_ref, dko_ref, dvo_ref, acc_ref, *, slot_count, row_tile, scale
):
    g = pl.program_id(0)
    h = pl.program_id(1)
    t = pl.program_id(2)

    @pl.when((h == 0) & (t == 0))
    def _():
        acc_ref[...] = jnp.zeros(acc_ref.shape, acc_ref.dtype)

    q = q_ref[...]
    do = do_ref[...]
    keys = [kvs_ref[r, 0] for r in range(slot_count - 1)] + [ko_ref[...]]
    values = [kvs_ref[r, 1] for r in range(slot_count - 1)] + [vo_ref[...]]
    trans_b = (((1,), (1,)), ((), ()))
    q_t = q.T
    do_t = do.T
    scores = []
    for r in range(slot_count):
        s = lax.dot_general(q, keys[r], trans_b, preferred_element_type=jnp.float32) * scale
        live = live_ref[g * slot_count + r] > 0
        if r == slot_count - 1:
            row = t * row_tile + lax.broadcasted_iota(jnp.int32, s.shape, 0)
            col = lax.broadcasted_iota(jnp.int32, s.shape, 1)
            s = jnp.where(live & (row >= col), s, -jnp.inf)
        else:
            s = jnp.where(live, s, -jnp.inf)
        scores.append(s)
    row_max = scores[0].max(axis=1, keepdims=True)
    for s in scores[1:]:
        row_max = jnp.maximum(row_max, s.max(axis=1, keepdims=True))
    weights = [jnp.exp(s - row_max) for s in scores]
    total = weights[0].sum(axis=1, keepdims=True)
    for w in weights[1:]:
        total = total + w.sum(axis=1, keepdims=True)
    inverse = 1.0 / total
    probs = [w * inverse for w in weights]
    probs_low = [p.astype(jnp.bfloat16) for p in probs]
    out = jnp.dot(probs_low[0], values[0], preferred_element_type=jnp.float32)
    for r in range(1, slot_count):
        out = out + jnp.dot(probs_low[r], values[r], preferred_element_type=jnp.float32)
    out_low = out.astype(jnp.bfloat16)
    o_ref[...] = out_low
    delta = jnp.sum(do.astype(jnp.float32) * out_low.astype(jnp.float32), axis=1, keepdims=True)
    grad_q = None
    for r in range(slot_count):
        grad_p = lax.dot_general(do, values[r], trans_b, preferred_element_type=jnp.float32)
        grad_s = (probs[r] * (grad_p - delta)).astype(jnp.bfloat16)
        part = jnp.dot(grad_s, keys[r], preferred_element_type=jnp.float32)
        grad_q = part if grad_q is None else grad_q + part
        acc_ref[r, 0] += jnp.dot(q_t, grad_s, preferred_element_type=jnp.float32) * scale
        acc_ref[r, 1] += jnp.dot(do_t, probs_low[r], preferred_element_type=jnp.float32)
    dq_ref[...] = (grad_q * scale).astype(jnp.bfloat16)

    @pl.when((h == pl.num_programs(1) - 1) & (t == pl.num_programs(2) - 1))
    def _():
        for r in range(slot_count - 1):
            dsel_ref[r, 0] = acc_ref[r, 0].T
            dsel_ref[r, 1] = acc_ref[r, 1].T
        dko_ref[...] = acc_ref[slot_count - 1, 0].T
        dvo_ref[...] = acc_ref[slot_count - 1, 1].T


def attention(live, tp_info, query_stack, upstream_stack, fetched, key_heads, value_heads, group_size, first):
    tp_size, row_tile, _ = query_stack.shape
    tokens = tp_size * row_tile
    head_count = fetched.shape[0]
    q_cols = head_count * group_size * HD
    slot_count = TOPK + 1
    grid = (head_count, group_size, tp_size)
    kernel = functools.partial(
        attention_kernel, slot_count=slot_count, row_tile=row_tile, scale=1.0 / math.sqrt(HD)
    )

    def piece_in(g, h, t, live, tp):
        return ((tp[0] - t + tp_size) % tp_size, 0, g * group_size + h)

    def piece_out(g, h, t, live, tp):
        return ((t - tp[0] + tp_size) % tp_size, 0, g * group_size + h)

    in_block = pl.BlockSpec((None, row_tile, HD), piece_in)
    out_block = pl.BlockSpec((None, row_tile, HD), piece_out)
    sel_block = pl.BlockSpec((None, TOPK, 2, BLK, HD), lambda g, h, t, live, tp: (g, 0, 0, 0, 0))
    own_in = pl.BlockSpec((BLK, HD), lambda g, h, t, live, tp: (0, first + g))
    own_out = pl.BlockSpec((BLK, HD), lambda g, h, t, live, tp: (0, g))
    flops = 12 * head_count * group_size * tokens * slot_count * BLK * HD
    bytes_accessed = 2 * (4 * tokens * q_cols + 3 * fetched.size + 6 * tokens * head_count * HD)
    return pl.pallas_call(
        kernel,
        grid_spec=pltpu.PrefetchScalarGridSpec(
            num_scalar_prefetch=2,
            grid=grid,
            in_specs=[in_block, in_block, sel_block, own_in, own_in],
            out_specs=[out_block, out_block, sel_block, own_out, own_out],
            scratch_shapes=[pltpu.VMEM((slot_count, 2, HD, BLK), jnp.float32)],
        ),
        out_shape=[
            jax.ShapeDtypeStruct((tp_size, row_tile, q_cols), jnp.bfloat16),
            jax.ShapeDtypeStruct((tp_size, row_tile, q_cols), jnp.bfloat16),
            jax.ShapeDtypeStruct(fetched.shape, jnp.float32),
            jax.ShapeDtypeStruct((tokens, head_count * HD), jnp.float32),
            jax.ShapeDtypeStruct((tokens, head_count * HD), jnp.float32),
        ],
        compiler_params=pltpu.CompilerParams(
            dimension_semantics=("arbitrary", "arbitrary", "arbitrary"),
        ),
        cost_estimate=pl.CostEstimate(
            flops=flops,
            transcendentals=head_count * group_size * tokens * slot_count * BLK,
            bytes_accessed=bytes_accessed,
        ),
    )(live, tp_info, query_stack, upstream_stack, fetched, key_heads, value_heads)


def shift(x, axis, step, size):
    return lax.ppermute(x, axis, perm=[(s, (s + step) % size) for s in range(size)])


def tp_receive(x, me, size, width, offset):
    stride = x.shape[1] // size
    pieces = [lax.dynamic_slice_in_dim(x, me * stride + offset, width, 1)]
    for step in range(1, size):
        dest = (me + step) % size
        piece = lax.dynamic_slice_in_dim(x, dest * stride + offset, width, 1)
        pieces.append(shift(piece, "tp", step, size))
    return jnp.stack(pieces)


def tp_receive_many(items, me, size):
    owns, sends = [], []
    for x, width, offset in items:
        stride = x.shape[1] // size
        owns.append(lax.dynamic_slice_in_dim(x, me * stride + offset, width, 1))
        sends.append(
            [lax.dynamic_slice_in_dim(x, ((me + step) % size) * stride + offset, width, 1)
             for step in range(1, size)]
        )
    received = [
        shift(tuple(s[step - 1] for s in sends), "tp", step, size) for step in range(1, size)
    ]
    return [
        jnp.stack([owns[i]] + [received[step - 1][i] for step in range(1, size)])
        for i in range(len(items))
    ]


def tp_send(stack, me, size):
    pieces = [stack[0]] + [shift(stack[step], "tp", step, size) for step in range(1, size)]
    order = (me - jnp.arange(size, dtype=jnp.int32)) % size
    arranged = jnp.take(jnp.stack(pieces), order, axis=0)
    return arranged.transpose(1, 0, 2).reshape(stack.shape[1], size * stack.shape[2])


def source_order(stack, me, size):
    order = (me - jnp.arange(size, dtype=jnp.int32)) % size
    return jnp.take(stack, order, axis=0)


def body(queries, key_rows, value_rows, selected, own_flag, cotangent):
    holders = lax.axis_size("ctx")
    tp_size = lax.axis_size("tp")
    position = lax.axis_index("ctx")
    me = lax.axis_index("tp")
    rows_in = queries.shape[0]
    q_cols = queries.shape[1] // tp_size
    k_cols = key_rows.shape[1] // tp_size
    tokens = rows_in * tp_size
    assert tokens == BLK
    head_count = k_cols // HD
    group_size = q_cols // k_cols
    chunk_count = 2 if head_count % 2 == 0 else 1
    chunk_heads = head_count // chunk_count
    q_width = chunk_heads * group_size * HD
    key_stack, value_stack, first_queries, first_upstream = tp_receive_many(
        [(key_rows, k_cols, 0), (value_rows, k_cols, 0), (queries, q_width, 0), (cotangent, q_width, 0)],
        me, tp_size,
    )
    key_heads = source_order(key_stack, me, tp_size).reshape(tokens, k_cols)
    value_heads = source_order(value_stack, me, tp_size).reshape(tokens, k_cols)
    head_count = k_cols // HD
    group_size = q_cols // k_cols
    span_rows = BLK // holders

    kv = jnp.stack(
        [key_heads.reshape(holders, span_rows, head_count, HD),
         value_heads.reshape(holders, span_rows, head_count, HD)],
        axis=1,
    )
    spread = lax.all_to_all(kv, "ctx", split_axis=0, concat_axis=0, tiled=True)
    my_selected = lax.dynamic_index_in_dim(selected, position, 0, keepdims=False)
    my_flags = lax.dynamic_index_in_dim(own_flag, position, 0, keepdims=False)
    live_all = jnp.concatenate(
        [(my_selected < position).astype(jnp.int32), (my_flags == 1).astype(jnp.int32)[:, None]],
        axis=1,
    )
    tp_info = me.astype(jnp.int32).reshape(1)
    chunk_k_cols = chunk_heads * HD

    next_stacks = [
        tp_receive(queries, me, tp_size, q_width, (chunk_count - 1) * q_width),
        tp_receive(cotangent, me, tp_size, q_width, (chunk_count - 1) * q_width),
    ]
    def add_own(back, grad_key_own, grad_value_own):
        back = back.astype(jnp.float32)
        total_keys = back[:, 0].transpose(1, 0, 2).reshape(tokens, chunk_k_cols) + grad_key_own
        total_values = (
            back[:, 1].transpose(1, 0, 2).reshape(tokens, chunk_k_cols) + grad_value_own
        )
        return (total_keys, total_values)

    results = []
    pending = []
    for chunk in range(chunk_count):
        first = chunk * chunk_heads
        chunk_selected = selected[:, first : first + chunk_heads]
        head_ids = jnp.arange(first, first + chunk_heads, dtype=jnp.int32)[None, :, None]
        send = spread[chunk_selected, :, :, head_ids, :]
        if chunk == 0:
            query_stack, upstream_stack = first_queries, first_upstream
            send, *next_stacks = lax.optimization_barrier((send, *next_stacks))
        else:
            query_stack, upstream_stack = next_stacks
            send, _, _ = lax.optimization_barrier((send, first_queries, first_upstream))
        got = lax.all_to_all(send, "ctx", split_axis=0, concat_axis=4, tiled=True)
        fetched = got[0]
        live = live_all[first : first + chunk_heads].reshape(-1)
        attended, grad_queries, grad_sel, grad_key_own, grad_value_own = attention(
            live, tp_info, query_stack, upstream_stack, fetched, key_heads, value_heads,
            group_size, first,
        )
        attended = tp_send(attended, me, tp_size)
        grad_queries = tp_send(grad_queries, me, tp_size)

        send_back = grad_sel.astype(jnp.bfloat16).reshape(
            chunk_heads, TOPK, 2, holders, span_rows, HD
        )
        if chunk == chunk_count - 1 and pending:
            parts = [send_back.transpose(3, 0, 1, 2, 4, 5).reshape(holders, -1)] + [
                p[0].transpose(1, 0, 2, 3, 4).reshape(holders, -1) for p in pending
            ]
            widths = [p.shape[1] for p in parts]
            merged = lax.all_to_all(
                jnp.concatenate(parts, axis=1), "ctx", split_axis=0, concat_axis=0, tiled=True
            )
            offsets = [sum(widths[:i]) for i in range(len(widths))]
            flat = (
                merged[:, : widths[0]]
                .reshape(holders, chunk_heads, TOPK, 2, span_rows, HD)
                .transpose(1, 0, 2, 3, 4, 5)
                .reshape(chunk_heads, holders * TOPK, 2 * span_rows * HD)
            )
            for p, offset, width in zip(pending, offsets[1:], widths[1:]):
                back = (
                    merged[:, offset : offset + width]
                    .reshape(holders, chunk_heads, 2, span_rows, HD)
                    .transpose(1, 2, 0, 3, 4)
                    .reshape(chunk_heads, 2, BLK, HD)
                )
                results.append(p[1:3] + add_own(back, *p[3:]))
            pending = []
        else:
            got_back = lax.all_to_all(send_back, "ctx", split_axis=3, concat_axis=1, tiled=True)
            flat = got_back.reshape(chunk_heads, holders * TOPK, 2 * span_rows * HD)
        flat = flat.astype(jnp.float32)
        targets = chunk_selected.transpose(1, 0, 2).reshape(chunk_heads, holders * TOPK)
        table = (
            targets[:, None, :] == jnp.arange(holders, dtype=jnp.int32)[None, :, None]
        ).astype(jnp.float32)
        summed = jnp.einsum("gjn,gnx->gjx", table, flat, precision=lax.Precision.HIGHEST)
        owner = summed.reshape(chunk_heads, holders, 2, span_rows, HD).astype(jnp.bfloat16)
        pending.append((owner, attended, grad_queries, grad_key_own, grad_value_own))

    for p in pending:
        back = lax.all_to_all(p[0], "ctx", split_axis=1, concat_axis=3, tiled=True)[:, 0]
        results.append(p[1:3] + add_own(back, *p[3:]))

    def rows_by_destination(total):
        stack = total.astype(jnp.bfloat16).reshape(tp_size, rows_in, k_cols)
        order = (me + jnp.arange(tp_size, dtype=jnp.int32)) % tp_size
        return tp_send(jnp.take(stack, order, axis=0), me, tp_size)

    def interleave(parts, width):
        stacked = jnp.stack([p.reshape(rows_in, tp_size, width) for p in parts], axis=2)
        return stacked.reshape(rows_in, tp_size * len(parts) * width)

    attended = interleave([r[0] for r in results], q_width)
    grad_queries = interleave([r[1] for r in results], q_width)
    total_keys = jnp.concatenate([r[2] for r in results], axis=1)
    total_values = jnp.concatenate([r[3] for r in results], axis=1)
    return (attended, grad_queries, rows_by_destination(total_keys), rows_by_destination(total_values))


def solution(mesh):
    in_specs = (
        P(("ctx", "tp"), None),
        P(("ctx", "tp"), None),
        P(("ctx", "tp"), None),
        P(None, "tp", None),
        P(None, "tp"),
        P(("ctx", "tp"), None),
    )
    out_specs = (
        P(("ctx", "tp"), None),
        P(("ctx", "tp"), None),
        P(("ctx", "tp"), None),
        P(("ctx", "tp"), None),
    )
    return jax.shard_map(body, mesh=mesh, in_specs=in_specs, out_specs=out_specs, check_vma=False)
```

```python
import functools
import math

import jax
import jax.numpy as jnp
from jax import lax
from jax.experimental import pallas as pl
from jax.experimental.pallas import tpu as pltpu
from jax.sharding import PartitionSpec as P

HD = 128
BLK = 512
TOPK = 3


def attention_kernel(
    live_ref, tp_ref, q_ref, do_ref, kvs_ref, ko_ref, vo_ref,
    o_ref, dq_ref, dsel_ref, dko_ref, dvo_ref, acc_ref, *, slot_count, row_tile, scale
):
    g = pl.program_id(0)
    h = pl.program_id(1)
    t = pl.program_id(2)

    @pl.when((h == 0) & (t == 0))
    def _():
        acc_ref[...] = jnp.zeros(acc_ref.shape, acc_ref.dtype)

    q = q_ref[...]
    do = do_ref[...]
    keys = [kvs_ref[r, 0] for r in range(slot_count - 1)] + [ko_ref[...]]
    values = [kvs_ref[r, 1] for r in range(slot_count - 1)] + [vo_ref[...]]
    trans_b = (((1,), (1,)), ((), ()))
    q_t = q.T
    do_t = do.T
    scores = []
    for r in range(slot_count):
        s = lax.dot_general(q, keys[r], trans_b, preferred_element_type=jnp.float32) * scale
        live = live_ref[g * slot_count + r] > 0
        if r == slot_count - 1:
            row = t * row_tile + lax.broadcasted_iota(jnp.int32, s.shape, 0)
            col = lax.broadcasted_iota(jnp.int32, s.shape, 1)
            s = jnp.where(live & (row >= col), s, -jnp.inf)
        else:
            s = jnp.where(live, s, -jnp.inf)
        scores.append(s)
    row_max = scores[0].max(axis=1, keepdims=True)
    for s in scores[1:]:
        row_max = jnp.maximum(row_max, s.max(axis=1, keepdims=True))
    weights = [jnp.exp(s - row_max) for s in scores]
    total = weights[0].sum(axis=1, keepdims=True)
    for w in weights[1:]:
        total = total + w.sum(axis=1, keepdims=True)
    inverse = 1.0 / total
    probs = [w * inverse for w in weights]
    probs_low = [p.astype(jnp.bfloat16) for p in probs]
    out = jnp.dot(probs_low[0], values[0], preferred_element_type=jnp.float32)
    for r in range(1, slot_count):
        out = out + jnp.dot(probs_low[r], values[r], preferred_element_type=jnp.float32)
    out_low = out.astype(jnp.bfloat16)
    o_ref[...] = out_low
    delta = jnp.sum(do.astype(jnp.float32) * out_low.astype(jnp.float32), axis=1, keepdims=True)
    grad_q = None
    for r in range(slot_count):
        grad_p = lax.dot_general(do, values[r], trans_b, preferred_element_type=jnp.float32)
        grad_s = (probs[r] * (grad_p - delta)).astype(jnp.bfloat16)
        part = jnp.dot(grad_s, keys[r], preferred_element_type=jnp.float32)
        grad_q = part if grad_q is None else grad_q + part
        acc_ref[r, 0] += jnp.dot(q_t, grad_s, preferred_element_type=jnp.float32) * scale
        acc_ref[r, 1] += jnp.dot(do_t, probs_low[r], preferred_element_type=jnp.float32)
    dq_ref[...] = (grad_q * scale).astype(jnp.bfloat16)

    @pl.when((h == pl.num_programs(1) - 1) & (t == pl.num_programs(2) - 1))
    def _():
        for r in range(slot_count - 1):
            dsel_ref[r, 0] = acc_ref[r, 0].T
            dsel_ref[r, 1] = acc_ref[r, 1].T
        dko_ref[...] = acc_ref[slot_count - 1, 0].T
        dvo_ref[...] = acc_ref[slot_count - 1, 1].T


def attention(live, tp_info, query_stack, upstream_stack, fetched, key_heads, value_heads, group_size, first):
    tp_size, row_tile, _ = query_stack.shape
    tokens = tp_size * row_tile
    head_count = fetched.shape[0]
    q_cols = head_count * group_size * HD
    slot_count = TOPK + 1
    grid = (head_count, group_size, tp_size)
    kernel = functools.partial(
        attention_kernel, slot_count=slot_count, row_tile=row_tile, scale=1.0 / math.sqrt(HD)
    )

    def piece_in(g, h, t, live, tp):
        return ((tp[0] - t + tp_size) % tp_size, 0, g * group_size + h)

    def piece_out(g, h, t, live, tp):
        return ((t - tp[0] + tp_size) % tp_size, 0, g * group_size + h)

    in_block = pl.BlockSpec((None, row_tile, HD), piece_in)
    out_block = pl.BlockSpec((None, row_tile, HD), piece_out)
    sel_block = pl.BlockSpec((None, TOPK, 2, BLK, HD), lambda g, h, t, live, tp: (g, 0, 0, 0, 0))
    own_in = pl.BlockSpec((BLK, HD), lambda g, h, t, live, tp: (0, first + g))
    own_out = pl.BlockSpec((BLK, HD), lambda g, h, t, live, tp: (0, g))
    flops = 12 * head_count * group_size * tokens * slot_count * BLK * HD
    bytes_accessed = 2 * (4 * tokens * q_cols + 3 * fetched.size + 6 * tokens * head_count * HD)
    return pl.pallas_call(
        kernel,
        grid_spec=pltpu.PrefetchScalarGridSpec(
            num_scalar_prefetch=2,
            grid=grid,
            in_specs=[in_block, in_block, sel_block, own_in, own_in],
            out_specs=[out_block, out_block, sel_block, own_out, own_out],
            scratch_shapes=[pltpu.VMEM((slot_count, 2, HD, BLK), jnp.float32)],
        ),
        out_shape=[
            jax.ShapeDtypeStruct((tp_size, row_tile, q_cols), jnp.bfloat16),
            jax.ShapeDtypeStruct((tp_size, row_tile, q_cols), jnp.bfloat16),
            jax.ShapeDtypeStruct(fetched.shape, jnp.float32),
            jax.ShapeDtypeStruct((tokens, head_count * HD), jnp.float32),
            jax.ShapeDtypeStruct((tokens, head_count * HD), jnp.float32),
        ],
        compiler_params=pltpu.CompilerParams(
            dimension_semantics=("arbitrary", "arbitrary", "arbitrary"),
        ),
        cost_estimate=pl.CostEstimate(
            flops=flops,
            transcendentals=head_count * group_size * tokens * slot_count * BLK,
            bytes_accessed=bytes_accessed,
        ),
    )(live, tp_info, query_stack, upstream_stack, fetched, key_heads, value_heads)


def shift(x, axis, step, size):
    return lax.ppermute(x, axis, perm=[(s, (s + step) % size) for s in range(size)])


def tp_receive(x, me, size, width, offset):
    stride = x.shape[1] // size
    pieces = [lax.dynamic_slice_in_dim(x, me * stride + offset, width, 1)]
    for step in range(1, size):
        dest = (me + step) % size
        piece = lax.dynamic_slice_in_dim(x, dest * stride + offset, width, 1)
        pieces.append(shift(piece, "tp", step, size))
    return jnp.stack(pieces)


def tp_receive_many(items, me, size):
    owns, sends = [], []
    for x, width, offset in items:
        stride = x.shape[1] // size
        owns.append(lax.dynamic_slice_in_dim(x, me * stride + offset, width, 1))
        sends.append(
            [lax.dynamic_slice_in_dim(x, ((me + step) % size) * stride + offset, width, 1)
             for step in range(1, size)]
        )
    received = [
        shift(tuple(s[step - 1] for s in sends), "tp", step, size) for step in range(1, size)
    ]
    return [
        jnp.stack([owns[i]] + [received[step - 1][i] for step in range(1, size)])
        for i in range(len(items))
    ]


def tp_send(stack, me, size):
    return [stack[0]] + [shift(stack[step], "tp", step, size) for step in range(1, size)]


def tp_columns(chunk_pieces, me, size):
    parts = []
    for source in range(size):
        step = (me - source) % size
        for pieces in chunk_pieces:
            parts.append(lax.dynamic_index_in_dim(jnp.stack(pieces), step, 0, keepdims=False))
    return jnp.concatenate(parts, axis=1)


def source_order(stack, me, size):
    order = (me - jnp.arange(size, dtype=jnp.int32)) % size
    return jnp.take(stack, order, axis=0)


def body(queries, key_rows, value_rows, selected, own_flag, cotangent):
    holders = lax.axis_size("ctx")
    tp_size = lax.axis_size("tp")
    position = lax.axis_index("ctx")
    me = lax.axis_index("tp")
    rows_in = queries.shape[0]
    q_cols = queries.shape[1] // tp_size
    k_cols = key_rows.shape[1] // tp_size
    tokens = rows_in * tp_size
    assert tokens == BLK
    head_count = k_cols // HD
    group_size = q_cols // k_cols
    chunk_count = 2 if head_count % 2 == 0 else 1
    chunk_heads = head_count // chunk_count
    q_width = chunk_heads * group_size * HD
    key_stack, value_stack, first_queries, first_upstream = tp_receive_many(
        [(key_rows, k_cols, 0), (value_rows, k_cols, 0), (queries, q_width, 0), (cotangent, q_width, 0)],
        me, tp_size,
    )
    key_heads = source_order(key_stack, me, tp_size).reshape(tokens, k_cols)
    value_heads = source_order(value_stack, me, tp_size).reshape(tokens, k_cols)
    head_count = k_cols // HD
    group_size = q_cols // k_cols
    span_rows = BLK // holders

    kv = jnp.stack(
        [key_heads.reshape(holders, span_rows, head_count, HD),
         value_heads.reshape(holders, span_rows, head_count, HD)],
        axis=1,
    )
    spread = lax.all_to_all(kv, "ctx", split_axis=0, concat_axis=0, tiled=True)
    my_selected = lax.dynamic_index_in_dim(selected, position, 0, keepdims=False)
    my_flags = lax.dynamic_index_in_dim(own_flag, position, 0, keepdims=False)
    live_all = jnp.concatenate(
        [(my_selected < position).astype(jnp.int32), (my_flags == 1).astype(jnp.int32)[:, None]],
        axis=1,
    )
    tp_info = me.astype(jnp.int32).reshape(1)
    chunk_k_cols = chunk_heads * HD

    next_stacks = [
        tp_receive(queries, me, tp_size, q_width, (chunk_count - 1) * q_width),
        tp_receive(cotangent, me, tp_size, q_width, (chunk_count - 1) * q_width),
    ]
    results = []
    for chunk in range(chunk_count):
        first = chunk * chunk_heads
        chunk_selected = selected[:, first : first + chunk_heads]
        head_ids = jnp.arange(first, first + chunk_heads, dtype=jnp.int32)[None, :, None]
        send = spread[chunk_selected, :, :, head_ids, :]
        if chunk == 0:
            query_stack, upstream_stack = first_queries, first_upstream
            send, *next_stacks = lax.optimization_barrier((send, *next_stacks))
        else:
            query_stack, upstream_stack = next_stacks
            send, _, _ = lax.optimization_barrier((send, first_queries, first_upstream))
        got = lax.all_to_all(send, "ctx", split_axis=0, concat_axis=4, tiled=True)
        fetched = got[0]
        live = live_all[first : first + chunk_heads].reshape(-1)
        attended, grad_queries, grad_sel, grad_key_own, grad_value_own = attention(
            live, tp_info, query_stack, upstream_stack, fetched, key_heads, value_heads,
            group_size, first,
        )
        attended = tp_send(attended, me, tp_size)
        grad_queries = tp_send(grad_queries, me, tp_size)

        send_back = grad_sel.astype(jnp.bfloat16).reshape(
            chunk_heads, TOPK, 2, holders, span_rows, HD
        )
        got_back = lax.all_to_all(send_back, "ctx", split_axis=3, concat_axis=1, tiled=True)
        flat = got_back.reshape(chunk_heads, holders * TOPK, 2 * span_rows * HD).astype(
            jnp.float32
        )
        targets = chunk_selected.transpose(1, 0, 2).reshape(chunk_heads, holders * TOPK)
        table = (
            targets[:, None, :] == jnp.arange(holders, dtype=jnp.int32)[None, :, None]
        ).astype(jnp.float32)
        summed = jnp.einsum("gjn,gnx->gjx", table, flat, precision=lax.Precision.HIGHEST)
        owner = summed.reshape(chunk_heads, holders, 2, span_rows, HD).astype(jnp.bfloat16)
        back = lax.all_to_all(owner, "ctx", split_axis=1, concat_axis=3, tiled=True)
        back = back[:, 0].astype(jnp.float32)
        total_keys = back[:, 0].transpose(1, 0, 2).reshape(tokens, chunk_k_cols) + grad_key_own
        total_values = (
            back[:, 1].transpose(1, 0, 2).reshape(tokens, chunk_k_cols) + grad_value_own
        )
        results.append((attended, grad_queries, total_keys, total_values))

    def rows_by_destination(total):
        stack = total.astype(jnp.bfloat16).reshape(tp_size, rows_in, k_cols)
        order = (me + jnp.arange(tp_size, dtype=jnp.int32)) % tp_size
        return tp_columns([tp_send(jnp.take(stack, order, axis=0), me, tp_size)], me, tp_size)

    attended = tp_columns([r[0] for r in results], me, tp_size)
    grad_queries = tp_columns([r[1] for r in results], me, tp_size)
    total_keys = jnp.concatenate([r[2] for r in results], axis=1)
    total_values = jnp.concatenate([r[3] for r in results], axis=1)
    return (attended, grad_queries, rows_by_destination(total_keys), rows_by_destination(total_values))


def solution(mesh):
    in_specs = (
        P(("ctx", "tp"), None),
        P(("ctx", "tp"), None),
        P(("ctx", "tp"), None),
        P(None, "tp", None),
        P(None, "tp"),
        P(("ctx", "tp"), None),
    )
    out_specs = (
        P(("ctx", "tp"), None),
        P(("ctx", "tp"), None),
        P(("ctx", "tp"), None),
        P(("ctx", "tp"), None),
    )
    return jax.shard_map(body, mesh=mesh, in_specs=in_specs, out_specs=out_specs, check_vma=False)
```

```python
import functools
import math

import jax
import jax.numpy as jnp
from jax import lax
from jax.experimental import pallas as pl
from jax.experimental.pallas import tpu as pltpu
from jax.sharding import PartitionSpec as P

HD = 128
BLK = 512
TOPK = 3


def attention_kernel(
    live_ref, tp_ref, q_ref, do_ref, kvs_ref, ko_ref, vo_ref,
    o_ref, dq_ref, dsel_ref, dko_ref, dvo_ref, acc_ref, *, slot_count, row_tile, scale, tiles, own_rows
):
    g = pl.program_id(0)
    h = pl.program_id(1)
    t = pl.program_id(2)

    @pl.when((h == 0) & (t == 0))
    def _():
        acc_ref[...] = jnp.zeros(acc_ref.shape, acc_ref.dtype)

    def run(own_width):
        q = q_ref[...]
        do = do_ref[...]
        keys = [kvs_ref[r, 0] for r in range(slot_count - 1)] + [ko_ref[:own_width]]
        values = [kvs_ref[r, 1] for r in range(slot_count - 1)] + [vo_ref[:own_width]]
        trans_b = (((1,), (1,)), ((), ()))
        q_t = q.T
        do_t = do.T
        scores = []
        for r in range(slot_count):
            s = lax.dot_general(q, keys[r], trans_b, preferred_element_type=jnp.float32) * scale
            live = live_ref[g * slot_count + r] > 0
            if r == slot_count - 1:
                row = t * row_tile + lax.broadcasted_iota(jnp.int32, s.shape, 0)
                col = lax.broadcasted_iota(jnp.int32, s.shape, 1)
                s = jnp.where(live & (row >= col), s, -jnp.inf)
            else:
                s = jnp.where(live, s, -jnp.inf)
            scores.append(s)
        row_max = scores[0].max(axis=1, keepdims=True)
        for s in scores[1:]:
            row_max = jnp.maximum(row_max, s.max(axis=1, keepdims=True))
        weights = [jnp.exp(s - row_max) for s in scores]
        total = weights[0].sum(axis=1, keepdims=True)
        for w in weights[1:]:
            total = total + w.sum(axis=1, keepdims=True)
        inverse = 1.0 / total
        probs = [w * inverse for w in weights]
        probs_low = [p.astype(jnp.bfloat16) for p in probs]
        out = jnp.dot(probs_low[0], values[0], preferred_element_type=jnp.float32)
        for r in range(1, slot_count):
            out = out + jnp.dot(probs_low[r], values[r], preferred_element_type=jnp.float32)
        out_low = out.astype(jnp.bfloat16)
        o_ref[...] = out_low
        delta = jnp.sum(do.astype(jnp.float32) * out_low.astype(jnp.float32), axis=1, keepdims=True)
        grad_q = None
        for r in range(slot_count):
            grad_p = lax.dot_general(do, values[r], trans_b, preferred_element_type=jnp.float32)
            grad_s = (probs[r] * (grad_p - delta)).astype(jnp.bfloat16)
            part = jnp.dot(grad_s, keys[r], preferred_element_type=jnp.float32)
            grad_q = part if grad_q is None else grad_q + part
            width = keys[r].shape[0]
            acc_ref[r, 0, :, :width] += jnp.dot(q_t, grad_s, preferred_element_type=jnp.float32) * scale
            acc_ref[r, 1, :, :width] += jnp.dot(do_t, probs_low[r], preferred_element_type=jnp.float32)
        dq_ref[...] = (grad_q * scale).astype(jnp.bfloat16)

    for tile in range(tiles):
        width = -(-(tile + 1) * row_tile // HD) * HD
        pl.when(t == tile)(functools.partial(run, min(width, own_rows)))

    @pl.when((h == pl.num_programs(1) - 1) & (t == pl.num_programs(2) - 1))
    def _():
        for r in range(slot_count - 1):
            dsel_ref[r, 0] = acc_ref[r, 0].T
            dsel_ref[r, 1] = acc_ref[r, 1].T
        dko_ref[...] = acc_ref[slot_count - 1, 0].T
        dvo_ref[...] = acc_ref[slot_count - 1, 1].T


def attention(live, tp_info, query_stack, upstream_stack, fetched, key_heads, value_heads, group_size, first):
    tp_size, row_tile, _ = query_stack.shape
    tokens = tp_size * row_tile
    head_count = fetched.shape[0]
    q_cols = head_count * group_size * HD
    slot_count = TOPK + 1
    grid = (head_count, group_size, tp_size)
    kernel = functools.partial(
        attention_kernel, slot_count=slot_count, row_tile=row_tile, scale=1.0 / math.sqrt(HD),
        tiles=tp_size, own_rows=BLK,
    )

    def piece_in(g, h, t, live, tp):
        return ((tp[0] - t + tp_size) % tp_size, 0, g * group_size + h)

    def piece_out(g, h, t, live, tp):
        return ((t - tp[0] + tp_size) % tp_size, 0, g * group_size + h)

    in_block = pl.BlockSpec((None, row_tile, HD), piece_in)
    out_block = pl.BlockSpec((None, row_tile, HD), piece_out)
    sel_block = pl.BlockSpec((None, TOPK, 2, BLK, HD), lambda g, h, t, live, tp: (g, 0, 0, 0, 0))
    own_in = pl.BlockSpec((BLK, HD), lambda g, h, t, live, tp: (0, first + g))
    own_out = pl.BlockSpec((BLK, HD), lambda g, h, t, live, tp: (0, g))
    flops = 12 * head_count * group_size * tokens * slot_count * BLK * HD
    bytes_accessed = 2 * (4 * tokens * q_cols + 3 * fetched.size + 6 * tokens * head_count * HD)
    return pl.pallas_call(
        kernel,
        grid_spec=pltpu.PrefetchScalarGridSpec(
            num_scalar_prefetch=2,
            grid=grid,
            in_specs=[in_block, in_block, sel_block, own_in, own_in],
            out_specs=[out_block, out_block, sel_block, own_out, own_out],
            scratch_shapes=[pltpu.VMEM((slot_count, 2, HD, BLK), jnp.float32)],
        ),
        out_shape=[
            jax.ShapeDtypeStruct((tp_size, row_tile, q_cols), jnp.bfloat16),
            jax.ShapeDtypeStruct((tp_size, row_tile, q_cols), jnp.bfloat16),
            jax.ShapeDtypeStruct(fetched.shape, jnp.float32),
            jax.ShapeDtypeStruct((tokens, head_count * HD), jnp.float32),
            jax.ShapeDtypeStruct((tokens, head_count * HD), jnp.float32),
        ],
        compiler_params=pltpu.CompilerParams(
            dimension_semantics=("arbitrary", "arbitrary", "arbitrary"),
        ),
        cost_estimate=pl.CostEstimate(
            flops=flops,
            transcendentals=head_count * group_size * tokens * slot_count * BLK,
            bytes_accessed=bytes_accessed,
        ),
    )(live, tp_info, query_stack, upstream_stack, fetched, key_heads, value_heads)


def shift(x, axis, step, size):
    return lax.ppermute(x, axis, perm=[(s, (s + step) % size) for s in range(size)])


def tp_receive(x, me, size, width, offset):
    stride = x.shape[1] // size
    pieces = [lax.dynamic_slice_in_dim(x, me * stride + offset, width, 1)]
    for step in range(1, size):
        dest = (me + step) % size
        piece = lax.dynamic_slice_in_dim(x, dest * stride + offset, width, 1)
        pieces.append(shift(piece, "tp", step, size))
    return jnp.stack(pieces)


def tp_receive_many(items, me, size):
    owns, sends = [], []
    for x, width, offset in items:
        stride = x.shape[1] // size
        owns.append(lax.dynamic_slice_in_dim(x, me * stride + offset, width, 1))
        sends.append(
            [lax.dynamic_slice_in_dim(x, ((me + step) % size) * stride + offset, width, 1)
             for step in range(1, size)]
        )
    received = [
        shift(tuple(s[step - 1] for s in sends), "tp", step, size) for step in range(1, size)
    ]
    return [
        jnp.stack([owns[i]] + [received[step - 1][i] for step in range(1, size)])
        for i in range(len(items))
    ]


def tp_send(stack, me, size):
    return [stack[0]] + [shift(stack[step], "tp", step, size) for step in range(1, size)]


def tp_columns(chunk_pieces, me, size):
    parts = []
    for source in range(size):
        step = (me - source) % size
        for pieces in chunk_pieces:
            parts.append(lax.dynamic_index_in_dim(jnp.stack(pieces), step, 0, keepdims=False))
    return jnp.concatenate(parts, axis=1)


def source_order(stack, me, size):
    order = (me - jnp.arange(size, dtype=jnp.int32)) % size
    return jnp.take(stack, order, axis=0)


def body(queries, key_rows, value_rows, selected, own_flag, cotangent):
    holders = lax.axis_size("ctx")
    tp_size = lax.axis_size("tp")
    position = lax.axis_index("ctx")
    me = lax.axis_index("tp")
    rows_in = queries.shape[0]
    q_cols = queries.shape[1] // tp_size
    k_cols = key_rows.shape[1] // tp_size
    tokens = rows_in * tp_size
    assert tokens == BLK
    head_count = k_cols // HD
    group_size = q_cols // k_cols
    chunk_count = 2 if head_count % 2 == 0 else 1
    chunk_heads = head_count // chunk_count
    q_width = chunk_heads * group_size * HD
    key_stack, value_stack, first_queries, first_upstream = tp_receive_many(
        [(key_rows, k_cols, 0), (value_rows, k_cols, 0), (queries, q_width, 0), (cotangent, q_width, 0)],
        me, tp_size,
    )
    key_heads = source_order(key_stack, me, tp_size).reshape(tokens, k_cols)
    value_heads = source_order(value_stack, me, tp_size).reshape(tokens, k_cols)
    head_count = k_cols // HD
    group_size = q_cols // k_cols
    span_rows = BLK // holders

    kv = jnp.stack(
        [key_heads.reshape(holders, span_rows, head_count, HD),
         value_heads.reshape(holders, span_rows, head_count, HD)],
        axis=1,
    )
    spread = lax.all_to_all(kv, "ctx", split_axis=0, concat_axis=0, tiled=True)
    my_selected = lax.dynamic_index_in_dim(selected, position, 0, keepdims=False)
    my_flags = lax.dynamic_index_in_dim(own_flag, position, 0, keepdims=False)
    live_all = jnp.concatenate(
        [(my_selected < position).astype(jnp.int32), (my_flags == 1).astype(jnp.int32)[:, None]],
        axis=1,
    )
    tp_info = me.astype(jnp.int32).reshape(1)
    chunk_k_cols = chunk_heads * HD

    next_stacks = [
        tp_receive(queries, me, tp_size, q_width, (chunk_count - 1) * q_width),
        tp_receive(cotangent, me, tp_size, q_width, (chunk_count - 1) * q_width),
    ]
    results = []
    for chunk in range(chunk_count):
        first = chunk * chunk_heads
        chunk_selected = selected[:, first : first + chunk_heads]
        head_ids = jnp.arange(first, first + chunk_heads, dtype=jnp.int32)[None, :, None]
        send = spread[chunk_selected, :, :, head_ids, :]
        if chunk == 0:
            query_stack, upstream_stack = first_queries, first_upstream
            send, *next_stacks = lax.optimization_barrier((send, *next_stacks))
        else:
            query_stack, upstream_stack = next_stacks
            send, _, _ = lax.optimization_barrier((send, first_queries, first_upstream))
        got = lax.all_to_all(send, "ctx", split_axis=0, concat_axis=4, tiled=True)
        fetched = got[0]
        live = live_all[first : first + chunk_heads].reshape(-1)
        attended, grad_queries, grad_sel, grad_key_own, grad_value_own = attention(
            live, tp_info, query_stack, upstream_stack, fetched, key_heads, value_heads,
            group_size, first,
        )
        attended = tp_send(attended, me, tp_size)
        grad_queries = tp_send(grad_queries, me, tp_size)

        send_back = grad_sel.astype(jnp.bfloat16).reshape(
            chunk_heads, TOPK, 2, holders, span_rows, HD
        )
        got_back = lax.all_to_all(send_back, "ctx", split_axis=3, concat_axis=1, tiled=True)
        flat = got_back.reshape(chunk_heads, holders * TOPK, 2 * span_rows * HD).astype(
            jnp.float32
        )
        targets = chunk_selected.transpose(1, 0, 2).reshape(chunk_heads, holders * TOPK)
        table = (
            targets[:, None, :] == jnp.arange(holders, dtype=jnp.int32)[None, :, None]
        ).astype(jnp.float32)
        summed = jnp.einsum("gjn,gnx->gjx", table, flat, precision=lax.Precision.HIGHEST)
        owner = summed.reshape(chunk_heads, holders, 2, span_rows, HD).astype(jnp.bfloat16)
        back = lax.all_to_all(owner, "ctx", split_axis=1, concat_axis=3, tiled=True)
        back = back[:, 0].astype(jnp.float32)
        total_keys = back[:, 0].transpose(1, 0, 2).reshape(tokens, chunk_k_cols) + grad_key_own
        total_values = (
            back[:, 1].transpose(1, 0, 2).reshape(tokens, chunk_k_cols) + grad_value_own
        )
        results.append((attended, grad_queries, total_keys, total_values))

    def rows_by_destination(total):
        stack = total.astype(jnp.bfloat16).reshape(tp_size, rows_in, k_cols)
        order = (me + jnp.arange(tp_size, dtype=jnp.int32)) % tp_size
        return tp_columns([tp_send(jnp.take(stack, order, axis=0), me, tp_size)], me, tp_size)

    attended = tp_columns([r[0] for r in results], me, tp_size)
    grad_queries = tp_columns([r[1] for r in results], me, tp_size)
    total_keys = jnp.concatenate([r[2] for r in results], axis=1)
    total_values = jnp.concatenate([r[3] for r in results], axis=1)
    return (attended, grad_queries, rows_by_destination(total_keys), rows_by_destination(total_values))


def solution(mesh):
    in_specs = (
        P(("ctx", "tp"), None),
        P(("ctx", "tp"), None),
        P(("ctx", "tp"), None),
        P(None, "tp", None),
        P(None, "tp"),
        P(("ctx", "tp"), None),
    )
    out_specs = (
        P(("ctx", "tp"), None),
        P(("ctx", "tp"), None),
        P(("ctx", "tp"), None),
        P(("ctx", "tp"), None),
    )
    return jax.shard_map(body, mesh=mesh, in_specs=in_specs, out_specs=out_specs, check_vma=False)
```

```python
import functools
import math

import jax
import jax.numpy as jnp
from jax import lax
from jax.experimental import pallas as pl
from jax.experimental.pallas import tpu as pltpu
from jax.sharding import PartitionSpec as P

HD = 128
BLK = 512
TOPK = 3


def attention_kernel(
    live_ref, tp_ref, q_ref, do_ref, kvs_ref, ko_ref, vo_ref,
    o_ref, dq_ref, dsel_ref, dko_ref, dvo_ref, acc_ref, *, slot_count, row_tile, scale, tiles, own_rows
):
    g = pl.program_id(0)
    h = pl.program_id(1)
    t = pl.program_id(2)

    @pl.when((h == 0) & (t == 0))
    def _():
        acc_ref[...] = jnp.zeros(acc_ref.shape, acc_ref.dtype)

    def run(own_width):
        q = q_ref[...]
        do = do_ref[...]
        keys = [kvs_ref[r, 0] for r in range(slot_count - 1)] + [ko_ref[:own_width]]
        values = [kvs_ref[r, 1] for r in range(slot_count - 1)] + [vo_ref[:own_width]]
        trans_b = (((1,), (1,)), ((), ()))
        q_t = q.T
        do_t = do.T
        scores = []
        for r in range(slot_count):
            s = lax.dot_general(q, keys[r], trans_b, preferred_element_type=jnp.float32)
            live = live_ref[g * slot_count + r] > 0
            if r == slot_count - 1:
                row = t * row_tile + lax.broadcasted_iota(jnp.int32, s.shape, 0)
                col = lax.broadcasted_iota(jnp.int32, s.shape, 1)
                s = jnp.where(live & (row >= col), s, -jnp.inf)
            else:
                s = jnp.where(live, s, -jnp.inf)
            scores.append(s)
        row_max = scores[0].max(axis=1, keepdims=True)
        for s in scores[1:]:
            row_max = jnp.maximum(row_max, s.max(axis=1, keepdims=True))
        weights = [jnp.exp((s - row_max) * scale) for s in scores]
        total = weights[0].sum(axis=1, keepdims=True)
        for w in weights[1:]:
            total = total + w.sum(axis=1, keepdims=True)
        inverse = 1.0 / total
        probs = [w * inverse for w in weights]
        probs_low = [p.astype(jnp.bfloat16) for p in probs]
        out = jnp.dot(probs_low[0], values[0], preferred_element_type=jnp.float32)
        for r in range(1, slot_count):
            out = out + jnp.dot(probs_low[r], values[r], preferred_element_type=jnp.float32)
        out_low = out.astype(jnp.bfloat16)
        o_ref[...] = out_low
        delta = jnp.sum(do.astype(jnp.float32) * out_low.astype(jnp.float32), axis=1, keepdims=True)
        grad_q = None
        for r in range(slot_count):
            grad_p = lax.dot_general(do, values[r], trans_b, preferred_element_type=jnp.float32)
            grad_s = (probs[r] * (grad_p - delta)).astype(jnp.bfloat16)
            part = jnp.dot(grad_s, keys[r], preferred_element_type=jnp.float32)
            grad_q = part if grad_q is None else grad_q + part
            width = keys[r].shape[0]
            acc_ref[r, 0, :, :width] += jnp.dot(q_t, grad_s, preferred_element_type=jnp.float32) * scale
            acc_ref[r, 1, :, :width] += jnp.dot(do_t, probs_low[r], preferred_element_type=jnp.float32)
        dq_ref[...] = (grad_q * scale).astype(jnp.bfloat16)

    for tile in range(tiles):
        width = -(-(tile + 1) * row_tile // HD) * HD
        pl.when(t == tile)(functools.partial(run, min(width, own_rows)))

    @pl.when((h == pl.num_programs(1) - 1) & (t == pl.num_programs(2) - 1))
    def _():
        for r in range(slot_count - 1):
            dsel_ref[r, 0] = acc_ref[r, 0].T
            dsel_ref[r, 1] = acc_ref[r, 1].T
        dko_ref[...] = acc_ref[slot_count - 1, 0].T
        dvo_ref[...] = acc_ref[slot_count - 1, 1].T


def attention(live, tp_info, query_stack, upstream_stack, fetched, key_heads, value_heads, group_size, first):
    tp_size, row_tile, _ = query_stack.shape
    tokens = tp_size * row_tile
    head_count = fetched.shape[0]
    q_cols = head_count * group_size * HD
    slot_count = TOPK + 1
    grid = (head_count, group_size, tp_size)
    kernel = functools.partial(
        attention_kernel, slot_count=slot_count, row_tile=row_tile, scale=1.0 / math.sqrt(HD),
        tiles=tp_size, own_rows=BLK,
    )

    def piece_in(g, h, t, live, tp):
        return ((tp[0] - t + tp_size) % tp_size, 0, g * group_size + h)

    def piece_out(g, h, t, live, tp):
        return ((t - tp[0] + tp_size) % tp_size, 0, g * group_size + h)

    in_block = pl.BlockSpec((None, row_tile, HD), piece_in)
    out_block = pl.BlockSpec((None, row_tile, HD), piece_out)
    sel_block = pl.BlockSpec((None, TOPK, 2, BLK, HD), lambda g, h, t, live, tp: (g, 0, 0, 0, 0))
    own_in = pl.BlockSpec((BLK, HD), lambda g, h, t, live, tp: (0, first + g))
    own_out = pl.BlockSpec((BLK, HD), lambda g, h, t, live, tp: (0, g))
    flops = 12 * head_count * group_size * tokens * slot_count * BLK * HD
    bytes_accessed = 2 * (4 * tokens * q_cols + 3 * fetched.size + 6 * tokens * head_count * HD)
    return pl.pallas_call(
        kernel,
        grid_spec=pltpu.PrefetchScalarGridSpec(
            num_scalar_prefetch=2,
            grid=grid,
            in_specs=[in_block, in_block, sel_block, own_in, own_in],
            out_specs=[out_block, out_block, sel_block, own_out, own_out],
            scratch_shapes=[pltpu.VMEM((slot_count, 2, HD, BLK), jnp.float32)],
        ),
        out_shape=[
            jax.ShapeDtypeStruct((tp_size, row_tile, q_cols), jnp.bfloat16),
            jax.ShapeDtypeStruct((tp_size, row_tile, q_cols), jnp.bfloat16),
            jax.ShapeDtypeStruct(fetched.shape, jnp.float32),
            jax.ShapeDtypeStruct((tokens, head_count * HD), jnp.float32),
            jax.ShapeDtypeStruct((tokens, head_count * HD), jnp.float32),
        ],
        compiler_params=pltpu.CompilerParams(
            dimension_semantics=("arbitrary", "arbitrary", "arbitrary"),
        ),
        cost_estimate=pl.CostEstimate(
            flops=flops,
            transcendentals=head_count * group_size * tokens * slot_count * BLK,
            bytes_accessed=bytes_accessed,
        ),
    )(live, tp_info, query_stack, upstream_stack, fetched, key_heads, value_heads)


def shift(x, axis, step, size):
    return lax.ppermute(x, axis, perm=[(s, (s + step) % size) for s in range(size)])


def tp_receive(x, me, size, width, offset):
    stride = x.shape[1] // size
    pieces = [lax.dynamic_slice_in_dim(x, me * stride + offset, width, 1)]
    for step in range(1, size):
        dest = (me + step) % size
        piece = lax.dynamic_slice_in_dim(x, dest * stride + offset, width, 1)
        pieces.append(shift(piece, "tp", step, size))
    return jnp.stack(pieces)


def tp_receive_many(items, me, size):
    owns, sends = [], []
    for x, width, offset in items:
        stride = x.shape[1] // size
        owns.append(lax.dynamic_slice_in_dim(x, me * stride + offset, width, 1))
        sends.append(
            [lax.dynamic_slice_in_dim(x, ((me + step) % size) * stride + offset, width, 1)
             for step in range(1, size)]
        )
    received = [
        shift(tuple(s[step - 1] for s in sends), "tp", step, size) for step in range(1, size)
    ]
    return [
        jnp.stack([owns[i]] + [received[step - 1][i] for step in range(1, size)])
        for i in range(len(items))
    ]


def tp_send(stack, me, size):
    return [stack[0]] + [shift(stack[step], "tp", step, size) for step in range(1, size)]


def tp_columns(chunk_pieces, me, size):
    parts = []
    for source in range(size):
        step = (me - source) % size
        for pieces in chunk_pieces:
            parts.append(lax.dynamic_index_in_dim(jnp.stack(pieces), step, 0, keepdims=False))
    return jnp.concatenate(parts, axis=1)


def source_order(stack, me, size):
    order = (me - jnp.arange(size, dtype=jnp.int32)) % size
    return jnp.take(stack, order, axis=0)


def body(queries, key_rows, value_rows, selected, own_flag, cotangent):
    holders = lax.axis_size("ctx")
    tp_size = lax.axis_size("tp")
    position = lax.axis_index("ctx")
    me = lax.axis_index("tp")
    rows_in = queries.shape[0]
    q_cols = queries.shape[1] // tp_size
    k_cols = key_rows.shape[1] // tp_size
    tokens = rows_in * tp_size
    assert tokens == BLK
    head_count = k_cols // HD
    group_size = q_cols // k_cols
    chunk_count = 2 if head_count % 2 == 0 else 1
    chunk_heads = head_count // chunk_count
    q_width = chunk_heads * group_size * HD
    key_stack, value_stack, first_queries, first_upstream = tp_receive_many(
        [(key_rows, k_cols, 0), (value_rows, k_cols, 0), (queries, q_width, 0), (cotangent, q_width, 0)],
        me, tp_size,
    )
    key_heads = source_order(key_stack, me, tp_size).reshape(tokens, k_cols)
    value_heads = source_order(value_stack, me, tp_size).reshape(tokens, k_cols)
    head_count = k_cols // HD
    group_size = q_cols // k_cols
    span_rows = BLK // holders

    kv = jnp.stack(
        [key_heads.reshape(holders, span_rows, head_count, HD),
         value_heads.reshape(holders, span_rows, head_count, HD)],
        axis=1,
    )
    spread = lax.all_to_all(kv, "ctx", split_axis=0, concat_axis=0, tiled=True)
    my_selected = lax.dynamic_index_in_dim(selected, position, 0, keepdims=False)
    my_flags = lax.dynamic_index_in_dim(own_flag, position, 0, keepdims=False)
    live_all = jnp.concatenate(
        [(my_selected < position).astype(jnp.int32), (my_flags == 1).astype(jnp.int32)[:, None]],
        axis=1,
    )
    tp_info = me.astype(jnp.int32).reshape(1)
    chunk_k_cols = chunk_heads * HD

    next_stacks = [
        tp_receive(queries, me, tp_size, q_width, (chunk_count - 1) * q_width),
        tp_receive(cotangent, me, tp_size, q_width, (chunk_count - 1) * q_width),
    ]
    results = []
    for chunk in range(chunk_count):
        first = chunk * chunk_heads
        chunk_selected = selected[:, first : first + chunk_heads]
        head_ids = jnp.arange(first, first + chunk_heads, dtype=jnp.int32)[None, :, None]
        send = spread[chunk_selected, :, :, head_ids, :]
        if chunk == 0:
            query_stack, upstream_stack = first_queries, first_upstream
            send, *next_stacks = lax.optimization_barrier((send, *next_stacks))
        else:
            query_stack, upstream_stack = next_stacks
            send, _, _ = lax.optimization_barrier((send, first_queries, first_upstream))
        got = lax.all_to_all(send, "ctx", split_axis=0, concat_axis=4, tiled=True)
        fetched = got[0]
        live = live_all[first : first + chunk_heads].reshape(-1)
        attended, grad_queries, grad_sel, grad_key_own, grad_value_own = attention(
            live, tp_info, query_stack, upstream_stack, fetched, key_heads, value_heads,
            group_size, first,
        )
        attended = tp_send(attended, me, tp_size)
        grad_queries = tp_send(grad_queries, me, tp_size)

        send_back = grad_sel.astype(jnp.bfloat16).reshape(
            chunk_heads, TOPK, 2, holders, span_rows, HD
        )
        got_back = lax.all_to_all(send_back, "ctx", split_axis=3, concat_axis=1, tiled=True)
        flat = got_back.reshape(chunk_heads, holders * TOPK, 2 * span_rows * HD).astype(
            jnp.float32
        )
        targets = chunk_selected.transpose(1, 0, 2).reshape(chunk_heads, holders * TOPK)
        table = (
            targets[:, None, :] == jnp.arange(holders, dtype=jnp.int32)[None, :, None]
        ).astype(jnp.float32)
        summed = jnp.einsum("gjn,gnx->gjx", table, flat, precision=lax.Precision.HIGHEST)
        owner = summed.reshape(chunk_heads, holders, 2, span_rows, HD).astype(jnp.bfloat16)
        back = lax.all_to_all(owner, "ctx", split_axis=1, concat_axis=3, tiled=True)
        back = back[:, 0].astype(jnp.float32)
        total_keys = back[:, 0].transpose(1, 0, 2).reshape(tokens, chunk_k_cols) + grad_key_own
        total_values = (
            back[:, 1].transpose(1, 0, 2).reshape(tokens, chunk_k_cols) + grad_value_own
        )
        results.append((attended, grad_queries, total_keys, total_values))

    def rows_by_destination(total):
        stack = total.astype(jnp.bfloat16).reshape(tp_size, rows_in, k_cols)
        order = (me + jnp.arange(tp_size, dtype=jnp.int32)) % tp_size
        return tp_columns([tp_send(jnp.take(stack, order, axis=0), me, tp_size)], me, tp_size)

    attended = tp_columns([r[0] for r in results], me, tp_size)
    grad_queries = tp_columns([r[1] for r in results], me, tp_size)
    total_keys = jnp.concatenate([r[2] for r in results], axis=1)
    total_values = jnp.concatenate([r[3] for r in results], axis=1)
    return (attended, grad_queries, rows_by_destination(total_keys), rows_by_destination(total_values))


def solution(mesh):
    in_specs = (
        P(("ctx", "tp"), None),
        P(("ctx", "tp"), None),
        P(("ctx", "tp"), None),
        P(None, "tp", None),
        P(None, "tp"),
        P(("ctx", "tp"), None),
    )
    out_specs = (
        P(("ctx", "tp"), None),
        P(("ctx", "tp"), None),
        P(("ctx", "tp"), None),
        P(("ctx", "tp"), None),
    )
    return jax.shard_map(body, mesh=mesh, in_specs=in_specs, out_specs=out_specs, check_vma=False)
```

```python
import functools
import math

import jax
import jax.numpy as jnp
from jax import lax
from jax.experimental import pallas as pl
from jax.experimental.pallas import tpu as pltpu
from jax.sharding import PartitionSpec as P

HD = 128
BLK = 512
TOPK = 3


def attention_kernel(
    live_ref, tp_ref, q_ref, do_ref, kvs_ref, ko_ref, vo_ref,
    o_ref, dq_ref, dsel_ref, dko_ref, dvo_ref, acc_ref, *, slot_count, row_tile, scale, tiles, own_rows
):
    g = pl.program_id(0)
    h = pl.program_id(1)
    t = pl.program_id(2)

    @pl.when((h == 0) & (t == 0))
    def _():
        acc_ref[...] = jnp.zeros(acc_ref.shape, acc_ref.dtype)

    def run(own_width):
        q = q_ref[...]
        do = do_ref[...]
        keys = [kvs_ref[r, 0] for r in range(slot_count - 1)] + [ko_ref[:own_width]]
        values = [kvs_ref[r, 1] for r in range(slot_count - 1)] + [vo_ref[:own_width]]
        trans_b = (((1,), (1,)), ((), ()))
        q_t = q.T
        do_t = do.T
        scores = []
        for r in range(slot_count):
            s = lax.dot_general(q, keys[r], trans_b, preferred_element_type=jnp.float32) * scale
            live = live_ref[g * slot_count + r] > 0
            if r == slot_count - 1:
                row = t * row_tile + lax.broadcasted_iota(jnp.int32, s.shape, 0)
                col = lax.broadcasted_iota(jnp.int32, s.shape, 1)
                s = jnp.where(live & (row >= col), s, -jnp.inf)
            else:
                s = jnp.where(live, s, -jnp.inf)
            scores.append(s)
        row_max = scores[0].max(axis=1, keepdims=True)
        for s in scores[1:]:
            row_max = jnp.maximum(row_max, s.max(axis=1, keepdims=True))
        weights = [jnp.exp(s - row_max) for s in scores]
        total = weights[0].sum(axis=1, keepdims=True)
        for w in weights[1:]:
            total = total + w.sum(axis=1, keepdims=True)
        inverse = 1.0 / total
        probs_low = [(w * inverse).astype(jnp.bfloat16) for w in weights]
        out = jnp.dot(probs_low[0], values[0], preferred_element_type=jnp.float32)
        for r in range(1, slot_count):
            out = out + jnp.dot(probs_low[r], values[r], preferred_element_type=jnp.float32)
        out_low = out.astype(jnp.bfloat16)
        o_ref[...] = out_low
        delta = jnp.sum(do.astype(jnp.float32) * out_low.astype(jnp.float32), axis=1, keepdims=True)
        grad_q = None
        for r in range(slot_count):
            grad_p = lax.dot_general(do, values[r], trans_b, preferred_element_type=jnp.float32)
            grad_s = (probs_low[r].astype(jnp.float32) * (grad_p - delta)).astype(jnp.bfloat16)
            part = jnp.dot(grad_s, keys[r], preferred_element_type=jnp.float32)
            grad_q = part if grad_q is None else grad_q + part
            width = keys[r].shape[0]
            acc_ref[r, 0, :, :width] += jnp.dot(q_t, grad_s, preferred_element_type=jnp.float32) * scale
            acc_ref[r, 1, :, :width] += jnp.dot(do_t, probs_low[r], preferred_element_type=jnp.float32)
        dq_ref[...] = (grad_q * scale).astype(jnp.bfloat16)

    for tile in range(tiles):
        width = -(-(tile + 1) * row_tile // HD) * HD
        pl.when(t == tile)(functools.partial(run, min(width, own_rows)))

    @pl.when((h == pl.num_programs(1) - 1) & (t == pl.num_programs(2) - 1))
    def _():
        for r in range(slot_count - 1):
            dsel_ref[r, 0] = acc_ref[r, 0].T
            dsel_ref[r, 1] = acc_ref[r, 1].T
        dko_ref[...] = acc_ref[slot_count - 1, 0].T
        dvo_ref[...] = acc_ref[slot_count - 1, 1].T


def attention(live, tp_info, query_stack, upstream_stack, fetched, key_heads, value_heads, group_size, first):
    tp_size, row_tile, _ = query_stack.shape
    tokens = tp_size * row_tile
    head_count = fetched.shape[0]
    q_cols = head_count * group_size * HD
    slot_count = TOPK + 1
    grid = (head_count, group_size, tp_size)
    kernel = functools.partial(
        attention_kernel, slot_count=slot_count, row_tile=row_tile, scale=1.0 / math.sqrt(HD),
        tiles=tp_size, own_rows=BLK,
    )

    def piece_in(g, h, t, live, tp):
        return ((tp[0] - t + tp_size) % tp_size, 0, g * group_size + h)

    def piece_out(g, h, t, live, tp):
        return ((t - tp[0] + tp_size) % tp_size, 0, g * group_size + h)

    in_block = pl.BlockSpec((None, row_tile, HD), piece_in)
    out_block = pl.BlockSpec((None, row_tile, HD), piece_out)
    sel_block = pl.BlockSpec((None, TOPK, 2, BLK, HD), lambda g, h, t, live, tp: (g, 0, 0, 0, 0))
    own_in = pl.BlockSpec((BLK, HD), lambda g, h, t, live, tp: (0, first + g))
    own_out = pl.BlockSpec((BLK, HD), lambda g, h, t, live, tp: (0, g))
    flops = 12 * head_count * group_size * tokens * slot_count * BLK * HD
    bytes_accessed = 2 * (4 * tokens * q_cols + 3 * fetched.size + 6 * tokens * head_count * HD)
    return pl.pallas_call(
        kernel,
        grid_spec=pltpu.PrefetchScalarGridSpec(
            num_scalar_prefetch=2,
            grid=grid,
            in_specs=[in_block, in_block, sel_block, own_in, own_in],
            out_specs=[out_block, out_block, sel_block, own_out, own_out],
            scratch_shapes=[pltpu.VMEM((slot_count, 2, HD, BLK), jnp.float32)],
        ),
        out_shape=[
            jax.ShapeDtypeStruct((tp_size, row_tile, q_cols), jnp.bfloat16),
            jax.ShapeDtypeStruct((tp_size, row_tile, q_cols), jnp.bfloat16),
            jax.ShapeDtypeStruct(fetched.shape, jnp.float32),
            jax.ShapeDtypeStruct((tokens, head_count * HD), jnp.float32),
            jax.ShapeDtypeStruct((tokens, head_count * HD), jnp.float32),
        ],
        compiler_params=pltpu.CompilerParams(
            dimension_semantics=("arbitrary", "arbitrary", "arbitrary"),
        ),
        cost_estimate=pl.CostEstimate(
            flops=flops,
            transcendentals=head_count * group_size * tokens * slot_count * BLK,
            bytes_accessed=bytes_accessed,
        ),
    )(live, tp_info, query_stack, upstream_stack, fetched, key_heads, value_heads)


def shift(x, axis, step, size):
    return lax.ppermute(x, axis, perm=[(s, (s + step) % size) for s in range(size)])


def tp_receive(x, me, size, width, offset):
    stride = x.shape[1] // size
    pieces = [lax.dynamic_slice_in_dim(x, me * stride + offset, width, 1)]
    for step in range(1, size):
        dest = (me + step) % size
        piece = lax.dynamic_slice_in_dim(x, dest * stride + offset, width, 1)
        pieces.append(shift(piece, "tp", step, size))
    return jnp.stack(pieces)


def tp_receive_many(items, me, size):
    owns, sends = [], []
    for x, width, offset in items:
        stride = x.shape[1] // size
        owns.append(lax.dynamic_slice_in_dim(x, me * stride + offset, width, 1))
        sends.append(
            [lax.dynamic_slice_in_dim(x, ((me + step) % size) * stride + offset, width, 1)
             for step in range(1, size)]
        )
    received = [
        shift(tuple(s[step - 1] for s in sends), "tp", step, size) for step in range(1, size)
    ]
    return [
        jnp.stack([owns[i]] + [received[step - 1][i] for step in range(1, size)])
        for i in range(len(items))
    ]


def tp_send(stack, me, size):
    return [stack[0]] + [shift(stack[step], "tp", step, size) for step in range(1, size)]


def tp_columns(chunk_pieces, me, size):
    parts = []
    for source in range(size):
        step = (me - source) % size
        for pieces in chunk_pieces:
            parts.append(lax.dynamic_index_in_dim(jnp.stack(pieces), step, 0, keepdims=False))
    return jnp.concatenate(parts, axis=1)


def source_order(stack, me, size):
    order = (me - jnp.arange(size, dtype=jnp.int32)) % size
    return jnp.take(stack, order, axis=0)


def body(queries, key_rows, value_rows, selected, own_flag, cotangent):
    holders = lax.axis_size("ctx")
    tp_size = lax.axis_size("tp")
    position = lax.axis_index("ctx")
    me = lax.axis_index("tp")
    rows_in = queries.shape[0]
    q_cols = queries.shape[1] // tp_size
    k_cols = key_rows.shape[1] // tp_size
    tokens = rows_in * tp_size
    assert tokens == BLK
    head_count = k_cols // HD
    group_size = q_cols // k_cols
    chunk_count = 2 if head_count % 2 == 0 else 1
    chunk_heads = head_count // chunk_count
    q_width = chunk_heads * group_size * HD
    key_stack, value_stack, first_queries, first_upstream = tp_receive_many(
        [(key_rows, k_cols, 0), (value_rows, k_cols, 0), (queries, q_width, 0), (cotangent, q_width, 0)],
        me, tp_size,
    )
    key_heads = source_order(key_stack, me, tp_size).reshape(tokens, k_cols)
    value_heads = source_order(value_stack, me, tp_size).reshape(tokens, k_cols)
    head_count = k_cols // HD
    group_size = q_cols // k_cols
    span_rows = BLK // holders

    kv = jnp.stack(
        [key_heads.reshape(holders, span_rows, head_count, HD),
         value_heads.reshape(holders, span_rows, head_count, HD)],
        axis=1,
    )
    spread = lax.all_to_all(kv, "ctx", split_axis=0, concat_axis=0, tiled=True)
    my_selected = lax.dynamic_index_in_dim(selected, position, 0, keepdims=False)
    my_flags = lax.dynamic_index_in_dim(own_flag, position, 0, keepdims=False)
    live_all = jnp.concatenate(
        [(my_selected < position).astype(jnp.int32), (my_flags == 1).astype(jnp.int32)[:, None]],
        axis=1,
    )
    tp_info = me.astype(jnp.int32).reshape(1)
    chunk_k_cols = chunk_heads * HD

    next_stacks = [
        tp_receive(queries, me, tp_size, q_width, (chunk_count - 1) * q_width),
        tp_receive(cotangent, me, tp_size, q_width, (chunk_count - 1) * q_width),
    ]
    results = []
    for chunk in range(chunk_count):
        first = chunk * chunk_heads
        chunk_selected = selected[:, first : first + chunk_heads]
        head_ids = jnp.arange(first, first + chunk_heads, dtype=jnp.int32)[None, :, None]
        send = spread[chunk_selected, :, :, head_ids, :]
        if chunk == 0:
            query_stack, upstream_stack = first_queries, first_upstream
            send, *next_stacks = lax.optimization_barrier((send, *next_stacks))
        else:
            query_stack, upstream_stack = next_stacks
            send, _, _ = lax.optimization_barrier((send, first_queries, first_upstream))
        got = lax.all_to_all(send, "ctx", split_axis=0, concat_axis=4, tiled=True)
        fetched = got[0]
        live = live_all[first : first + chunk_heads].reshape(-1)
        attended, grad_queries, grad_sel, grad_key_own, grad_value_own = attention(
            live, tp_info, query_stack, upstream_stack, fetched, key_heads, value_heads,
            group_size, first,
        )
        attended = tp_send(attended, me, tp_size)
        grad_queries = tp_send(grad_queries, me, tp_size)

        send_back = grad_sel.astype(jnp.bfloat16).reshape(
            chunk_heads, TOPK, 2, holders, span_rows, HD
        )
        got_back = lax.all_to_all(send_back, "ctx", split_axis=3, concat_axis=1, tiled=True)
        flat = got_back.reshape(chunk_heads, holders * TOPK, 2 * span_rows * HD).astype(
            jnp.float32
        )
        targets = chunk_selected.transpose(1, 0, 2).reshape(chunk_heads, holders * TOPK)
        table = (
            targets[:, None, :] == jnp.arange(holders, dtype=jnp.int32)[None, :, None]
        ).astype(jnp.float32)
        summed = jnp.einsum("gjn,gnx->gjx", table, flat, precision=lax.Precision.HIGHEST)
        owner = summed.reshape(chunk_heads, holders, 2, span_rows, HD).astype(jnp.bfloat16)
        back = lax.all_to_all(owner, "ctx", split_axis=1, concat_axis=3, tiled=True)
        back = back[:, 0].astype(jnp.float32)
        total_keys = back[:, 0].transpose(1, 0, 2).reshape(tokens, chunk_k_cols) + grad_key_own
        total_values = (
            back[:, 1].transpose(1, 0, 2).reshape(tokens, chunk_k_cols) + grad_value_own
        )
        results.append((attended, grad_queries, total_keys, total_values))

    def rows_by_destination(total):
        stack = total.astype(jnp.bfloat16).reshape(tp_size, rows_in, k_cols)
        order = (me + jnp.arange(tp_size, dtype=jnp.int32)) % tp_size
        return tp_columns([tp_send(jnp.take(stack, order, axis=0), me, tp_size)], me, tp_size)

    attended = tp_columns([r[0] for r in results], me, tp_size)
    grad_queries = tp_columns([r[1] for r in results], me, tp_size)
    total_keys = jnp.concatenate([r[2] for r in results], axis=1)
    total_values = jnp.concatenate([r[3] for r in results], axis=1)
    return (attended, grad_queries, rows_by_destination(total_keys), rows_by_destination(total_values))


def solution(mesh):
    in_specs = (
        P(("ctx", "tp"), None),
        P(("ctx", "tp"), None),
        P(("ctx", "tp"), None),
        P(None, "tp", None),
        P(None, "tp"),
        P(("ctx", "tp"), None),
    )
    out_specs = (
        P(("ctx", "tp"), None),
        P(("ctx", "tp"), None),
        P(("ctx", "tp"), None),
        P(("ctx", "tp"), None),
    )
    return jax.shard_map(body, mesh=mesh, in_specs=in_specs, out_specs=out_specs, check_vma=False)
```

```python
import functools
import math

import jax
import jax.numpy as jnp
from jax import lax
from jax.experimental import pallas as pl
from jax.experimental.pallas import tpu as pltpu
from jax.sharding import PartitionSpec as P

HD = 128
BLK = 512
TOPK = 3


def attention_kernel(
    live_ref, tp_ref, q_ref, do_ref, kvs_ref, ko_ref, vo_ref,
    o_ref, dq_ref, dsel_ref, dko_ref, dvo_ref, acc_ref, kt_ref, vt_ref, *, slot_count, row_tile, scale, tiles, own_rows
):
    g = pl.program_id(0)
    h = pl.program_id(1)
    t = pl.program_id(2)

    @pl.when((h == 0) & (t == 0))
    def _():
        acc_ref[...] = jnp.zeros(acc_ref.shape, acc_ref.dtype)
        for r in range(slot_count - 1):
            kt_ref[r] = kvs_ref[r, 0].T
            vt_ref[r] = kvs_ref[r, 1].T
        kt_ref[slot_count - 1] = ko_ref[...].T
        vt_ref[slot_count - 1] = vo_ref[...].T

    def run(own_width):
        q = q_ref[...]
        do = do_ref[...]
        keys = [kvs_ref[r, 0] for r in range(slot_count - 1)] + [ko_ref[:own_width]]
        values = [kvs_ref[r, 1] for r in range(slot_count - 1)] + [vo_ref[:own_width]]
        keys_t = [kt_ref[r] for r in range(slot_count - 1)] + [kt_ref[slot_count - 1, :, :own_width]]
        values_t = [vt_ref[r] for r in range(slot_count - 1)] + [vt_ref[slot_count - 1, :, :own_width]]
        q_t = q.T
        do_t = do.T
        scores = []
        for r in range(slot_count):
            s = jnp.dot(q, keys_t[r], preferred_element_type=jnp.float32) * scale
            live = live_ref[g * slot_count + r] > 0
            if r == slot_count - 1:
                row = t * row_tile + lax.broadcasted_iota(jnp.int32, s.shape, 0)
                col = lax.broadcasted_iota(jnp.int32, s.shape, 1)
                s = jnp.where(live & (row >= col), s, -jnp.inf)
            else:
                s = jnp.where(live, s, -jnp.inf)
            scores.append(s)
        row_max = scores[0].max(axis=1, keepdims=True)
        for s in scores[1:]:
            row_max = jnp.maximum(row_max, s.max(axis=1, keepdims=True))
        weights = [jnp.exp(s - row_max) for s in scores]
        total = weights[0].sum(axis=1, keepdims=True)
        for w in weights[1:]:
            total = total + w.sum(axis=1, keepdims=True)
        inverse = 1.0 / total
        probs = [w * inverse for w in weights]
        probs_low = [p.astype(jnp.bfloat16) for p in probs]
        out = jnp.dot(probs_low[0], values[0], preferred_element_type=jnp.float32)
        for r in range(1, slot_count):
            out = out + jnp.dot(probs_low[r], values[r], preferred_element_type=jnp.float32)
        out_low = out.astype(jnp.bfloat16)
        o_ref[...] = out_low
        delta = jnp.sum(do.astype(jnp.float32) * out_low.astype(jnp.float32), axis=1, keepdims=True)
        grad_q = None
        for r in range(slot_count):
            grad_p = jnp.dot(do, values_t[r], preferred_element_type=jnp.float32)
            grad_s = (probs[r] * (grad_p - delta)).astype(jnp.bfloat16)
            part = jnp.dot(grad_s, keys[r], preferred_element_type=jnp.float32)
            grad_q = part if grad_q is None else grad_q + part
            width = keys[r].shape[0]
            acc_ref[r, 0, :, :width] += jnp.dot(q_t, grad_s, preferred_element_type=jnp.float32) * scale
            acc_ref[r, 1, :, :width] += jnp.dot(do_t, probs_low[r], preferred_element_type=jnp.float32)
        dq_ref[...] = (grad_q * scale).astype(jnp.bfloat16)

    for tile in range(tiles):
        width = -(-(tile + 1) * row_tile // HD) * HD
        pl.when(t == tile)(functools.partial(run, min(width, own_rows)))

    @pl.when((h == pl.num_programs(1) - 1) & (t == pl.num_programs(2) - 1))
    def _():
        for r in range(slot_count - 1):
            dsel_ref[r, 0] = acc_ref[r, 0].T
            dsel_ref[r, 1] = acc_ref[r, 1].T
        dko_ref[...] = acc_ref[slot_count - 1, 0].T
        dvo_ref[...] = acc_ref[slot_count - 1, 1].T


def attention(live, tp_info, query_stack, upstream_stack, fetched, key_heads, value_heads, group_size, first):
    tp_size, row_tile, _ = query_stack.shape
    tokens = tp_size * row_tile
    head_count = fetched.shape[0]
    q_cols = head_count * group_size * HD
    slot_count = TOPK + 1
    grid = (head_count, group_size, tp_size)
    kernel = functools.partial(
        attention_kernel, slot_count=slot_count, row_tile=row_tile, scale=1.0 / math.sqrt(HD),
        tiles=tp_size, own_rows=BLK,
    )

    def piece_in(g, h, t, live, tp):
        return ((tp[0] - t + tp_size) % tp_size, 0, g * group_size + h)

    def piece_out(g, h, t, live, tp):
        return ((t - tp[0] + tp_size) % tp_size, 0, g * group_size + h)

    in_block = pl.BlockSpec((None, row_tile, HD), piece_in)
    out_block = pl.BlockSpec((None, row_tile, HD), piece_out)
    sel_block = pl.BlockSpec((None, TOPK, 2, BLK, HD), lambda g, h, t, live, tp: (g, 0, 0, 0, 0))
    own_in = pl.BlockSpec((BLK, HD), lambda g, h, t, live, tp: (0, first + g))
    own_out = pl.BlockSpec((BLK, HD), lambda g, h, t, live, tp: (0, g))
    flops = 12 * head_count * group_size * tokens * slot_count * BLK * HD
    bytes_accessed = 2 * (4 * tokens * q_cols + 3 * fetched.size + 6 * tokens * head_count * HD)
    return pl.pallas_call(
        kernel,
        grid_spec=pltpu.PrefetchScalarGridSpec(
            num_scalar_prefetch=2,
            grid=grid,
            in_specs=[in_block, in_block, sel_block, own_in, own_in],
            out_specs=[out_block, out_block, sel_block, own_out, own_out],
            scratch_shapes=[
                pltpu.VMEM((slot_count, 2, HD, BLK), jnp.float32),
                pltpu.VMEM((slot_count, HD, BLK), jnp.bfloat16),
                pltpu.VMEM((slot_count, HD, BLK), jnp.bfloat16),
            ],
        ),
        out_shape=[
            jax.ShapeDtypeStruct((tp_size, row_tile, q_cols), jnp.bfloat16),
            jax.ShapeDtypeStruct((tp_size, row_tile, q_cols), jnp.bfloat16),
            jax.ShapeDtypeStruct(fetched.shape, jnp.float32),
            jax.ShapeDtypeStruct((tokens, head_count * HD), jnp.float32),
            jax.ShapeDtypeStruct((tokens, head_count * HD), jnp.float32),
        ],
        compiler_params=pltpu.CompilerParams(
            dimension_semantics=("arbitrary", "arbitrary", "arbitrary"),
        ),
        cost_estimate=pl.CostEstimate(
            flops=flops,
            transcendentals=head_count * group_size * tokens * slot_count * BLK,
            bytes_accessed=bytes_accessed,
        ),
    )(live, tp_info, query_stack, upstream_stack, fetched, key_heads, value_heads)


def shift(x, axis, step, size):
    return lax.ppermute(x, axis, perm=[(s, (s + step) % size) for s in range(size)])


def tp_receive(x, me, size, width, offset):
    stride = x.shape[1] // size
    pieces = [lax.dynamic_slice_in_dim(x, me * stride + offset, width, 1)]
    for step in range(1, size):
        dest = (me + step) % size
        piece = lax.dynamic_slice_in_dim(x, dest * stride + offset, width, 1)
        pieces.append(shift(piece, "tp", step, size))
    return jnp.stack(pieces)


def tp_receive_many(items, me, size):
    owns, sends = [], []
    for x, width, offset in items:
        stride = x.shape[1] // size
        owns.append(lax.dynamic_slice_in_dim(x, me * stride + offset, width, 1))
        sends.append(
            [lax.dynamic_slice_in_dim(x, ((me + step) % size) * stride + offset, width, 1)
             for step in range(1, size)]
        )
    received = [
        shift(tuple(s[step - 1] for s in sends), "tp", step, size) for step in range(1, size)
    ]
    return [
        jnp.stack([owns[i]] + [received[step - 1][i] for step in range(1, size)])
        for i in range(len(items))
    ]


def tp_send(stack, me, size):
    return [stack[0]] + [shift(stack[step], "tp", step, size) for step in range(1, size)]


def tp_columns(chunk_pieces, me, size):
    parts = []
    for source in range(size):
        step = (me - source) % size
        for pieces in chunk_pieces:
            parts.append(lax.dynamic_index_in_dim(jnp.stack(pieces), step, 0, keepdims=False))
    return jnp.concatenate(parts, axis=1)


def source_order(stack, me, size):
    order = (me - jnp.arange(size, dtype=jnp.int32)) % size
    return jnp.take(stack, order, axis=0)


def body(queries, key_rows, value_rows, selected, own_flag, cotangent):
    holders = lax.axis_size("ctx")
    tp_size = lax.axis_size("tp")
    position = lax.axis_index("ctx")
    me = lax.axis_index("tp")
    rows_in = queries.shape[0]
    q_cols = queries.shape[1] // tp_size
    k_cols = key_rows.shape[1] // tp_size
    tokens = rows_in * tp_size
    assert tokens == BLK
    head_count = k_cols // HD
    group_size = q_cols // k_cols
    chunk_count = 2 if head_count % 2 == 0 else 1
    chunk_heads = head_count // chunk_count
    q_width = chunk_heads * group_size * HD
    key_stack, value_stack, first_queries, first_upstream = tp_receive_many(
        [(key_rows, k_cols, 0), (value_rows, k_cols, 0), (queries, q_width, 0), (cotangent, q_width, 0)],
        me, tp_size,
    )
    key_heads = source_order(key_stack, me, tp_size).reshape(tokens, k_cols)
    value_heads = source_order(value_stack, me, tp_size).reshape(tokens, k_cols)
    head_count = k_cols // HD
    group_size = q_cols // k_cols
    span_rows = BLK // holders

    kv = jnp.stack(
        [key_heads.reshape(holders, span_rows, head_count, HD),
         value_heads.reshape(holders, span_rows, head_count, HD)],
        axis=1,
    )
    spread = lax.all_to_all(kv, "ctx", split_axis=0, concat_axis=0, tiled=True)
    my_selected = lax.dynamic_index_in_dim(selected, position, 0, keepdims=False)
    my_flags = lax.dynamic_index_in_dim(own_flag, position, 0, keepdims=False)
    live_all = jnp.concatenate(
        [(my_selected < position).astype(jnp.int32), (my_flags == 1).astype(jnp.int32)[:, None]],
        axis=1,
    )
    tp_info = me.astype(jnp.int32).reshape(1)
    chunk_k_cols = chunk_heads * HD

    next_stacks = [
        tp_receive(queries, me, tp_size, q_width, (chunk_count - 1) * q_width),
        tp_receive(cotangent, me, tp_size, q_width, (chunk_count - 1) * q_width),
    ]
    results = []
    for chunk in range(chunk_count):
        first = chunk * chunk_heads
        chunk_selected = selected[:, first : first + chunk_heads]
        head_ids = jnp.arange(first, first + chunk_heads, dtype=jnp.int32)[None, :, None]
        send = spread[chunk_selected, :, :, head_ids, :]
        if chunk == 0:
            query_stack, upstream_stack = first_queries, first_upstream
            send, *next_stacks = lax.optimization_barrier((send, *next_stacks))
        else:
            query_stack, upstream_stack = next_stacks
            send, _, _ = lax.optimization_barrier((send, first_queries, first_upstream))
        got = lax.all_to_all(send, "ctx", split_axis=0, concat_axis=4, tiled=True)
        fetched = got[0]
        live = live_all[first : first + chunk_heads].reshape(-1)
        attended, grad_queries, grad_sel, grad_key_own, grad_value_own = attention(
            live, tp_info, query_stack, upstream_stack, fetched, key_heads, value_heads,
            group_size, first,
        )
        attended = tp_send(attended, me, tp_size)
        grad_queries = tp_send(grad_queries, me, tp_size)

        send_back = grad_sel.astype(jnp.bfloat16).reshape(
            chunk_heads, TOPK, 2, holders, span_rows, HD
        )
        got_back = lax.all_to_all(send_back, "ctx", split_axis=3, concat_axis=1, tiled=True)
        flat = got_back.reshape(chunk_heads, holders * TOPK, 2 * span_rows * HD).astype(
            jnp.float32
        )
        targets = chunk_selected.transpose(1, 0, 2).reshape(chunk_heads, holders * TOPK)
        table = (
            targets[:, None, :] == jnp.arange(holders, dtype=jnp.int32)[None, :, None]
        ).astype(jnp.float32)
        summed = jnp.einsum("gjn,gnx->gjx", table, flat, precision=lax.Precision.HIGHEST)
        owner = summed.reshape(chunk_heads, holders, 2, span_rows, HD).astype(jnp.bfloat16)
        back = lax.all_to_all(owner, "ctx", split_axis=1, concat_axis=3, tiled=True)
        back = back[:, 0].astype(jnp.float32)
        total_keys = back[:, 0].transpose(1, 0, 2).reshape(tokens, chunk_k_cols) + grad_key_own
        total_values = (
            back[:, 1].transpose(1, 0, 2).reshape(tokens, chunk_k_cols) + grad_value_own
        )
        results.append((attended, grad_queries, total_keys, total_values))

    def rows_by_destination(total):
        stack = total.astype(jnp.bfloat16).reshape(tp_size, rows_in, k_cols)
        order = (me + jnp.arange(tp_size, dtype=jnp.int32)) % tp_size
        return tp_columns([tp_send(jnp.take(stack, order, axis=0), me, tp_size)], me, tp_size)

    attended = tp_columns([r[0] for r in results], me, tp_size)
    grad_queries = tp_columns([r[1] for r in results], me, tp_size)
    total_keys = jnp.concatenate([r[2] for r in results], axis=1)
    total_values = jnp.concatenate([r[3] for r in results], axis=1)
    return (attended, grad_queries, rows_by_destination(total_keys), rows_by_destination(total_values))


def solution(mesh):
    in_specs = (
        P(("ctx", "tp"), None),
        P(("ctx", "tp"), None),
        P(("ctx", "tp"), None),
        P(None, "tp", None),
        P(None, "tp"),
        P(("ctx", "tp"), None),
    )
    out_specs = (
        P(("ctx", "tp"), None),
        P(("ctx", "tp"), None),
        P(("ctx", "tp"), None),
        P(("ctx", "tp"), None),
    )
    return jax.shard_map(body, mesh=mesh, in_specs=in_specs, out_specs=out_specs, check_vma=False)
```

```python
import functools
import math

import jax
import jax.numpy as jnp
from jax import lax
from jax.experimental import pallas as pl
from jax.experimental.pallas import tpu as pltpu
from jax.sharding import PartitionSpec as P

HD = 128
BLK = 512
TOPK = 3


def attention_kernel(
    live_ref, tp_ref, q_ref, do_ref, kvs_ref, ko_ref, vo_ref,
    o_ref, dq_ref, dsel_ref, dko_ref, dvo_ref, acc_ref, kt_ref, vt_ref, *, slot_count, row_tile, scale, tiles, own_rows
):
    g = pl.program_id(0)
    h = pl.program_id(1)
    t = pl.program_id(2)

    @pl.when((h == 0) & (t == 0))
    def _():
        acc_ref[...] = jnp.zeros(acc_ref.shape, acc_ref.dtype)
        for r in range(slot_count - 1):
            kt_ref[r] = kvs_ref[r, 0].T
            vt_ref[r] = kvs_ref[r, 1].T
        kt_ref[slot_count - 1] = ko_ref[...].T
        vt_ref[slot_count - 1] = vo_ref[...].T

    def run(own_width):
        q = q_ref[...]
        do = do_ref[...]
        keys = [kvs_ref[r, 0] for r in range(slot_count - 1)] + [ko_ref[:own_width]]
        values = [kvs_ref[r, 1] for r in range(slot_count - 1)] + [vo_ref[:own_width]]
        keys_t = [kt_ref[r] for r in range(slot_count - 1)] + [kt_ref[slot_count - 1, :, :own_width]]
        values_t = [vt_ref[r] for r in range(slot_count - 1)] + [vt_ref[slot_count - 1, :, :own_width]]
        q_t = q.T
        do_t = do.T
        scores = []
        for r in range(slot_count):
            s = jnp.dot(q, keys_t[r], preferred_element_type=jnp.float32) * scale
            live = live_ref[g * slot_count + r] > 0
            if r == slot_count - 1:
                row = t * row_tile + lax.broadcasted_iota(jnp.int32, s.shape, 0)
                col = lax.broadcasted_iota(jnp.int32, s.shape, 1)
                s = jnp.where(live & (row >= col), s, -jnp.inf)
            else:
                s = jnp.where(live, s, -jnp.inf)
            scores.append(s)
        row_max = scores[0].max(axis=1, keepdims=True)
        for s in scores[1:]:
            row_max = jnp.maximum(row_max, s.max(axis=1, keepdims=True))
        weights = [jnp.exp(s - row_max) for s in scores]
        total = weights[0].sum(axis=1, keepdims=True)
        for w in weights[1:]:
            total = total + w.sum(axis=1, keepdims=True)
        inverse = 1.0 / total
        probs = [w * inverse for w in weights]
        probs_low = [p.astype(jnp.bfloat16) for p in probs]
        out = jnp.dot(probs_low[0], values[0], preferred_element_type=jnp.float32)
        for r in range(1, slot_count):
            out = out + jnp.dot(probs_low[r], values[r], preferred_element_type=jnp.float32)
        out_low = out.astype(jnp.bfloat16)
        o_ref[...] = out_low
        delta = jnp.sum(do.astype(jnp.float32) * out_low.astype(jnp.float32), axis=1, keepdims=True)
        grad_q = None
        for r in range(slot_count):
            grad_p = jnp.dot(do, values_t[r], preferred_element_type=jnp.float32)
            grad_s = (probs[r] * (grad_p - delta)).astype(jnp.bfloat16)
            part = jnp.dot(grad_s, keys[r], preferred_element_type=jnp.float32)
            grad_q = part if grad_q is None else grad_q + part
            width = keys[r].shape[0]
            acc_ref[r, 0, :, :width] += jnp.dot(q_t, grad_s, preferred_element_type=jnp.float32)
            acc_ref[r, 1, :, :width] += jnp.dot(do_t, probs_low[r], preferred_element_type=jnp.float32)
        dq_ref[...] = (grad_q * scale).astype(jnp.bfloat16)

    for tile in range(tiles):
        width = -(-(tile + 1) * row_tile // HD) * HD
        pl.when(t == tile)(functools.partial(run, min(width, own_rows)))

    @pl.when((h == pl.num_programs(1) - 1) & (t == pl.num_programs(2) - 1))
    def _():
        for r in range(slot_count - 1):
            dsel_ref[r, 0] = acc_ref[r, 0].T * scale
            dsel_ref[r, 1] = acc_ref[r, 1].T
        dko_ref[...] = acc_ref[slot_count - 1, 0].T * scale
        dvo_ref[...] = acc_ref[slot_count - 1, 1].T


def attention(live, tp_info, query_stack, upstream_stack, fetched, key_heads, value_heads, group_size, first):
    tp_size, row_tile, _ = query_stack.shape
    tokens = tp_size * row_tile
    head_count = fetched.shape[0]
    q_cols = head_count * group_size * HD
    slot_count = TOPK + 1
    grid = (head_count, group_size, tp_size)
    kernel = functools.partial(
        attention_kernel, slot_count=slot_count, row_tile=row_tile, scale=1.0 / math.sqrt(HD),
        tiles=tp_size, own_rows=BLK,
    )

    def piece_in(g, h, t, live, tp):
        return ((tp[0] - t + tp_size) % tp_size, 0, g * group_size + h)

    def piece_out(g, h, t, live, tp):
        return ((t - tp[0] + tp_size) % tp_size, 0, g * group_size + h)

    in_block = pl.BlockSpec((None, row_tile, HD), piece_in)
    out_block = pl.BlockSpec((None, row_tile, HD), piece_out)
    sel_block = pl.BlockSpec((None, TOPK, 2, BLK, HD), lambda g, h, t, live, tp: (g, 0, 0, 0, 0))
    own_in = pl.BlockSpec((BLK, HD), lambda g, h, t, live, tp: (0, first + g))
    own_out = pl.BlockSpec((BLK, HD), lambda g, h, t, live, tp: (0, g))
    flops = 12 * head_count * group_size * tokens * slot_count * BLK * HD
    bytes_accessed = 2 * (4 * tokens * q_cols + 3 * fetched.size + 6 * tokens * head_count * HD)
    return pl.pallas_call(
        kernel,
        grid_spec=pltpu.PrefetchScalarGridSpec(
            num_scalar_prefetch=2,
            grid=grid,
            in_specs=[in_block, in_block, sel_block, own_in, own_in],
            out_specs=[out_block, out_block, sel_block, own_out, own_out],
            scratch_shapes=[
                pltpu.VMEM((slot_count, 2, HD, BLK), jnp.float32),
                pltpu.VMEM((slot_count, HD, BLK), jnp.bfloat16),
                pltpu.VMEM((slot_count, HD, BLK), jnp.bfloat16),
            ],
        ),
        out_shape=[
            jax.ShapeDtypeStruct((tp_size, row_tile, q_cols), jnp.bfloat16),
            jax.ShapeDtypeStruct((tp_size, row_tile, q_cols), jnp.bfloat16),
            jax.ShapeDtypeStruct(fetched.shape, jnp.float32),
            jax.ShapeDtypeStruct((tokens, head_count * HD), jnp.float32),
            jax.ShapeDtypeStruct((tokens, head_count * HD), jnp.float32),
        ],
        compiler_params=pltpu.CompilerParams(
            dimension_semantics=("arbitrary", "arbitrary", "arbitrary"),
        ),
        cost_estimate=pl.CostEstimate(
            flops=flops,
            transcendentals=head_count * group_size * tokens * slot_count * BLK,
            bytes_accessed=bytes_accessed,
        ),
    )(live, tp_info, query_stack, upstream_stack, fetched, key_heads, value_heads)


def shift(x, axis, step, size):
    return lax.ppermute(x, axis, perm=[(s, (s + step) % size) for s in range(size)])


def tp_receive(x, me, size, width, offset):
    stride = x.shape[1] // size
    pieces = [lax.dynamic_slice_in_dim(x, me * stride + offset, width, 1)]
    for step in range(1, size):
        dest = (me + step) % size
        piece = lax.dynamic_slice_in_dim(x, dest * stride + offset, width, 1)
        pieces.append(shift(piece, "tp", step, size))
    return jnp.stack(pieces)


def tp_receive_many(items, me, size):
    owns, sends = [], []
    for x, width, offset in items:
        stride = x.shape[1] // size
        owns.append(lax.dynamic_slice_in_dim(x, me * stride + offset, width, 1))
        sends.append(
            [lax.dynamic_slice_in_dim(x, ((me + step) % size) * stride + offset, width, 1)
             for step in range(1, size)]
        )
    received = [
        shift(tuple(s[step - 1] for s in sends), "tp", step, size) for step in range(1, size)
    ]
    return [
        jnp.stack([owns[i]] + [received[step - 1][i] for step in range(1, size)])
        for i in range(len(items))
    ]


def tp_send(stack, me, size):
    return [stack[0]] + [shift(stack[step], "tp", step, size) for step in range(1, size)]


def tp_columns(chunk_pieces, me, size):
    parts = []
    for source in range(size):
        step = (me - source) % size
        for pieces in chunk_pieces:
            parts.append(lax.dynamic_index_in_dim(jnp.stack(pieces), step, 0, keepdims=False))
    return jnp.concatenate(parts, axis=1)


def source_order(stack, me, size):
    order = (me - jnp.arange(size, dtype=jnp.int32)) % size
    return jnp.take(stack, order, axis=0)


def body(queries, key_rows, value_rows, selected, own_flag, cotangent):
    holders = lax.axis_size("ctx")
    tp_size = lax.axis_size("tp")
    position = lax.axis_index("ctx")
    me = lax.axis_index("tp")
    rows_in = queries.shape[0]
    q_cols = queries.shape[1] // tp_size
    k_cols = key_rows.shape[1] // tp_size
    tokens = rows_in * tp_size
    assert tokens == BLK
    head_count = k_cols // HD
    group_size = q_cols // k_cols
    chunk_count = 2 if head_count % 2 == 0 else 1
    chunk_heads = head_count // chunk_count
    q_width = chunk_heads * group_size * HD
    key_stack, value_stack, first_queries, first_upstream = tp_receive_many(
        [(key_rows, k_cols, 0), (value_rows, k_cols, 0), (queries, q_width, 0), (cotangent, q_width, 0)],
        me, tp_size,
    )
    key_heads = source_order(key_stack, me, tp_size).reshape(tokens, k_cols)
    value_heads = source_order(value_stack, me, tp_size).reshape(tokens, k_cols)
    head_count = k_cols // HD
    group_size = q_cols // k_cols
    span_rows = BLK // holders

    kv = jnp.stack(
        [key_heads.reshape(holders, span_rows, head_count, HD),
         value_heads.reshape(holders, span_rows, head_count, HD)],
        axis=1,
    )
    spread = lax.all_to_all(kv, "ctx", split_axis=0, concat_axis=0, tiled=True)
    my_selected = lax.dynamic_index_in_dim(selected, position, 0, keepdims=False)
    my_flags = lax.dynamic_index_in_dim(own_flag, position, 0, keepdims=False)
    live_all = jnp.concatenate(
        [(my_selected < position).astype(jnp.int32), (my_flags == 1).astype(jnp.int32)[:, None]],
        axis=1,
    )
    tp_info = me.astype(jnp.int32).reshape(1)
    chunk_k_cols = chunk_heads * HD

    next_stacks = [
        tp_receive(queries, me, tp_size, q_width, (chunk_count - 1) * q_width),
        tp_receive(cotangent, me, tp_size, q_width, (chunk_count - 1) * q_width),
    ]
    results = []
    for chunk in range(chunk_count):
        first = chunk * chunk_heads
        chunk_selected = selected[:, first : first + chunk_heads]
        head_ids = jnp.arange(first, first + chunk_heads, dtype=jnp.int32)[None, :, None]
        send = spread[chunk_selected, :, :, head_ids, :]
        if chunk == 0:
            query_stack, upstream_stack = first_queries, first_upstream
            send, *next_stacks = lax.optimization_barrier((send, *next_stacks))
        else:
            query_stack, upstream_stack = next_stacks
            send, _, _ = lax.optimization_barrier((send, first_queries, first_upstream))
        got = lax.all_to_all(send, "ctx", split_axis=0, concat_axis=4, tiled=True)
        fetched = got[0]
        live = live_all[first : first + chunk_heads].reshape(-1)
        attended, grad_queries, grad_sel, grad_key_own, grad_value_own = attention(
            live, tp_info, query_stack, upstream_stack, fetched, key_heads, value_heads,
            group_size, first,
        )
        attended = tp_send(attended, me, tp_size)
        grad_queries = tp_send(grad_queries, me, tp_size)

        send_back = grad_sel.astype(jnp.bfloat16).reshape(
            chunk_heads, TOPK, 2, holders, span_rows, HD
        )
        got_back = lax.all_to_all(send_back, "ctx", split_axis=3, concat_axis=1, tiled=True)
        flat = got_back.reshape(chunk_heads, holders * TOPK, 2 * span_rows * HD).astype(
            jnp.float32
        )
        targets = chunk_selected.transpose(1, 0, 2).reshape(chunk_heads, holders * TOPK)
        table = (
            targets[:, None, :] == jnp.arange(holders, dtype=jnp.int32)[None, :, None]
        ).astype(jnp.float32)
        summed = jnp.einsum("gjn,gnx->gjx", table, flat, precision=lax.Precision.HIGHEST)
        owner = summed.reshape(chunk_heads, holders, 2, span_rows, HD).astype(jnp.bfloat16)
        back = lax.all_to_all(owner, "ctx", split_axis=1, concat_axis=3, tiled=True)
        back = back[:, 0].astype(jnp.float32)
        total_keys = back[:, 0].transpose(1, 0, 2).reshape(tokens, chunk_k_cols) + grad_key_own
        total_values = (
            back[:, 1].transpose(1, 0, 2).reshape(tokens, chunk_k_cols) + grad_value_own
        )
        results.append((attended, grad_queries, total_keys, total_values))

    def rows_by_destination(total):
        stack = total.astype(jnp.bfloat16).reshape(tp_size, rows_in, k_cols)
        order = (me + jnp.arange(tp_size, dtype=jnp.int32)) % tp_size
        return tp_columns([tp_send(jnp.take(stack, order, axis=0), me, tp_size)], me, tp_size)

    attended = tp_columns([r[0] for r in results], me, tp_size)
    grad_queries = tp_columns([r[1] for r in results], me, tp_size)
    total_keys = jnp.concatenate([r[2] for r in results], axis=1)
    total_values = jnp.concatenate([r[3] for r in results], axis=1)
    return (attended, grad_queries, rows_by_destination(total_keys), rows_by_destination(total_values))


def solution(mesh):
    in_specs = (
        P(("ctx", "tp"), None),
        P(("ctx", "tp"), None),
        P(("ctx", "tp"), None),
        P(None, "tp", None),
        P(None, "tp"),
        P(("ctx", "tp"), None),
    )
    out_specs = (
        P(("ctx", "tp"), None),
        P(("ctx", "tp"), None),
        P(("ctx", "tp"), None),
        P(("ctx", "tp"), None),
    )
    return jax.shard_map(body, mesh=mesh, in_specs=in_specs, out_specs=out_specs, check_vma=False)
```

```python
import functools
import math

import jax
import jax.numpy as jnp
from jax import lax
from jax.experimental import pallas as pl
from jax.experimental.pallas import tpu as pltpu
from jax.sharding import PartitionSpec as P

HD = 128
BLK = 512
TOPK = 3


def attention_kernel(
    live_ref, tp_ref, q_ref, do_ref, kvs_ref, ko_ref, vo_ref,
    o_ref, dq_ref, dsel_ref, dko_ref, dvo_ref, acc_ref, kt_ref, vt_ref, *, slot_count, row_tile, scale, tiles, own_rows
):
    g = pl.program_id(0)
    h = pl.program_id(1)
    t = pl.program_id(2)

    @pl.when((h == 0) & (t == 0))
    def _():
        acc_ref[...] = jnp.zeros(acc_ref.shape, acc_ref.dtype)
        for r in range(slot_count - 1):
            kt_ref[r] = kvs_ref[r, 0].T
            vt_ref[r] = kvs_ref[r, 1].T
        kt_ref[slot_count - 1] = ko_ref[...].T
        vt_ref[slot_count - 1] = vo_ref[...].T

    def run(own_width):
        q = q_ref[...]
        do = do_ref[...]
        keys = [kvs_ref[r, 0] for r in range(slot_count - 1)] + [ko_ref[:own_width]]
        values = [kvs_ref[r, 1] for r in range(slot_count - 1)] + [vo_ref[:own_width]]
        keys_t = [kt_ref[r] for r in range(slot_count - 1)] + [kt_ref[slot_count - 1, :, :own_width]]
        values_t = [vt_ref[r] for r in range(slot_count - 1)] + [vt_ref[slot_count - 1, :, :own_width]]
        q_t = q.T
        do_t = do.T
        scores = []
        for r in range(slot_count):
            s = jnp.dot(q, keys_t[r], preferred_element_type=jnp.float32) * scale
            live = live_ref[g * slot_count + r] > 0
            if r == slot_count - 1:
                row = t * row_tile + lax.broadcasted_iota(jnp.int32, s.shape, 0)
                col = lax.broadcasted_iota(jnp.int32, s.shape, 1)
                s = jnp.where(live & (row >= col), s, -jnp.inf)
            else:
                s = jnp.where(live, s, -jnp.inf)
            scores.append(s)
        row_max = scores[0].max(axis=1, keepdims=True)
        for s in scores[1:]:
            row_max = jnp.maximum(row_max, s.max(axis=1, keepdims=True))
        weights = [jnp.exp(s - row_max) for s in scores]
        total = weights[0].sum(axis=1, keepdims=True)
        for w in weights[1:]:
            total = total + w.sum(axis=1, keepdims=True)
        inverse = 1.0 / total
        probs_low = [(w * inverse).astype(jnp.bfloat16) for w in weights]
        out = jnp.dot(probs_low[0], values[0], preferred_element_type=jnp.float32)
        for r in range(1, slot_count):
            out = out + jnp.dot(probs_low[r], values[r], preferred_element_type=jnp.float32)
        out_low = out.astype(jnp.bfloat16)
        o_ref[...] = out_low
        delta = jnp.sum(do.astype(jnp.float32) * out_low.astype(jnp.float32), axis=1, keepdims=True)
        grad_q = None
        for r in range(slot_count):
            grad_p = jnp.dot(do, values_t[r], preferred_element_type=jnp.float32)
            grad_s = (probs_low[r].astype(jnp.float32) * (grad_p - delta)).astype(jnp.bfloat16)
            part = jnp.dot(grad_s, keys[r], preferred_element_type=jnp.float32)
            grad_q = part if grad_q is None else grad_q + part
            width = keys[r].shape[0]
            acc_ref[r, 0, :, :width] += jnp.dot(q_t, grad_s, preferred_element_type=jnp.float32) * scale
            acc_ref[r, 1, :, :width] += jnp.dot(do_t, probs_low[r], preferred_element_type=jnp.float32)
        dq_ref[...] = (grad_q * scale).astype(jnp.bfloat16)

    for tile in range(tiles):
        width = -(-(tile + 1) * row_tile // HD) * HD
        pl.when(t == tile)(functools.partial(run, min(width, own_rows)))

    @pl.when((h == pl.num_programs(1) - 1) & (t == pl.num_programs(2) - 1))
    def _():
        for r in range(slot_count - 1):
            dsel_ref[r, 0] = acc_ref[r, 0].T
            dsel_ref[r, 1] = acc_ref[r, 1].T
        dko_ref[...] = acc_ref[slot_count - 1, 0].T
        dvo_ref[...] = acc_ref[slot_count - 1, 1].T


def attention(live, tp_info, query_stack, upstream_stack, fetched, key_heads, value_heads, group_size, first):
    tp_size, row_tile, _ = query_stack.shape
    tokens = tp_size * row_tile
    head_count = fetched.shape[0]
    q_cols = head_count * group_size * HD
    slot_count = TOPK + 1
    grid = (head_count, group_size, tp_size)
    kernel = functools.partial(
        attention_kernel, slot_count=slot_count, row_tile=row_tile, scale=1.0 / math.sqrt(HD),
        tiles=tp_size, own_rows=BLK,
    )

    def piece_in(g, h, t, live, tp):
        return ((tp[0] - t + tp_size) % tp_size, 0, g * group_size + h)

    def piece_out(g, h, t, live, tp):
        return ((t - tp[0] + tp_size) % tp_size, 0, g * group_size + h)

    in_block = pl.BlockSpec((None, row_tile, HD), piece_in)
    out_block = pl.BlockSpec((None, row_tile, HD), piece_out)
    sel_block = pl.BlockSpec((None, TOPK, 2, BLK, HD), lambda g, h, t, live, tp: (g, 0, 0, 0, 0))
    own_in = pl.BlockSpec((BLK, HD), lambda g, h, t, live, tp: (0, first + g))
    own_out = pl.BlockSpec((BLK, HD), lambda g, h, t, live, tp: (0, g))
    flops = 12 * head_count * group_size * tokens * slot_count * BLK * HD
    bytes_accessed = 2 * (4 * tokens * q_cols + 3 * fetched.size + 6 * tokens * head_count * HD)
    return pl.pallas_call(
        kernel,
        grid_spec=pltpu.PrefetchScalarGridSpec(
            num_scalar_prefetch=2,
            grid=grid,
            in_specs=[in_block, in_block, sel_block, own_in, own_in],
            out_specs=[out_block, out_block, sel_block, own_out, own_out],
            scratch_shapes=[
                pltpu.VMEM((slot_count, 2, HD, BLK), jnp.float32),
                pltpu.VMEM((slot_count, HD, BLK), jnp.bfloat16),
                pltpu.VMEM((slot_count, HD, BLK), jnp.bfloat16),
            ],
        ),
        out_shape=[
            jax.ShapeDtypeStruct((tp_size, row_tile, q_cols), jnp.bfloat16),
            jax.ShapeDtypeStruct((tp_size, row_tile, q_cols), jnp.bfloat16),
            jax.ShapeDtypeStruct(fetched.shape, jnp.float32),
            jax.ShapeDtypeStruct((tokens, head_count * HD), jnp.float32),
            jax.ShapeDtypeStruct((tokens, head_count * HD), jnp.float32),
        ],
        compiler_params=pltpu.CompilerParams(
            dimension_semantics=("arbitrary", "arbitrary", "arbitrary"),
        ),
        cost_estimate=pl.CostEstimate(
            flops=flops,
            transcendentals=head_count * group_size * tokens * slot_count * BLK,
            bytes_accessed=bytes_accessed,
        ),
    )(live, tp_info, query_stack, upstream_stack, fetched, key_heads, value_heads)


def shift(x, axis, step, size):
    return lax.ppermute(x, axis, perm=[(s, (s + step) % size) for s in range(size)])


def tp_receive(x, me, size, width, offset):
    stride = x.shape[1] // size
    pieces = [lax.dynamic_slice_in_dim(x, me * stride + offset, width, 1)]
    for step in range(1, size):
        dest = (me + step) % size
        piece = lax.dynamic_slice_in_dim(x, dest * stride + offset, width, 1)
        pieces.append(shift(piece, "tp", step, size))
    return jnp.stack(pieces)


def tp_receive_many(items, me, size):
    owns, sends = [], []
    for x, width, offset in items:
        stride = x.shape[1] // size
        owns.append(lax.dynamic_slice_in_dim(x, me * stride + offset, width, 1))
        sends.append(
            [lax.dynamic_slice_in_dim(x, ((me + step) % size) * stride + offset, width, 1)
             for step in range(1, size)]
        )
    received = [
        shift(tuple(s[step - 1] for s in sends), "tp", step, size) for step in range(1, size)
    ]
    return [
        jnp.stack([owns[i]] + [received[step - 1][i] for step in range(1, size)])
        for i in range(len(items))
    ]


def tp_send(stack, me, size):
    return [stack[0]] + [shift(stack[step], "tp", step, size) for step in range(1, size)]


def tp_columns(chunk_pieces, me, size):
    parts = []
    for source in range(size):
        step = (me - source) % size
        for pieces in chunk_pieces:
            parts.append(lax.dynamic_index_in_dim(jnp.stack(pieces), step, 0, keepdims=False))
    return jnp.concatenate(parts, axis=1)


def source_order(stack, me, size):
    order = (me - jnp.arange(size, dtype=jnp.int32)) % size
    return jnp.take(stack, order, axis=0)


def body(queries, key_rows, value_rows, selected, own_flag, cotangent):
    holders = lax.axis_size("ctx")
    tp_size = lax.axis_size("tp")
    position = lax.axis_index("ctx")
    me = lax.axis_index("tp")
    rows_in = queries.shape[0]
    q_cols = queries.shape[1] // tp_size
    k_cols = key_rows.shape[1] // tp_size
    tokens = rows_in * tp_size
    assert tokens == BLK
    head_count = k_cols // HD
    group_size = q_cols // k_cols
    chunk_count = 2 if head_count % 2 == 0 else 1
    chunk_heads = head_count // chunk_count
    q_width = chunk_heads * group_size * HD
    key_stack, value_stack, first_queries, first_upstream = tp_receive_many(
        [(key_rows, k_cols, 0), (value_rows, k_cols, 0), (queries, q_width, 0), (cotangent, q_width, 0)],
        me, tp_size,
    )
    key_heads = source_order(key_stack, me, tp_size).reshape(tokens, k_cols)
    value_heads = source_order(value_stack, me, tp_size).reshape(tokens, k_cols)
    head_count = k_cols // HD
    group_size = q_cols // k_cols
    span_rows = BLK // holders

    kv = jnp.stack(
        [key_heads.reshape(holders, span_rows, head_count, HD),
         value_heads.reshape(holders, span_rows, head_count, HD)],
        axis=1,
    )
    spread = lax.all_to_all(kv, "ctx", split_axis=0, concat_axis=0, tiled=True)
    my_selected = lax.dynamic_index_in_dim(selected, position, 0, keepdims=False)
    my_flags = lax.dynamic_index_in_dim(own_flag, position, 0, keepdims=False)
    live_all = jnp.concatenate(
        [(my_selected < position).astype(jnp.int32), (my_flags == 1).astype(jnp.int32)[:, None]],
        axis=1,
    )
    tp_info = me.astype(jnp.int32).reshape(1)
    chunk_k_cols = chunk_heads * HD

    next_stacks = [
        tp_receive(queries, me, tp_size, q_width, (chunk_count - 1) * q_width),
        tp_receive(cotangent, me, tp_size, q_width, (chunk_count - 1) * q_width),
    ]
    results = []
    for chunk in range(chunk_count):
        first = chunk * chunk_heads
        chunk_selected = selected[:, first : first + chunk_heads]
        head_ids = jnp.arange(first, first + chunk_heads, dtype=jnp.int32)[None, :, None]
        send = spread[chunk_selected, :, :, head_ids, :]
        if chunk == 0:
            query_stack, upstream_stack = first_queries, first_upstream
            send, *next_stacks = lax.optimization_barrier((send, *next_stacks))
        else:
            query_stack, upstream_stack = next_stacks
            send, _, _ = lax.optimization_barrier((send, first_queries, first_upstream))
        got = lax.all_to_all(send, "ctx", split_axis=0, concat_axis=4, tiled=True)
        fetched = got[0]
        live = live_all[first : first + chunk_heads].reshape(-1)
        attended, grad_queries, grad_sel, grad_key_own, grad_value_own = attention(
            live, tp_info, query_stack, upstream_stack, fetched, key_heads, value_heads,
            group_size, first,
        )
        attended = tp_send(attended, me, tp_size)
        grad_queries = tp_send(grad_queries, me, tp_size)

        send_back = grad_sel.astype(jnp.bfloat16).reshape(
            chunk_heads, TOPK, 2, holders, span_rows, HD
        )
        got_back = lax.all_to_all(send_back, "ctx", split_axis=3, concat_axis=1, tiled=True)
        flat = got_back.reshape(chunk_heads, holders * TOPK, 2 * span_rows * HD).astype(
            jnp.float32
        )
        targets = chunk_selected.transpose(1, 0, 2).reshape(chunk_heads, holders * TOPK)
        table = (
            targets[:, None, :] == jnp.arange(holders, dtype=jnp.int32)[None, :, None]
        ).astype(jnp.float32)
        summed = jnp.einsum("gjn,gnx->gjx", table, flat, precision=lax.Precision.HIGHEST)
        owner = summed.reshape(chunk_heads, holders, 2, span_rows, HD).astype(jnp.bfloat16)
        back = lax.all_to_all(owner, "ctx", split_axis=1, concat_axis=3, tiled=True)
        back = back[:, 0].astype(jnp.float32)
        total_keys = back[:, 0].transpose(1, 0, 2).reshape(tokens, chunk_k_cols) + grad_key_own
        total_values = (
            back[:, 1].transpose(1, 0, 2).reshape(tokens, chunk_k_cols) + grad_value_own
        )
        results.append((attended, grad_queries, total_keys, total_values))

    def rows_by_destination(total):
        stack = total.astype(jnp.bfloat16).reshape(tp_size, rows_in, k_cols)
        order = (me + jnp.arange(tp_size, dtype=jnp.int32)) % tp_size
        return tp_columns([tp_send(jnp.take(stack, order, axis=0), me, tp_size)], me, tp_size)

    attended = tp_columns([r[0] for r in results], me, tp_size)
    grad_queries = tp_columns([r[1] for r in results], me, tp_size)
    total_keys = jnp.concatenate([r[2] for r in results], axis=1)
    total_values = jnp.concatenate([r[3] for r in results], axis=1)
    return (attended, grad_queries, rows_by_destination(total_keys), rows_by_destination(total_values))


def solution(mesh):
    in_specs = (
        P(("ctx", "tp"), None),
        P(("ctx", "tp"), None),
        P(("ctx", "tp"), None),
        P(None, "tp", None),
        P(None, "tp"),
        P(("ctx", "tp"), None),
    )
    out_specs = (
        P(("ctx", "tp"), None),
        P(("ctx", "tp"), None),
        P(("ctx", "tp"), None),
        P(("ctx", "tp"), None),
    )
    return jax.shard_map(body, mesh=mesh, in_specs=in_specs, out_specs=out_specs, check_vma=False)
```
